32 devices in a mesh: wide: 8 (over z, y), narrow: 4 (over x, core).
Axes of the slice: x: 2, y: 2, z: 4, core: 2. Of those that a mesh axis runs over, the one named last changes fastest.
Arguments:
- embeddings: bfloat16 [32768, 768], P(('wide', 'narrow')), may hold values from -6 to 6
- start: bfloat16 [32768, 64], P(('wide', 'narrow')), may hold values from -6 to 6
- neighbours: int32 [32, 3], replicated, may hold values from -1 to 31, as said below
Outputs:
- basis: float32 [32768, 64], P(('wide', 'narrow'))
- degrees: float32 [32768], P(('wide', 'narrow'))
The draws below stay inside these ranges and needn't reach their ends.
Inputs may be any that keep to these rules, and one draw needn't show every extreme that they name: `neighbours`: row b lists distinct blocks c, then -1 in its unused slots; every listed c has c % 4 == b % 4 and (c // 4 - b // 4) mod 8 between 1 and 3, so no unordered pair is listed twice. Some row is full and some row is empty.
All inputs are finite; a program needn't handle non-finite values.
Results may differ from the reference program's by a relative error of at most 0.0034.
Values may be sent and summed in bfloat16 or wider, within the bound.
No kernel may reach another device: no remote copies, remote signals or barrier semaphores. Data moves between devices by JAX's collectives and lax.ppermute only.
A program may use at most 128 MiB of HBM per device.

```python
import math
import jax
import jax.numpy as jnp
from jax import lax

DIM = 768
VECS = 64
BLK = 1024
ITERS = 2
SPAN = 8
LANES = 4
BLOCKS = 32
ROWS = 32768
OWN_MAX = 3


def draw_neighbours(key, part):
    far_reach = SPAN // 2 - 1
    key_counts, selected_key, key_order = jax.random.split(key, 3)
    row_ids = jnp.arange(BLOCKS, dtype=jnp.int32)
    counts = jax.random.randint(key_counts, (BLOCKS,), 1, OWN_MAX + 1)
    chosen = jax.random.randint(selected_key, (2,), 0, BLOCKS)
    forced_row = BLOCKS - 1 - LANES
    full_row = chosen[0]
    empty_row = (forced_row + 1 + chosen[1] % (BLOCKS - 2)) % BLOCKS
    empty_row = jnp.where(empty_row == full_row, (empty_row + 1) % BLOCKS, empty_row)
    counts = jnp.where(row_ids == forced_row, jnp.maximum(counts, 1), counts)
    counts = jnp.where(row_ids == full_row, OWN_MAX, counts)
    counts = jnp.where(row_ids == empty_row, 0, counts)
    target_positions = jnp.arange(far_reach, dtype=jnp.int32)[None, :]
    scoring = jax.random.randint(key_order, (BLOCKS, far_reach), 0, 1 << 20) * far_reach + target_positions
    scoring = jnp.where((row_ids[:, None] == forced_row) & (target_positions == 0), -1, scoring)
    ranking = jnp.argsort(scoring, axis=1)
    offsets = ranking[:, :OWN_MAX] + 1
    wide_ids = row_ids // LANES
    lane_ids = row_ids % LANES
    paired_neighbour = (wide_ids[:, None] + offsets) % SPAN * LANES + lane_ids[:, None]
    slot_ids = jnp.arange(OWN_MAX, dtype=jnp.int32)[None, :]
    return jnp.where(slot_ids < counts[:, None], paired_neighbour, -1).astype(jnp.int32)


def level_of(own_key, dims, shards, least, high):
    def one(dim, parts):
        heights = jax.random.uniform(jax.random.fold_in(jax.random.fold_in(own_key, 6), dim), (parts,), jnp.float32, least / len(shards), high / len(shards))
        return jnp.repeat(jnp.exp(heights), dims[dim] // parts).reshape((-1,) + (1,) * (len(dims) - dim - 1))

    factor_of = one(*shards[0])
    for cut in shards[1:]:
        factor_of = factor_of * one(*cut)
    return factor_of


def gaussian(stream_key, dims, spread, reach, cuts=(), kind=jnp.bfloat16):
    level = level_of(stream_key, dims, cuts, -0.22, 0.18) if cuts else 1.0
    entries = jax.random.normal(stream_key, dims, jnp.float32) * spread * level
    return jnp.minimum(jnp.maximum(entries, -reach), reach).astype(kind)


def setup_inputs(seed: int = 0) -> dict:
    splits = jax.random.split(jax.random.key(seed), 4)
    return {
        "embeddings": gaussian(splits[0], (ROWS, DIM), 1.0, 6.0, ((0, 32),)),
        "start": gaussian(splits[1], (ROWS, VECS), 1.0, 6.0, ((0, 32),)),
        "neighbours": draw_neighbours(jax.random.fold_in(splits[3], 71), 0),
    }


kernel_width_factor = 0.05

def normalize_rows(values):
    values_wide = values.astype(jnp.float32)
    scaling = lax.rsqrt(lax.optimization_barrier(jnp.mean(values_wide * values_wide, axis=-1, keepdims=True)) + 1e-06)
    return (values_wide * scaling / math.sqrt(values_wide.shape[-1])).astype(jnp.bfloat16)

def tile_of(leftside_block, right_block):
    kernel_entries = jnp.dot(leftside_block.astype(jnp.float32), right_block.astype(jnp.float32).T, precision=lax.Precision.HIGHEST)
    return jnp.exp(kernel_entries / kernel_width_factor).astype(jnp.bfloat16)

def sweep(unit_blocks, weight_blocks, neighbours):
    block_count = unit_blocks.shape[0]
    self_mask = lax.broadcasted_iota(jnp.int32, (BLK, BLK), 0) == lax.broadcasted_iota(jnp.int32, (BLK, BLK), 1)

    def diagonal_terms(pair_item):
        unit_block, weight_block = pair_item
        affinity = jnp.where(self_mask, jnp.zeros((), jnp.bfloat16), tile_of(unit_block, unit_block))
        tile_wide = affinity.astype(jnp.float32)
        return (jnp.dot(tile_wide, weight_block.astype(jnp.float32), precision=lax.Precision.HIGHEST), lax.optimization_barrier(jnp.sum(tile_wide, axis=1)))
    product, vertex_valence = lax.map(diagonal_terms, (unit_blocks, weight_blocks))
    owner_ids = jnp.repeat(jnp.arange(block_count, dtype=jnp.int32), neighbours.shape[1])
    partner_ids = neighbours.reshape(-1).astype(jnp.int32)

    def step_pair(carried, pair_item):
        owner_id, paired_neighbour = pair_item

        def compute_pair(inner):
            pairwise_dots, degree_now = inner
            partner_safe = jnp.maximum(paired_neighbour, 0).astype(jnp.int32)
            tile_wide = tile_of(unit_blocks[owner_id], unit_blocks[partner_safe]).astype(jnp.float32)
            pairwise_dots = pairwise_dots.at[owner_id].add(jnp.dot(tile_wide, weight_blocks[partner_safe].astype(jnp.float32), precision=lax.Precision.HIGHEST))
            pairwise_dots = pairwise_dots.at[partner_safe].add(jnp.dot(tile_wide.T, weight_blocks[owner_id].astype(jnp.float32), precision=lax.Precision.HIGHEST))
            degree_now = degree_now.at[owner_id].add(lax.optimization_barrier(jnp.sum(tile_wide, axis=1)))
            degree_now = degree_now.at[partner_safe].add(lax.optimization_barrier(jnp.sum(tile_wide, axis=0)))
            return (pairwise_dots, degree_now)

        def skip_pair(inner):
            return inner
        return (lax.cond(paired_neighbour >= 0, compute_pair, skip_pair, carried), None)
    (product, vertex_valence), unused = lax.scan(step_pair, (product, vertex_valence), (owner_ids, partner_ids))
    return (product, vertex_valence)

def orthonormal(product, vertex_valence):
    column_sums = lax.optimization_barrier(jnp.sum(product, axis=0))
    total_degree_sum = jnp.sum(vertex_valence)
    displaced_entries = product / vertex_valence[:, None] - column_sums / total_degree_sum
    gram_matrix = jnp.dot(displaced_entries.T, displaced_entries, precision=lax.Precision.HIGHEST) / displaced_entries.shape[0]
    normalizer_coefficient = jnp.linalg.cholesky(gram_matrix)
    return jax.scipy.linalg.solve_triangular(normalizer_coefficient, displaced_entries.T, lower=True).T

def reference(embeddings, start, neighbours):
    unit_blocks = normalize_rows(embeddings).reshape(BLOCKS, BLK, DIM)
    weight_blocks = start.reshape(BLOCKS, BLK, VECS)
    vertex_valence = None
    basis = None
    for iteration in range(ITERS):
        product, degree_now = sweep(unit_blocks, weight_blocks, neighbours)
        if iteration == 0:
            vertex_valence = degree_now.reshape(ROWS)
        basis = orthonormal(product.reshape(ROWS, VECS), vertex_valence)
        weight_blocks = basis.astype(jnp.bfloat16).reshape(BLOCKS, BLK, VECS)
    return (basis, vertex_valence / BLK)
```

```python
from functools import partial
import itertools
import math

import jax
import jax.numpy as jnp
from jax import lax
from jax.sharding import PartitionSpec as P

ITERS = 2


kernel_width_factor = 0.05


def shifted(block, axis, distance):
    devices = range(lax.axis_size(axis))
    route = [((i - distance) % len(devices), i) for i in devices]
    return lax.ppermute(block, axis, route)


def ring_gap(offset, span):
    offset %= span
    return min(offset, span - offset)


def difference_plan(span, far_reach):
    candidates = sorted(range(1, span), key=lambda s: (ring_gap(s, span), s))
    for count in range(1, span):
        best = None
        for chosen in itertools.combinations(candidates, count):
            points = (0,) + chosen
            plan = {}
            for a, b in itertools.permutations(points, 2):
                gap = (b - a) % span
                if 1 <= gap <= far_reach and gap not in plan:
                    plan[gap] = (a, b)
            if len(plan) == far_reach:
                cost = sum(ring_gap(s, span) for s in chosen)
                if best is None or cost < best[0]:
                    best = (cost, chosen, plan)
        if best is not None:
            return list(best[1]), [best[2][gap] for gap in range(1, far_reach + 1)]
    raise ValueError("no plan")


def normalize_rows(values):
    values_wide = values.astype(jnp.float32)
    scaling = lax.rsqrt(jnp.mean(values_wide * values_wide, axis=-1, keepdims=True) + 1e-06)
    return (values_wide * scaling / math.sqrt(values_wide.shape[-1])).astype(jnp.bfloat16)


def scores_tile(leftside_block, right_block):
    kernel_entries = lax.dot_general(
        leftside_block, right_block, (((1,), (1,)), ((), ())), preferred_element_type=jnp.float32
    )
    return jnp.exp(kernel_entries / kernel_width_factor).astype(jnp.bfloat16)


def row_product(affinity, weights):
    return jnp.dot(affinity, weights, preferred_element_type=jnp.float32)


def col_product(affinity, weights):
    return lax.dot_general(
        affinity, weights, (((0,), (0,)), ((), ())), preferred_element_type=jnp.float32
    )


def first_pass(owned, left_unit, right_unit, left_weights, right_weights):
    block_rows = left_unit.shape[0]
    vector_count = left_weights.shape[1]

    def compute_pair():
        affinity = scores_tile(left_unit, right_unit)
        return (
            affinity,
            row_product(affinity, right_weights),
            jnp.sum(affinity, axis=1, dtype=jnp.float32),
            col_product(affinity, left_weights),
            jnp.sum(affinity, axis=0, dtype=jnp.float32),
        )

    def skip_pair():
        zero_part = jnp.zeros((block_rows, vector_count), jnp.float32)
        zero_sum = jnp.zeros((block_rows,), jnp.float32)
        return (
            jnp.zeros((block_rows, block_rows), jnp.bfloat16),
            zero_part,
            zero_sum,
            zero_part,
            zero_sum,
        )

    return lax.cond(owned, compute_pair, skip_pair)


def later_pass(owned, affinity, left_weights, right_weights):
    block_rows = affinity.shape[0]
    vector_count = left_weights.shape[1]

    def compute_pair():
        return (row_product(affinity, right_weights), col_product(affinity, left_weights))

    def skip_pair():
        zero_part = jnp.zeros((block_rows, vector_count), jnp.float32)
        return (zero_part, zero_part)

    return lax.cond(owned, compute_pair, skip_pair)


def butterfly(axis, summed, gathered):
    size = lax.axis_size(axis)
    if size & (size - 1):
        return (
            jax.tree.map(lambda v: lax.psum(v, axis), summed),
            lax.all_gather(gathered, axis, tiled=True),
        )
    index = lax.axis_index(axis)
    step = 1
    while step < size:
        route = [(i, i ^ step) for i in range(size)]
        other_summed, other_gathered = lax.ppermute((summed, gathered), axis, route)
        summed = jax.tree.map(jnp.add, summed, other_summed)
        upper = (index // step) % 2 == 1
        gathered = jnp.where(
            upper,
            jnp.concatenate([other_gathered, gathered]),
            jnp.concatenate([gathered, other_gathered]),
        )
        step *= 2
    return summed, gathered


def hdot(left, right):
    return jnp.dot(left, right, precision=lax.Precision.HIGHEST, preferred_element_type=jnp.float32)


def orthonormal(product, vertex_valence, total_rows):
    block_rows, vector_count = product.shape
    walk = product / vertex_valence[:, None]
    centre = jnp.mean(walk, axis=0)
    centred = walk - centre
    local_gram = hdot(centred.T, centred)
    local_drift = jnp.sum(centred, axis=0)
    summed = (local_gram, jnp.sum(product, axis=0), jnp.sum(vertex_valence))
    gathered = jnp.concatenate([centre, local_drift])[None, :]
    for axis in ("narrow", "wide"):
        summed, gathered = butterfly(axis, summed, gathered)
    gram_sum, column_sums, total_degree_sum = summed
    mean_walk = column_sums / total_degree_sum
    centres = gathered[:, :vector_count] - mean_walk
    drifts = gathered[:, vector_count:]
    cross = hdot(centres.T, drifts)
    gram_matrix = (gram_sum + cross + cross.T + block_rows * hdot(centres.T, centres)) / total_rows
    displaced_entries = walk - mean_walk
    normalizer_coefficient = jnp.linalg.cholesky(gram_matrix)
    return jax.scipy.linalg.solve_triangular(
        normalizer_coefficient, displaced_entries.T, lower=True
    ).T


def on_device(embeddings, start, neighbours):
    wide_count = lax.axis_size("wide")
    lane_count = lax.axis_size("narrow")
    broad_index = lax.axis_index("wide")
    lane_index = lax.axis_index("narrow")
    far_reach = wide_count // 2 - 1
    fetch_offsets, pair_plan = difference_plan(wide_count, far_reach)
    unit_block = normalize_rows(embeddings)
    block_rows = unit_block.shape[0]
    total_rows = block_rows * wide_count * lane_count

    def block_at(offset):
        return (broad_index + offset) % wide_count * lane_count + lane_index

    owned_list = []
    for left, right in pair_plan:
        own_row = lax.dynamic_slice_in_dim(neighbours, block_at(left), 1, 0)[0]
        owned_list.append(jnp.any(own_row == block_at(right)))

    units = {0: unit_block}
    weights = {0: start}
    for offset in fetch_offsets:
        units[offset], weights[offset] = shifted((unit_block, start), "wide", -offset)

    self_mask = lax.broadcasted_iota(
        jnp.int32, (block_rows, block_rows), 0
    ) == lax.broadcasted_iota(jnp.int32, (block_rows, block_rows), 1)
    near_tile = jnp.where(
        self_mask, jnp.zeros((), jnp.bfloat16), scores_tile(unit_block, unit_block)
    )

    vector_count = start.shape[1]
    zero_part = jnp.zeros((block_rows, vector_count), jnp.float32)
    zero_sum = jnp.zeros((block_rows,), jnp.float32)
    parts = {offset: zero_part for offset in units}
    sums = {offset: zero_sum for offset in units}
    tiles = []
    for (left, right), owned in zip(pair_plan, owned_list):
        affinity, row_part, row_sum, col_part, col_sum = first_pass(
            owned, units[left], units[right], weights[left], weights[right]
        )
        tiles.append(affinity)
        parts[left] = parts[left] + row_part
        sums[left] = sums[left] + row_sum
        parts[right] = parts[right] + col_part
        sums[right] = sums[right] + col_sum

    product = row_product(near_tile, start) + parts[0]
    vertex_valence = jnp.sum(near_tile, axis=1, dtype=jnp.float32) + sums[0]
    for offset in fetch_offsets:
        returned, returned_sum = shifted((parts[offset], sums[offset]), "wide", offset)
        product = product + returned
        vertex_valence = vertex_valence + returned_sum
    basis = orthonormal(product, vertex_valence, total_rows)

    for iteration in range(1, ITERS):
        current = basis.astype(jnp.bfloat16)
        weights = {0: current}
        for offset in fetch_offsets:
            weights[offset] = shifted(current, "wide", -offset)
        parts = {offset: zero_part for offset in units}
        for (left, right), owned, affinity in zip(pair_plan, owned_list, tiles):
            row_part, col_part = later_pass(owned, affinity, weights[left], weights[right])
            parts[left] = parts[left] + row_part
            parts[right] = parts[right] + col_part
        product = row_product(near_tile, current) + parts[0]
        for offset in fetch_offsets:
            product = product + shifted(parts[offset], "wide", offset)
        basis = orthonormal(product, vertex_valence, total_rows)
    return (basis, vertex_valence / block_rows)


def solution(mesh):
    in_specs = (P(("wide", "narrow"), None), P(("wide", "narrow"), None), P())
    out_specs = (P(("wide", "narrow"), None), P(("wide", "narrow")))
    return jax.shard_map(
        on_device, mesh=mesh, in_specs=in_specs, out_specs=out_specs, check_vma=False
    )
```

```python
from functools import partial
import itertools
import math

import jax
import jax.numpy as jnp
from jax import lax
from jax.sharding import PartitionSpec as P

ITERS = 2


kernel_width_factor = 0.05


def shifted(block, axis, distance):
    devices = range(lax.axis_size(axis))
    route = [((i - distance) % len(devices), i) for i in devices]
    return lax.ppermute(block, axis, route)


def ring_gap(offset, span):
    offset %= span
    return min(offset, span - offset)


def difference_plan(span, far_reach):
    candidates = sorted(range(1, span), key=lambda s: (ring_gap(s, span), s))
    for count in range(1, span):
        best = None
        for chosen in itertools.combinations(candidates, count):
            points = (0,) + chosen
            plan = {}
            for a, b in itertools.permutations(points, 2):
                gap = (b - a) % span
                if 1 <= gap <= far_reach and gap not in plan:
                    plan[gap] = (a, b)
            if len(plan) == far_reach:
                cost = sum(ring_gap(s, span) for s in chosen)
                if best is None or cost < best[0]:
                    best = (cost, chosen, plan)
        if best is not None:
            return list(best[1]), [best[2][gap] for gap in range(1, far_reach + 1)]
    raise ValueError("no plan")


def normalize_rows(values):
    values_wide = values.astype(jnp.float32)
    scaling = lax.rsqrt(jnp.mean(values_wide * values_wide, axis=-1, keepdims=True) + 1e-06)
    return (values_wide * scaling / math.sqrt(values_wide.shape[-1])).astype(jnp.bfloat16)


def scores_tile(leftside_block, right_block):
    kernel_entries = lax.dot_general(
        leftside_block, right_block, (((1,), (1,)), ((), ())), preferred_element_type=jnp.float32
    )
    return jnp.exp(kernel_entries / kernel_width_factor).astype(jnp.bfloat16)


def row_product(affinity, weights):
    return jnp.dot(affinity, weights, preferred_element_type=jnp.float32)


def col_product(affinity, weights):
    return lax.dot_general(
        affinity, weights, (((0,), (0,)), ((), ())), preferred_element_type=jnp.float32
    )


def first_pass(owned, left_unit, right_unit, left_weights, right_weights):
    block_rows = left_unit.shape[0]
    vector_count = left_weights.shape[1]

    def compute_pair():
        affinity = scores_tile(left_unit, right_unit)
        return (
            affinity,
            row_product(affinity, right_weights),
            jnp.sum(affinity, axis=1, dtype=jnp.float32),
            col_product(affinity, left_weights),
            jnp.sum(affinity, axis=0, dtype=jnp.float32),
        )

    def skip_pair():
        zero_part = jnp.zeros((block_rows, vector_count), jnp.float32)
        zero_sum = jnp.zeros((block_rows,), jnp.float32)
        return (
            jnp.zeros((block_rows, block_rows), jnp.bfloat16),
            zero_part,
            zero_sum,
            zero_part,
            zero_sum,
        )

    return lax.cond(owned, compute_pair, skip_pair)


def later_pass(owned, affinity, left_weights, right_weights):
    block_rows = affinity.shape[0]
    vector_count = left_weights.shape[1]

    def compute_pair():
        return (row_product(affinity, right_weights), col_product(affinity, left_weights))

    def skip_pair():
        zero_part = jnp.zeros((block_rows, vector_count), jnp.float32)
        return (zero_part, zero_part)

    return lax.cond(owned, compute_pair, skip_pair)


def butterfly(axis, summed_rows, block):
    size = lax.axis_size(axis)
    if size & (size - 1):
        return jnp.concatenate(
            [
                lax.psum(block[:summed_rows], axis),
                lax.all_gather(block[summed_rows:], axis, tiled=True),
            ]
        )
    index = lax.axis_index(axis)
    step = 1
    while step < size:
        route = [(i, i ^ step) for i in range(size)]
        other = lax.ppermute(block, axis, route)
        summed = block[:summed_rows] + other[:summed_rows]
        mine = block[summed_rows:]
        theirs = other[summed_rows:]
        upper = (index // step) % 2 == 1
        gathered = jnp.where(
            upper, jnp.concatenate([theirs, mine]), jnp.concatenate([mine, theirs])
        )
        block = jnp.concatenate([summed, gathered])
        step *= 2
    return block


def as_rows(vector, lanes=128):
    pad = (-vector.shape[0]) % lanes
    return jnp.pad(vector, (0, pad)).reshape(-1, lanes)


def hdot(left, right):
    return jnp.dot(left, right, precision=lax.Precision.HIGHEST, preferred_element_type=jnp.float32)


def orthonormal(product, vertex_valence, total_rows):
    block_rows, vector_count = product.shape
    walk = product / vertex_valence[:, None]
    centre = jnp.mean(walk, axis=0)
    centred = walk - centre
    local_gram = hdot(centred.T, centred)
    local_drift = jnp.sum(centred, axis=0)
    summed = jnp.concatenate(
        [
            as_rows(local_gram.reshape(-1)),
            as_rows(jnp.concatenate([jnp.sum(product, axis=0), jnp.sum(vertex_valence)[None]])),
        ]
    )
    summed_rows = summed.shape[0]
    block = jnp.concatenate([summed, as_rows(jnp.concatenate([centre, local_drift]))])
    gather_width = block.shape[0] - summed_rows
    for axis in ("narrow", "wide"):
        block = butterfly(axis, summed_rows, block)
    totals = block[:summed_rows].reshape(-1)
    gram_sum = totals[: vector_count * vector_count].reshape(vector_count, vector_count)
    column_sums = totals[vector_count * vector_count : vector_count * vector_count + vector_count]
    total_degree_sum = totals[vector_count * vector_count + vector_count]
    gathered = block[summed_rows:].reshape(-1, gather_width * 128)
    mean_walk = column_sums / total_degree_sum
    centres = gathered[:, :vector_count] - mean_walk
    drifts = gathered[:, vector_count:]
    cross = hdot(centres.T, drifts)
    gram_matrix = (gram_sum + cross + cross.T + block_rows * hdot(centres.T, centres)) / total_rows
    displaced_entries = walk - mean_walk
    normalizer_coefficient = jnp.linalg.cholesky(gram_matrix)
    return jax.scipy.linalg.solve_triangular(
        normalizer_coefficient, displaced_entries.T, lower=True
    ).T


def on_device(embeddings, start, neighbours):
    wide_count = lax.axis_size("wide")
    lane_count = lax.axis_size("narrow")
    broad_index = lax.axis_index("wide")
    lane_index = lax.axis_index("narrow")
    far_reach = wide_count // 2 - 1
    fetch_offsets, pair_plan = difference_plan(wide_count, far_reach)
    unit_block = normalize_rows(embeddings)
    block_rows = unit_block.shape[0]
    total_rows = block_rows * wide_count * lane_count

    def block_at(offset):
        return (broad_index + offset) % wide_count * lane_count + lane_index

    owned_list = []
    for left, right in pair_plan:
        own_row = lax.dynamic_slice_in_dim(neighbours, block_at(left), 1, 0)[0]
        owned_list.append(jnp.any(own_row == block_at(right)))

    units = {0: unit_block}
    weights = {0: start}
    unit_width = unit_block.shape[1]
    packed = jnp.concatenate([unit_block, start], axis=1)
    for offset in fetch_offsets:
        arrived = shifted(packed, "wide", -offset)
        units[offset] = arrived[:, :unit_width]
        weights[offset] = arrived[:, unit_width:]

    self_mask = lax.broadcasted_iota(
        jnp.int32, (block_rows, block_rows), 0
    ) == lax.broadcasted_iota(jnp.int32, (block_rows, block_rows), 1)
    near_tile = jnp.where(
        self_mask, jnp.zeros((), jnp.bfloat16), scores_tile(unit_block, unit_block)
    )

    vector_count = start.shape[1]
    zero_part = jnp.zeros((block_rows, vector_count), jnp.float32)
    zero_sum = jnp.zeros((block_rows,), jnp.float32)
    parts = {offset: zero_part for offset in units}
    sums = {offset: zero_sum for offset in units}
    tiles = []
    for (left, right), owned in zip(pair_plan, owned_list):
        affinity, row_part, row_sum, col_part, col_sum = first_pass(
            owned, units[left], units[right], weights[left], weights[right]
        )
        tiles.append(affinity)
        parts[left] = parts[left] + row_part
        sums[left] = sums[left] + row_sum
        parts[right] = parts[right] + col_part
        sums[right] = sums[right] + col_sum

    product = row_product(near_tile, start) + parts[0]
    vertex_valence = jnp.sum(near_tile, axis=1, dtype=jnp.float32) + sums[0]
    part_size = block_rows * vector_count
    for offset in fetch_offsets:
        sent = jnp.concatenate([as_rows(parts[offset].reshape(-1)), as_rows(sums[offset])])
        returned = shifted(sent, "wide", offset).reshape(-1)
        product = product + returned[:part_size].reshape(block_rows, vector_count)
        vertex_valence = vertex_valence + returned[part_size : part_size + block_rows]
    basis = orthonormal(product, vertex_valence, total_rows)

    for iteration in range(1, ITERS):
        current = basis.astype(jnp.bfloat16)
        weights = {0: current}
        for offset in fetch_offsets:
            weights[offset] = shifted(current, "wide", -offset)
        parts = {offset: zero_part for offset in units}
        for (left, right), owned, affinity in zip(pair_plan, owned_list, tiles):
            row_part, col_part = later_pass(owned, affinity, weights[left], weights[right])
            parts[left] = parts[left] + row_part
            parts[right] = parts[right] + col_part
        product = row_product(near_tile, current) + parts[0]
        for offset in fetch_offsets:
            product = product + shifted(parts[offset], "wide", offset)
        basis = orthonormal(product, vertex_valence, total_rows)
    return (basis, vertex_valence / block_rows)


def solution(mesh):
    in_specs = (P(("wide", "narrow"), None), P(("wide", "narrow"), None), P())
    out_specs = (P(("wide", "narrow"), None), P(("wide", "narrow")))
    return jax.shard_map(
        on_device, mesh=mesh, in_specs=in_specs, out_specs=out_specs, check_vma=False
    )
```

```python
from functools import partial
import itertools
import math

import jax
import jax.numpy as jnp
from jax import lax
from jax.sharding import PartitionSpec as P
from jax.experimental import pallas as pl

ITERS = 2


kernel_width_factor = 0.05


def shifted(block, axis, distance):
    devices = range(lax.axis_size(axis))
    route = [((i - distance) % len(devices), i) for i in devices]
    return lax.ppermute(block, axis, route)


def ring_gap(offset, span):
    offset %= span
    return min(offset, span - offset)


def difference_plan(span, far_reach):
    candidates = sorted(range(1, span), key=lambda s: (ring_gap(s, span), s))
    for count in range(1, span):
        best = None
        for chosen in itertools.combinations(candidates, count):
            points = (0,) + chosen
            plan = {}
            for a, b in itertools.permutations(points, 2):
                gap = (b - a) % span
                if 1 <= gap <= far_reach and gap not in plan:
                    plan[gap] = (a, b)
            if len(plan) == far_reach:
                cost = sum(ring_gap(s, span) for s in chosen)
                if best is None or cost < best[0]:
                    best = (cost, chosen, plan)
        if best is not None:
            return list(best[1]), [best[2][gap] for gap in range(1, far_reach + 1)]
    raise ValueError("no plan")


def normalize_rows(values):
    values_wide = values.astype(jnp.float32)
    scaling = lax.rsqrt(jnp.mean(values_wide * values_wide, axis=-1, keepdims=True) + 1e-06)
    return (values_wide * scaling / math.sqrt(values_wide.shape[-1])).astype(jnp.bfloat16)


def scores_tile(leftside_block, right_block):
    kernel_entries = lax.dot_general(
        leftside_block, right_block, (((1,), (1,)), ((), ())), preferred_element_type=jnp.float32
    )
    return jnp.exp(kernel_entries / kernel_width_factor).astype(jnp.bfloat16)


def row_product(affinity, weights):
    return jnp.dot(affinity, weights, preferred_element_type=jnp.float32)


def col_product(affinity, weights):
    return lax.dot_general(
        affinity, weights, (((0,), (0,)), ((), ())), preferred_element_type=jnp.float32
    )


def pair_kernel(left_ref, right_ref, left_t_ref, right_w_ref, tile_ref, row_ref, col_ref):
    step = pl.program_id(0)
    entries = lax.dot_general(
        left_ref[...], right_ref[...], (((1,), (1,)), ((), ())), preferred_element_type=jnp.float32
    )
    affinity = jnp.exp(entries / kernel_width_factor).astype(jnp.bfloat16)
    tile_ref[...] = affinity
    part = jnp.dot(affinity, right_w_ref[...], preferred_element_type=jnp.float32)

    @pl.when(step == 0)
    def _():
        row_ref[...] = part

    @pl.when(step > 0)
    def _():
        row_ref[...] += part

    col_ref[...] = jnp.dot(left_t_ref[...], affinity, preferred_element_type=jnp.float32)


def apply_kernel(tile_ref, left_t_ref, right_w_ref, row_ref, col_ref):
    step = pl.program_id(0)
    affinity = tile_ref[...]
    part = jnp.dot(affinity, right_w_ref[...], preferred_element_type=jnp.float32)

    @pl.when(step == 0)
    def _():
        row_ref[...] = part

    @pl.when(step > 0)
    def _():
        row_ref[...] += part

    col_ref[...] = jnp.dot(left_t_ref[...], affinity, preferred_element_type=jnp.float32)


COLUMN_CHUNK = 256


def pair_terms(left_packed, right_packed, left_t, right_w, block_rows):
    unit_width = left_packed.shape[1]
    width = right_w.shape[1]
    chunk = min(COLUMN_CHUNK, block_rows)
    return pl.pallas_call(
        pair_kernel,
        grid=(block_rows // chunk,),
        in_specs=[
            pl.BlockSpec((block_rows, unit_width), lambda j: (0, 0)),
            pl.BlockSpec((chunk, unit_width), lambda j: (j, 0)),
            pl.BlockSpec((width, block_rows), lambda j: (0, 0)),
            pl.BlockSpec((chunk, width), lambda j: (j, 0)),
        ],
        out_specs=[
            pl.BlockSpec((block_rows, chunk), lambda j: (0, j)),
            pl.BlockSpec((block_rows, width), lambda j: (0, 0)),
            pl.BlockSpec((width, chunk), lambda j: (0, j)),
        ],
        out_shape=[
            jax.ShapeDtypeStruct((block_rows, block_rows), jnp.bfloat16),
            jax.ShapeDtypeStruct((block_rows, width), jnp.float32),
            jax.ShapeDtypeStruct((width, block_rows), jnp.float32),
        ],
    )(left_packed, right_packed, left_t, right_w)


def apply_terms(affinity, left_t, right_w):
    block_rows = affinity.shape[0]
    width = right_w.shape[1]
    chunk = min(COLUMN_CHUNK, block_rows)
    return pl.pallas_call(
        apply_kernel,
        grid=(block_rows // chunk,),
        in_specs=[
            pl.BlockSpec((block_rows, chunk), lambda j: (0, j)),
            pl.BlockSpec((width, block_rows), lambda j: (0, 0)),
            pl.BlockSpec((chunk, width), lambda j: (j, 0)),
        ],
        out_specs=[
            pl.BlockSpec((block_rows, width), lambda j: (0, 0)),
            pl.BlockSpec((width, chunk), lambda j: (0, j)),
        ],
        out_shape=[
            jax.ShapeDtypeStruct((block_rows, width), jnp.float32),
            jax.ShapeDtypeStruct((width, block_rows), jnp.float32),
        ],
    )(affinity, left_t, right_w)


def with_ones(weights):
    rows, count = weights.shape
    ones = jnp.ones((rows, 1), weights.dtype)
    pad = (-(count + 1)) % 128
    return jnp.concatenate([weights, ones, jnp.zeros((rows, pad), weights.dtype)], axis=1)


def first_pass(owned, left_packed, right_packed, left_weights, right_weights, block_rows):
    vector_count = left_weights.shape[1]

    def compute_pair():
        affinity, row_wide, col_wide = pair_terms(
            left_packed, right_packed, with_ones(left_weights).T, with_ones(right_weights), block_rows
        )
        return (
            affinity,
            row_wide[:, :vector_count],
            row_wide[:, vector_count],
            col_wide[:vector_count].T,
            col_wide[vector_count],
        )

    def skip_pair():
        zero_part = jnp.zeros((block_rows, vector_count), jnp.float32)
        zero_sum = jnp.zeros((block_rows,), jnp.float32)
        return (
            jnp.zeros((block_rows, block_rows), jnp.bfloat16),
            zero_part,
            zero_sum,
            zero_part,
            zero_sum,
        )

    return lax.cond(owned, compute_pair, skip_pair)


def later_pass(owned, affinity, left_weights, right_weights):
    block_rows = affinity.shape[0]
    vector_count = left_weights.shape[1]

    def compute_pair():
        row_part, col_t = apply_terms(affinity, left_weights.T, right_weights)
        return (row_part, col_t.T)

    def skip_pair():
        zero_part = jnp.zeros((block_rows, vector_count), jnp.float32)
        return (zero_part, zero_part)

    return lax.cond(owned, compute_pair, skip_pair)


def butterfly(axis, summed_rows, block):
    size = lax.axis_size(axis)
    if size & (size - 1):
        return jnp.concatenate(
            [
                lax.psum(block[:summed_rows], axis),
                lax.all_gather(block[summed_rows:], axis, tiled=True),
            ]
        )
    index = lax.axis_index(axis)
    step = 1
    while step < size:
        route = [(i, i ^ step) for i in range(size)]
        other = lax.ppermute(block, axis, route)
        summed = block[:summed_rows] + other[:summed_rows]
        mine = block[summed_rows:]
        theirs = other[summed_rows:]
        upper = (index // step) % 2 == 1
        gathered = jnp.where(
            upper, jnp.concatenate([theirs, mine]), jnp.concatenate([mine, theirs])
        )
        block = jnp.concatenate([summed, gathered])
        step *= 2
    return block


def as_rows(vector, lanes=128):
    pad = (-vector.shape[0]) % lanes
    return jnp.pad(vector, (0, pad)).reshape(-1, lanes)


def hdot(left, right):
    return jnp.dot(left, right, precision=lax.Precision.HIGHEST, preferred_element_type=jnp.float32)


def orthonormal(product, vertex_valence, total_rows):
    block_rows, vector_count = product.shape
    walk = product / vertex_valence[:, None]
    centre = jnp.mean(walk, axis=0)
    centred = walk - centre
    local_gram = hdot(centred.T, centred)
    local_drift = jnp.sum(centred, axis=0)
    summed = jnp.concatenate(
        [
            as_rows(local_gram.reshape(-1)),
            as_rows(jnp.concatenate([jnp.sum(product, axis=0), jnp.sum(vertex_valence)[None]])),
        ]
    )
    summed_rows = summed.shape[0]
    block = jnp.concatenate([summed, as_rows(jnp.concatenate([centre, local_drift]))])
    gather_width = block.shape[0] - summed_rows
    for axis in ("narrow", "wide"):
        block = butterfly(axis, summed_rows, block)
    totals = block[:summed_rows].reshape(-1)
    gram_sum = totals[: vector_count * vector_count].reshape(vector_count, vector_count)
    column_sums = totals[vector_count * vector_count : vector_count * vector_count + vector_count]
    total_degree_sum = totals[vector_count * vector_count + vector_count]
    gathered = block[summed_rows:].reshape(-1, gather_width * 128)
    mean_walk = column_sums / total_degree_sum
    centres = gathered[:, :vector_count] - mean_walk
    drifts = gathered[:, vector_count:]
    cross = hdot(centres.T, drifts)
    gram_matrix = (gram_sum + cross + cross.T + block_rows * hdot(centres.T, centres)) / total_rows
    displaced_entries = walk - mean_walk
    normalizer_coefficient = jnp.linalg.cholesky(gram_matrix)
    return jax.scipy.linalg.solve_triangular(
        normalizer_coefficient, displaced_entries.T, lower=True
    ).T


def on_device(embeddings, start, neighbours):
    wide_count = lax.axis_size("wide")
    lane_count = lax.axis_size("narrow")
    broad_index = lax.axis_index("wide")
    lane_index = lax.axis_index("narrow")
    far_reach = wide_count // 2 - 1
    fetch_offsets, pair_plan = difference_plan(wide_count, far_reach)
    unit_block = normalize_rows(embeddings)
    block_rows = unit_block.shape[0]
    total_rows = block_rows * wide_count * lane_count

    def block_at(offset):
        return (broad_index + offset) % wide_count * lane_count + lane_index

    owned_list = []
    for left, right in pair_plan:
        own_row = lax.dynamic_slice_in_dim(neighbours, block_at(left), 1, 0)[0]
        owned_list.append(jnp.any(own_row == block_at(right)))

    unit_width = unit_block.shape[1]
    vector_count = start.shape[1]
    packed = jnp.concatenate([unit_block, as_rows(start.reshape(-1), unit_width)])
    units = {0: packed}
    weights = {0: start}
    for offset in fetch_offsets:
        arrived = shifted(packed, "wide", -offset)
        units[offset] = arrived
        weights[offset] = (
            arrived[block_rows:].reshape(-1)[: block_rows * vector_count].reshape(block_rows, vector_count)
        )

    self_mask = lax.broadcasted_iota(
        jnp.int32, (block_rows, block_rows), 0
    ) == lax.broadcasted_iota(jnp.int32, (block_rows, block_rows), 1)
    near_tile = jnp.where(
        self_mask, jnp.zeros((), jnp.bfloat16), scores_tile(unit_block, unit_block)
    )

    zero_part = jnp.zeros((block_rows, vector_count), jnp.float32)
    zero_sum = jnp.zeros((block_rows,), jnp.float32)
    parts = {offset: zero_part for offset in units}
    sums = {offset: zero_sum for offset in units}
    tiles = []
    for (left, right), owned in zip(pair_plan, owned_list):
        affinity, row_part, row_sum, col_part, col_sum = first_pass(
            owned, units[left], units[right], weights[left], weights[right], block_rows
        )
        tiles.append(affinity)
        parts[left] = parts[left] + row_part
        sums[left] = sums[left] + row_sum
        parts[right] = parts[right] + col_part
        sums[right] = sums[right] + col_sum

    product = row_product(near_tile, start) + parts[0]
    vertex_valence = jnp.sum(near_tile, axis=1, dtype=jnp.float32) + sums[0]
    part_size = block_rows * vector_count
    for offset in fetch_offsets:
        sent = jnp.concatenate([as_rows(parts[offset].reshape(-1)), as_rows(sums[offset])])
        returned = shifted(sent, "wide", offset).reshape(-1)
        product = product + returned[:part_size].reshape(block_rows, vector_count)
        vertex_valence = vertex_valence + returned[part_size : part_size + block_rows]
    basis = orthonormal(product, vertex_valence, total_rows)

    for iteration in range(1, ITERS):
        current = basis.astype(jnp.bfloat16)
        weights = {0: current}
        for offset in fetch_offsets:
            weights[offset] = shifted(current, "wide", -offset)
        parts = {offset: zero_part for offset in units}
        for (left, right), owned, affinity in zip(pair_plan, owned_list, tiles):
            row_part, col_part = later_pass(owned, affinity, weights[left], weights[right])
            parts[left] = parts[left] + row_part
            parts[right] = parts[right] + col_part
        product = row_product(near_tile, current) + parts[0]
        for offset in fetch_offsets:
            product = product + shifted(parts[offset], "wide", offset)
        basis = orthonormal(product, vertex_valence, total_rows)
    return (basis, vertex_valence / block_rows)


def solution(mesh):
    in_specs = (P(("wide", "narrow"), None), P(("wide", "narrow"), None), P())
    out_specs = (P(("wide", "narrow"), None), P(("wide", "narrow")))
    return jax.shard_map(
        on_device, mesh=mesh, in_specs=in_specs, out_specs=out_specs, check_vma=False
    )
```

```python
from functools import partial
import itertools
import math

import jax
import jax.numpy as jnp
from jax import lax
from jax.sharding import PartitionSpec as P

ITERS = 2


kernel_width_factor = 0.05


def shifted(block, axis, distance):
    devices = range(lax.axis_size(axis))
    route = [((i - distance) % len(devices), i) for i in devices]
    return lax.ppermute(block, axis, route)


def ring_gap(offset, span):
    offset %= span
    return min(offset, span - offset)


def difference_plan(span, far_reach):
    candidates = sorted(range(1, span), key=lambda s: (ring_gap(s, span), s))
    for count in range(1, span):
        best = None
        for chosen in itertools.combinations(candidates, count):
            points = (0,) + chosen
            plan = {}
            for a, b in itertools.permutations(points, 2):
                gap = (b - a) % span
                if 1 <= gap <= far_reach and gap not in plan:
                    plan[gap] = (a, b)
            if len(plan) == far_reach:
                cost = sum(ring_gap(s, span) for s in chosen)
                if best is None or cost < best[0]:
                    best = (cost, chosen, plan)
        if best is not None:
            return list(best[1]), [best[2][gap] for gap in range(1, far_reach + 1)]
    raise ValueError("no plan")


def normalize_rows(values):
    values_wide = values.astype(jnp.float32)
    scaling = lax.rsqrt(jnp.mean(values_wide * values_wide, axis=-1, keepdims=True) + 1e-06)
    return (values_wide * scaling / math.sqrt(values_wide.shape[-1])).astype(jnp.bfloat16)


def scores_tile(leftside_block, right_block):
    kernel_entries = lax.dot_general(
        leftside_block, right_block, (((1,), (1,)), ((), ())), preferred_element_type=jnp.float32
    )
    return jnp.exp(kernel_entries / kernel_width_factor).astype(jnp.bfloat16)


def row_product(affinity, weights):
    return jnp.dot(affinity, weights, preferred_element_type=jnp.float32)


def col_product(affinity, weights):
    return lax.dot_general(
        affinity, weights, (((0,), (0,)), ((), ())), preferred_element_type=jnp.float32
    )


def first_pass(owned, left_unit, right_unit, left_weights, right_weights):
    block_rows = left_unit.shape[0]
    vector_count = left_weights.shape[1]

    def compute_pair():
        affinity = scores_tile(left_unit, right_unit)
        return (
            affinity,
            row_product(affinity, right_weights),
            jnp.sum(affinity, axis=1, dtype=jnp.float32),
            col_product(affinity, left_weights),
            jnp.sum(affinity, axis=0, dtype=jnp.float32),
        )

    def skip_pair():
        zero_part = jnp.zeros((block_rows, vector_count), jnp.float32)
        zero_sum = jnp.zeros((block_rows,), jnp.float32)
        return (
            jnp.zeros((block_rows, block_rows), jnp.bfloat16),
            zero_part,
            zero_sum,
            zero_part,
            zero_sum,
        )

    return lax.cond(owned, compute_pair, skip_pair)


def later_pass(owned, affinity, left_weights, right_weights):
    block_rows = affinity.shape[0]
    vector_count = left_weights.shape[1]

    def compute_pair():
        return (row_product(affinity, right_weights), col_product(affinity, left_weights))

    def skip_pair():
        zero_part = jnp.zeros((block_rows, vector_count), jnp.float32)
        return (zero_part, zero_part)

    return lax.cond(owned, compute_pair, skip_pair)


def butterfly(axis, summed_rows, block):
    size = lax.axis_size(axis)
    if size & (size - 1):
        return jnp.concatenate(
            [
                lax.psum(block[:summed_rows], axis),
                lax.all_gather(block[summed_rows:], axis, tiled=True),
            ]
        )
    index = lax.axis_index(axis)
    step = 1
    while step < size:
        route = [(i, i ^ step) for i in range(size)]
        other = lax.ppermute(block, axis, route)
        summed = block[:summed_rows] + other[:summed_rows]
        mine = block[summed_rows:]
        theirs = other[summed_rows:]
        upper = (index // step) % 2 == 1
        gathered = jnp.where(
            upper, jnp.concatenate([theirs, mine]), jnp.concatenate([mine, theirs])
        )
        block = jnp.concatenate([summed, gathered])
        step *= 2
    return block


def as_rows(vector, lanes=128):
    pad = (-vector.shape[0]) % lanes
    return jnp.pad(vector, (0, pad)).reshape(-1, lanes)


def hdot(left, right):
    return jnp.dot(left, right, precision=lax.Precision.HIGHEST, preferred_element_type=jnp.float32)


def orthonormal(product, vertex_valence, total_rows):
    block_rows, vector_count = product.shape
    walk = product / vertex_valence[:, None]
    centre = jnp.mean(walk, axis=0)
    centred = walk - centre
    local_gram = hdot(centred.T, centred)
    local_drift = jnp.sum(centred, axis=0)
    summed = jnp.concatenate(
        [
            as_rows(local_gram.reshape(-1)),
            as_rows(jnp.concatenate([jnp.sum(product, axis=0), jnp.sum(vertex_valence)[None]])),
        ]
    )
    summed_rows = summed.shape[0]
    block = jnp.concatenate([summed, as_rows(jnp.concatenate([centre, local_drift]))])
    gather_width = block.shape[0] - summed_rows
    for axis in ("narrow", "wide"):
        block = butterfly(axis, summed_rows, block)
    totals = block[:summed_rows].reshape(-1)
    gram_sum = totals[: vector_count * vector_count].reshape(vector_count, vector_count)
    column_sums = totals[vector_count * vector_count : vector_count * vector_count + vector_count]
    total_degree_sum = totals[vector_count * vector_count + vector_count]
    gathered = block[summed_rows:].reshape(-1, gather_width * 128)
    mean_walk = column_sums / total_degree_sum
    centres = gathered[:, :vector_count] - mean_walk
    drifts = gathered[:, vector_count:]
    cross = hdot(centres.T, drifts)
    gram_matrix = (gram_sum + cross + cross.T + block_rows * hdot(centres.T, centres)) / total_rows
    displaced_entries = walk - mean_walk
    normalizer_coefficient = jnp.linalg.cholesky(gram_matrix)
    return jax.scipy.linalg.solve_triangular(
        normalizer_coefficient, displaced_entries.T, lower=True
    ).T


def on_device(embeddings, start, neighbours):
    wide_count = lax.axis_size("wide")
    lane_count = lax.axis_size("narrow")
    broad_index = lax.axis_index("wide")
    lane_index = lax.axis_index("narrow")
    far_reach = wide_count // 2 - 1
    fetch_offsets, pair_plan = difference_plan(wide_count, far_reach)
    unit_block = normalize_rows(embeddings)
    block_rows = unit_block.shape[0]
    total_rows = block_rows * wide_count * lane_count

    def block_at(offset):
        return (broad_index + offset) % wide_count * lane_count + lane_index

    owned_list = []
    for left, right in pair_plan:
        own_row = lax.dynamic_slice_in_dim(neighbours, block_at(left), 1, 0)[0]
        owned_list.append(jnp.any(own_row == block_at(right)))

    units = {0: unit_block}
    weights = {0: start}
    unit_width = unit_block.shape[1]
    vector_count = start.shape[1]
    packed = jnp.concatenate([unit_block, as_rows(start.reshape(-1), unit_width)])
    for offset in fetch_offsets:
        arrived = shifted(packed, "wide", -offset)
        units[offset] = arrived[:block_rows]
        weights[offset] = (
            arrived[block_rows:].reshape(-1)[: block_rows * vector_count].reshape(block_rows, vector_count)
        )

    self_mask = lax.broadcasted_iota(
        jnp.int32, (block_rows, block_rows), 0
    ) == lax.broadcasted_iota(jnp.int32, (block_rows, block_rows), 1)
    near_tile = jnp.where(
        self_mask, jnp.zeros((), jnp.bfloat16), scores_tile(unit_block, unit_block)
    )

    vector_count = start.shape[1]
    zero_part = jnp.zeros((block_rows, vector_count), jnp.float32)
    zero_sum = jnp.zeros((block_rows,), jnp.float32)
    parts = {offset: zero_part for offset in units}
    sums = {offset: zero_sum for offset in units}
    tiles = []
    for (left, right), owned in zip(pair_plan, owned_list):
        affinity, row_part, row_sum, col_part, col_sum = first_pass(
            owned, units[left], units[right], weights[left], weights[right]
        )
        tiles.append(affinity)
        parts[left] = parts[left] + row_part
        sums[left] = sums[left] + row_sum
        parts[right] = parts[right] + col_part
        sums[right] = sums[right] + col_sum

    product = row_product(near_tile, start) + parts[0]
    vertex_valence = jnp.sum(near_tile, axis=1, dtype=jnp.float32) + sums[0]
    part_size = block_rows * vector_count
    for offset in fetch_offsets:
        sent = jnp.concatenate([as_rows(parts[offset].reshape(-1)), as_rows(sums[offset])])
        returned = shifted(sent, "wide", offset).reshape(-1)
        product = product + returned[:part_size].reshape(block_rows, vector_count)
        vertex_valence = vertex_valence + returned[part_size : part_size + block_rows]
    basis = orthonormal(product, vertex_valence, total_rows)

    for iteration in range(1, ITERS):
        current = basis.astype(jnp.bfloat16)
        weights = {0: current}
        for offset in fetch_offsets:
            weights[offset] = shifted(current, "wide", -offset)
        parts = {offset: zero_part for offset in units}
        for (left, right), owned, affinity in zip(pair_plan, owned_list, tiles):
            row_part, col_part = later_pass(owned, affinity, weights[left], weights[right])
            parts[left] = parts[left] + row_part
            parts[right] = parts[right] + col_part
        product = row_product(near_tile, current) + parts[0]
        for offset in fetch_offsets:
            product = product + shifted(parts[offset], "wide", offset)
        basis = orthonormal(product, vertex_valence, total_rows)
    return (basis, vertex_valence / block_rows)


def solution(mesh):
    in_specs = (P(("wide", "narrow"), None), P(("wide", "narrow"), None), P())
    out_specs = (P(("wide", "narrow"), None), P(("wide", "narrow")))
    return jax.shard_map(
        on_device, mesh=mesh, in_specs=in_specs, out_specs=out_specs, check_vma=False
    )
```

```python
from functools import partial
import itertools
import math

import jax
import jax.numpy as jnp
from jax import lax
from jax.sharding import PartitionSpec as P

ITERS = 2


kernel_width_factor = 0.05


def shifted(block, axis, distance):
    devices = range(lax.axis_size(axis))
    route = [((i - distance) % len(devices), i) for i in devices]
    return lax.ppermute(block, axis, route)


def ring_gap(offset, span):
    offset %= span
    return min(offset, span - offset)


def difference_plan(span, far_reach):
    candidates = sorted(range(1, span), key=lambda s: (ring_gap(s, span), s))
    for count in range(1, span):
        best = None
        for chosen in itertools.combinations(candidates, count):
            points = (0,) + chosen
            plan = {}
            for a, b in itertools.permutations(points, 2):
                gap = (b - a) % span
                if 1 <= gap <= far_reach and gap not in plan:
                    plan[gap] = (a, b)
            if len(plan) == far_reach:
                cost = sum(ring_gap(s, span) for s in chosen)
                if best is None or cost < best[0]:
                    best = (cost, chosen, plan)
        if best is not None:
            return list(best[1]), [best[2][gap] for gap in range(1, far_reach + 1)]
    raise ValueError("no plan")


def normalize_rows(values):
    values_wide = values.astype(jnp.float32)
    scaling = lax.rsqrt(jnp.mean(values_wide * values_wide, axis=-1, keepdims=True) + 1e-06)
    return (values_wide * scaling / math.sqrt(values_wide.shape[-1])).astype(jnp.bfloat16)


def scores_tile(leftside_block, right_block):
    kernel_entries = lax.dot_general(
        leftside_block, right_block, (((1,), (1,)), ((), ())), preferred_element_type=jnp.float32
    )
    return jnp.exp(kernel_entries / kernel_width_factor).astype(jnp.bfloat16)


def row_product(affinity, weights):
    return jnp.dot(affinity, weights, preferred_element_type=jnp.float32)


def col_product(affinity, weights):
    return lax.dot_general(
        affinity, weights, (((0,), (0,)), ((), ())), preferred_element_type=jnp.float32
    )


def unpack(packed, block_rows, vector_count):
    weights = packed[block_rows:].reshape(-1)[: block_rows * vector_count]
    return packed[:block_rows], weights.reshape(block_rows, vector_count)


def first_pass(owned, left_packed, right_packed, block_rows, vector_count):

    def compute_pair():
        left_unit, left_weights = unpack(left_packed, block_rows, vector_count)
        right_unit, right_weights = unpack(right_packed, block_rows, vector_count)
        affinity = scores_tile(left_unit, right_unit)
        return (
            affinity,
            row_product(affinity, right_weights),
            jnp.sum(affinity, axis=1, dtype=jnp.float32),
            col_product(affinity, left_weights),
            jnp.sum(affinity, axis=0, dtype=jnp.float32),
        )

    def skip_pair():
        zero_part = jnp.zeros((block_rows, vector_count), jnp.float32)
        zero_sum = jnp.zeros((block_rows,), jnp.float32)
        return (
            jnp.zeros((block_rows, block_rows), jnp.bfloat16),
            zero_part,
            zero_sum,
            zero_part,
            zero_sum,
        )

    return lax.cond(owned, compute_pair, skip_pair)


def later_pass(owned, affinity, left_weights, right_weights):
    block_rows = affinity.shape[0]
    vector_count = left_weights.shape[1]

    def compute_pair():
        return (row_product(affinity, right_weights), col_product(affinity, left_weights))

    def skip_pair():
        zero_part = jnp.zeros((block_rows, vector_count), jnp.float32)
        return (zero_part, zero_part)

    return lax.cond(owned, compute_pair, skip_pair)


def butterfly(axis, summed_rows, block):
    size = lax.axis_size(axis)
    if size & (size - 1):
        return jnp.concatenate(
            [
                lax.psum(block[:summed_rows], axis),
                lax.all_gather(block[summed_rows:], axis, tiled=True),
            ]
        )
    index = lax.axis_index(axis)
    step = 1
    while step < size:
        route = [(i, i ^ step) for i in range(size)]
        other = lax.ppermute(block, axis, route)
        summed = block[:summed_rows] + other[:summed_rows]
        mine = block[summed_rows:]
        theirs = other[summed_rows:]
        upper = (index // step) % 2 == 1
        gathered = jnp.where(
            upper, jnp.concatenate([theirs, mine]), jnp.concatenate([mine, theirs])
        )
        block = jnp.concatenate([summed, gathered])
        step *= 2
    return block


def as_rows(vector, lanes=128):
    pad = (-vector.shape[0]) % lanes
    return jnp.pad(vector, (0, pad)).reshape(-1, lanes)


def hdot(left, right):
    return jnp.dot(left, right, precision=lax.Precision.HIGHEST, preferred_element_type=jnp.float32)


def orthonormal(product, vertex_valence, total_rows):
    block_rows, vector_count = product.shape
    walk = product / vertex_valence[:, None]
    centre = jnp.mean(walk, axis=0)
    centred = walk - centre
    local_gram = hdot(centred.T, centred)
    local_drift = jnp.sum(centred, axis=0)
    summed = jnp.concatenate(
        [
            as_rows(local_gram.reshape(-1)),
            as_rows(jnp.concatenate([jnp.sum(product, axis=0), jnp.sum(vertex_valence)[None]])),
        ]
    )
    summed_rows = summed.shape[0]
    block = jnp.concatenate([summed, as_rows(jnp.concatenate([centre, local_drift]))])
    gather_width = block.shape[0] - summed_rows
    for axis in ("narrow", "wide"):
        block = butterfly(axis, summed_rows, block)
    totals = block[:summed_rows].reshape(-1)
    gram_sum = totals[: vector_count * vector_count].reshape(vector_count, vector_count)
    column_sums = totals[vector_count * vector_count : vector_count * vector_count + vector_count]
    total_degree_sum = totals[vector_count * vector_count + vector_count]
    gathered = block[summed_rows:].reshape(-1, gather_width * 128)
    mean_walk = column_sums / total_degree_sum
    centres = gathered[:, :vector_count] - mean_walk
    drifts = gathered[:, vector_count:]
    cross = hdot(centres.T, drifts)
    gram_matrix = (gram_sum + cross + cross.T + block_rows * hdot(centres.T, centres)) / total_rows
    displaced_entries = walk - mean_walk
    normalizer_coefficient = jnp.linalg.cholesky(gram_matrix)
    return jax.scipy.linalg.solve_triangular(
        normalizer_coefficient, displaced_entries.T, lower=True
    ).T


def on_device(embeddings, start, neighbours):
    wide_count = lax.axis_size("wide")
    lane_count = lax.axis_size("narrow")
    broad_index = lax.axis_index("wide")
    lane_index = lax.axis_index("narrow")
    far_reach = wide_count // 2 - 1
    fetch_offsets, pair_plan = difference_plan(wide_count, far_reach)
    unit_block = normalize_rows(embeddings)
    block_rows = unit_block.shape[0]
    total_rows = block_rows * wide_count * lane_count

    def block_at(offset):
        return (broad_index + offset) % wide_count * lane_count + lane_index

    owned_list = []
    for left, right in pair_plan:
        own_row = lax.dynamic_slice_in_dim(neighbours, block_at(left), 1, 0)[0]
        owned_list.append(jnp.any(own_row == block_at(right)))

    unit_width = unit_block.shape[1]
    vector_count = start.shape[1]
    packed = jnp.concatenate([unit_block, as_rows(start.reshape(-1), unit_width)])
    units = {0: packed}
    for offset in fetch_offsets:
        units[offset] = shifted(packed, "wide", -offset)

    self_mask = lax.broadcasted_iota(
        jnp.int32, (block_rows, block_rows), 0
    ) == lax.broadcasted_iota(jnp.int32, (block_rows, block_rows), 1)
    near_tile = jnp.where(
        self_mask, jnp.zeros((), jnp.bfloat16), scores_tile(unit_block, unit_block)
    )

    zero_part = jnp.zeros((block_rows, vector_count), jnp.float32)
    zero_sum = jnp.zeros((block_rows,), jnp.float32)
    parts = {offset: zero_part for offset in units}
    sums = {offset: zero_sum for offset in units}
    tiles = []
    for (left, right), owned in zip(pair_plan, owned_list):
        affinity, row_part, row_sum, col_part, col_sum = first_pass(
            owned, units[left], units[right], block_rows, vector_count
        )
        tiles.append(affinity)
        parts[left] = parts[left] + row_part
        sums[left] = sums[left] + row_sum
        parts[right] = parts[right] + col_part
        sums[right] = sums[right] + col_sum

    product = row_product(near_tile, start) + parts[0]
    vertex_valence = jnp.sum(near_tile, axis=1, dtype=jnp.float32) + sums[0]
    part_size = block_rows * vector_count
    for offset in fetch_offsets:
        sent = jnp.concatenate([as_rows(parts[offset].reshape(-1)), as_rows(sums[offset])])
        returned = shifted(sent, "wide", offset).reshape(-1)
        product = product + returned[:part_size].reshape(block_rows, vector_count)
        vertex_valence = vertex_valence + returned[part_size : part_size + block_rows]
    basis = orthonormal(product, vertex_valence, total_rows)

    for iteration in range(1, ITERS):
        current = basis.astype(jnp.bfloat16)
        weights = {0: current}
        for offset in fetch_offsets:
            weights[offset] = shifted(current, "wide", -offset)
        parts = {offset: zero_part for offset in units}
        for (left, right), owned, affinity in zip(pair_plan, owned_list, tiles):
            row_part, col_part = later_pass(owned, affinity, weights[left], weights[right])
            parts[left] = parts[left] + row_part
            parts[right] = parts[right] + col_part
        product = row_product(near_tile, current) + parts[0]
        for offset in fetch_offsets:
            product = product + shifted(parts[offset], "wide", offset)
        basis = orthonormal(product, vertex_valence, total_rows)
    return (basis, vertex_valence / block_rows)


def solution(mesh):
    in_specs = (P(("wide", "narrow"), None), P(("wide", "narrow"), None), P())
    out_specs = (P(("wide", "narrow"), None), P(("wide", "narrow")))
    return jax.shard_map(
        on_device, mesh=mesh, in_specs=in_specs, out_specs=out_specs, check_vma=False
    )
```

```python
from functools import partial
import itertools
import math

import jax
import jax.numpy as jnp
from jax import lax
from jax.sharding import PartitionSpec as P

ITERS = 2


kernel_width_factor = 0.05


def shifted(block, axis, distance):
    devices = range(lax.axis_size(axis))
    route = [((i - distance) % len(devices), i) for i in devices]
    return lax.ppermute(block, axis, route)


def ring_gap(offset, span):
    offset %= span
    return min(offset, span - offset)


def difference_plan(span, far_reach):
    candidates = sorted(range(1, span), key=lambda s: (ring_gap(s, span), s))
    for count in range(1, span):
        best = None
        for chosen in itertools.combinations(candidates, count):
            points = (0,) + chosen
            plan = {}
            for a, b in itertools.permutations(points, 2):
                gap = (b - a) % span
                if 1 <= gap <= far_reach and gap not in plan:
                    plan[gap] = (a, b)
            if len(plan) == far_reach:
                cost = sum(ring_gap(s, span) for s in chosen)
                if best is None or cost < best[0]:
                    best = (cost, chosen, plan)
        if best is not None:
            return list(best[1]), [best[2][gap] for gap in range(1, far_reach + 1)]
    raise ValueError("no plan")


def normalize_rows(values):
    values_wide = values.astype(jnp.float32)
    scaling = lax.rsqrt(jnp.mean(values_wide * values_wide, axis=-1, keepdims=True) + 1e-06)
    return (values_wide * scaling / math.sqrt(values_wide.shape[-1])).astype(jnp.bfloat16)


def scores_tile(leftside_block, right_block):
    kernel_entries = lax.dot_general(
        leftside_block, right_block, (((1,), (1,)), ((), ())), preferred_element_type=jnp.float32
    )
    return jnp.exp(kernel_entries / kernel_width_factor).astype(jnp.bfloat16)


def row_product(affinity, weights):
    return jnp.dot(affinity, weights, preferred_element_type=jnp.float32)


def col_product(affinity, weights):
    return lax.dot_general(
        affinity, weights, (((0,), (0,)), ((), ())), preferred_element_type=jnp.float32
    )


def unpack(packed, block_rows, vector_count):
    weights = packed[block_rows:].reshape(-1)[: block_rows * vector_count]
    return packed[:block_rows], weights.reshape(block_rows, vector_count)


def first_pass(owned, left_packed, right_packed, block_rows, vector_count):

    def compute_pair():
        left_unit, left_weights = unpack(left_packed, block_rows, vector_count)
        right_unit, right_weights = unpack(right_packed, block_rows, vector_count)
        affinity = scores_tile(left_unit, right_unit)
        return (
            affinity,
            row_product(affinity, right_weights),
            jnp.sum(affinity, axis=1, dtype=jnp.float32),
            col_product(affinity, left_weights),
            jnp.sum(affinity, axis=0, dtype=jnp.float32),
        )

    def skip_pair():
        zero_part = jnp.zeros((block_rows, vector_count), jnp.float32)
        zero_sum = jnp.zeros((block_rows,), jnp.float32)
        return (
            jnp.zeros((block_rows, block_rows), jnp.bfloat16),
            zero_part,
            zero_sum,
            zero_part,
            zero_sum,
        )

    return lax.cond(owned, compute_pair, skip_pair)


def later_pass(owned, affinity, left_weights, right_weights):
    block_rows = affinity.shape[0]
    vector_count = left_weights.shape[1]

    def compute_pair():
        return (row_product(affinity, right_weights), col_product(affinity, left_weights))

    def skip_pair():
        zero_part = jnp.zeros((block_rows, vector_count), jnp.float32)
        return (zero_part, zero_part)

    return lax.cond(owned, compute_pair, skip_pair)


def butterfly(axis, summed_rows, block):
    size = lax.axis_size(axis)
    if size & (size - 1):
        return jnp.concatenate(
            [
                lax.psum(block[:summed_rows], axis),
                lax.all_gather(block[summed_rows:], axis, tiled=True),
            ]
        )
    index = lax.axis_index(axis)
    step = 1
    while step < size:
        route = [(i, i ^ step) for i in range(size)]
        other = lax.ppermute(block, axis, route)
        summed = block[:summed_rows] + other[:summed_rows]
        mine = block[summed_rows:]
        theirs = other[summed_rows:]
        upper = (index // step) % 2 == 1
        gathered = jnp.where(
            upper, jnp.concatenate([theirs, mine]), jnp.concatenate([mine, theirs])
        )
        block = jnp.concatenate([summed, gathered])
        step *= 2
    return block


def as_rows(vector, lanes=128):
    pad = (-vector.shape[0]) % lanes
    return jnp.pad(vector, (0, pad)).reshape(-1, lanes)


def hdot(left, right):
    return jnp.dot(left, right, precision=lax.Precision.HIGHEST, preferred_element_type=jnp.float32)


def orthonormal(product, vertex_valence, total_rows, fetch_offsets=()):
    block_rows, vector_count = product.shape
    walk = product / vertex_valence[:, None]
    partner_walks = [shifted(walk, "wide", -offset) for offset in fetch_offsets]
    centre = jnp.mean(walk, axis=0)
    centred = walk - centre
    local_gram = hdot(centred.T, centred)
    local_drift = jnp.sum(centred, axis=0)
    summed = jnp.concatenate(
        [
            as_rows(local_gram.reshape(-1)),
            as_rows(jnp.concatenate([jnp.sum(product, axis=0), jnp.sum(vertex_valence)[None]])),
        ]
    )
    summed_rows = summed.shape[0]
    block = jnp.concatenate([summed, as_rows(jnp.concatenate([centre, local_drift]))])
    gather_width = block.shape[0] - summed_rows
    for axis in ("narrow", "wide"):
        block = butterfly(axis, summed_rows, block)
    totals = block[:summed_rows].reshape(-1)
    gram_sum = totals[: vector_count * vector_count].reshape(vector_count, vector_count)
    column_sums = totals[vector_count * vector_count : vector_count * vector_count + vector_count]
    total_degree_sum = totals[vector_count * vector_count + vector_count]
    gathered = block[summed_rows:].reshape(-1, gather_width * 128)
    mean_walk = column_sums / total_degree_sum
    centres = gathered[:, :vector_count] - mean_walk
    drifts = gathered[:, vector_count:]
    cross = hdot(centres.T, drifts)
    gram_matrix = (gram_sum + cross + cross.T + block_rows * hdot(centres.T, centres)) / total_rows
    displaced_entries = jnp.concatenate([walk] + partner_walks) - mean_walk
    normalizer_coefficient = jnp.linalg.cholesky(gram_matrix)
    bases = jax.scipy.linalg.solve_triangular(
        normalizer_coefficient, displaced_entries.T, lower=True
    ).T
    return [bases[i * block_rows : (i + 1) * block_rows] for i in range(1 + len(partner_walks))]


def on_device(embeddings, start, neighbours):
    wide_count = lax.axis_size("wide")
    lane_count = lax.axis_size("narrow")
    broad_index = lax.axis_index("wide")
    lane_index = lax.axis_index("narrow")
    far_reach = wide_count // 2 - 1
    fetch_offsets, pair_plan = difference_plan(wide_count, far_reach)
    unit_block = normalize_rows(embeddings)
    block_rows = unit_block.shape[0]
    total_rows = block_rows * wide_count * lane_count

    def block_at(offset):
        return (broad_index + offset) % wide_count * lane_count + lane_index

    owned_list = []
    for left, right in pair_plan:
        own_row = lax.dynamic_slice_in_dim(neighbours, block_at(left), 1, 0)[0]
        owned_list.append(jnp.any(own_row == block_at(right)))

    unit_width = unit_block.shape[1]
    vector_count = start.shape[1]
    packed = jnp.concatenate([unit_block, as_rows(start.reshape(-1), unit_width)])
    units = {0: packed}
    for offset in fetch_offsets:
        units[offset] = shifted(packed, "wide", -offset)

    self_mask = lax.broadcasted_iota(
        jnp.int32, (block_rows, block_rows), 0
    ) == lax.broadcasted_iota(jnp.int32, (block_rows, block_rows), 1)
    near_tile = jnp.where(
        self_mask, jnp.zeros((), jnp.bfloat16), scores_tile(unit_block, unit_block)
    )

    zero_part = jnp.zeros((block_rows, vector_count), jnp.float32)
    zero_sum = jnp.zeros((block_rows,), jnp.float32)
    parts = {offset: zero_part for offset in units}
    sums = {offset: zero_sum for offset in units}
    tiles = []
    for (left, right), owned in zip(pair_plan, owned_list):
        affinity, row_part, row_sum, col_part, col_sum = first_pass(
            owned, units[left], units[right], block_rows, vector_count
        )
        tiles.append(affinity)
        parts[left] = parts[left] + row_part
        sums[left] = sums[left] + row_sum
        parts[right] = parts[right] + col_part
        sums[right] = sums[right] + col_sum

    product = row_product(near_tile, start) + parts[0]
    vertex_valence = jnp.sum(near_tile, axis=1, dtype=jnp.float32) + sums[0]
    part_size = block_rows * vector_count
    for offset in fetch_offsets:
        sent = jnp.concatenate([as_rows(parts[offset].reshape(-1)), as_rows(sums[offset])])
        returned = shifted(sent, "wide", offset).reshape(-1)
        product = product + returned[:part_size].reshape(block_rows, vector_count)
        vertex_valence = vertex_valence + returned[part_size : part_size + block_rows]
    bases = orthonormal(product, vertex_valence, total_rows, fetch_offsets if ITERS > 1 else ())

    for iteration in range(1, ITERS):
        weights = {0: bases[0].astype(jnp.bfloat16)}
        for position, offset in enumerate(fetch_offsets):
            weights[offset] = bases[position + 1].astype(jnp.bfloat16)
        current = weights[0]
        parts = {offset: zero_part for offset in units}
        for (left, right), owned, affinity in zip(pair_plan, owned_list, tiles):
            row_part, col_part = later_pass(owned, affinity, weights[left], weights[right])
            parts[left] = parts[left] + row_part
            parts[right] = parts[right] + col_part
        product = row_product(near_tile, current) + parts[0]
        for offset in fetch_offsets:
            product = product + shifted(parts[offset], "wide", offset)
        last = iteration == ITERS - 1
        bases = orthonormal(product, vertex_valence, total_rows, () if last else fetch_offsets)
    return (bases[0], vertex_valence / block_rows)


def solution(mesh):
    in_specs = (P(("wide", "narrow"), None), P(("wide", "narrow"), None), P())
    out_specs = (P(("wide", "narrow"), None), P(("wide", "narrow")))
    return jax.shard_map(
        on_device, mesh=mesh, in_specs=in_specs, out_specs=out_specs, check_vma=False
    )
```

```python
from functools import partial
import itertools
import math

import jax
import jax.numpy as jnp
from jax import lax
from jax.sharding import PartitionSpec as P
from jax.experimental import pallas as pl

ITERS = 2


kernel_width_factor = 0.05


def shifted(block, axis, distance):
    devices = range(lax.axis_size(axis))
    route = [((i - distance) % len(devices), i) for i in devices]
    return lax.ppermute(block, axis, route)


def ring_gap(offset, span):
    offset %= span
    return min(offset, span - offset)


def difference_plan(span, far_reach):
    candidates = sorted(range(1, span), key=lambda s: (ring_gap(s, span), s))
    for count in range(1, span):
        best = None
        for chosen in itertools.combinations(candidates, count):
            points = (0,) + chosen
            plan = {}
            for a, b in itertools.permutations(points, 2):
                gap = (b - a) % span
                if 1 <= gap <= far_reach and gap not in plan:
                    plan[gap] = (a, b)
            if len(plan) == far_reach:
                cost = sum(ring_gap(s, span) for s in chosen)
                if best is None or cost < best[0]:
                    best = (cost, chosen, plan)
        if best is not None:
            return list(best[1]), [best[2][gap] for gap in range(1, far_reach + 1)]
    raise ValueError("no plan")


def normalize_rows(values):
    values_wide = values.astype(jnp.float32)
    scaling = lax.rsqrt(jnp.mean(values_wide * values_wide, axis=-1, keepdims=True) + 1e-06)
    return (values_wide * scaling / math.sqrt(values_wide.shape[-1])).astype(jnp.bfloat16)


def scores_tile(leftside_block, right_block):
    kernel_entries = lax.dot_general(
        leftside_block, right_block, (((1,), (1,)), ((), ())), preferred_element_type=jnp.float32
    )
    return jnp.exp(kernel_entries / kernel_width_factor).astype(jnp.bfloat16)


def row_product(affinity, weights):
    return jnp.dot(affinity, weights, preferred_element_type=jnp.float32)


def col_product(affinity, weights):
    return lax.dot_general(
        affinity, weights, (((0,), (0,)), ((), ())), preferred_element_type=jnp.float32
    )


def unpack(packed, block_rows, vector_count):
    weights = packed[block_rows:].reshape(-1)[: block_rows * vector_count]
    return packed[:block_rows], weights.reshape(block_rows, vector_count)


def first_pass(owned, left_packed, right_packed, block_rows, vector_count):

    def compute_pair():
        left_unit, left_weights = unpack(left_packed, block_rows, vector_count)
        right_unit, right_weights = unpack(right_packed, block_rows, vector_count)
        affinity = scores_tile(left_unit, right_unit)
        return (
            affinity,
            row_product(affinity, right_weights),
            jnp.sum(affinity, axis=1, dtype=jnp.float32),
            col_product(affinity, left_weights),
            jnp.sum(affinity, axis=0, dtype=jnp.float32),
        )

    def skip_pair():
        zero_part = jnp.zeros((block_rows, vector_count), jnp.float32)
        zero_sum = jnp.zeros((block_rows,), jnp.float32)
        return (
            jnp.zeros((block_rows, block_rows), jnp.bfloat16),
            zero_part,
            zero_sum,
            zero_part,
            zero_sum,
        )

    return lax.cond(owned, compute_pair, skip_pair)


def later_pass(owned, affinity, left_weights, right_weights):
    block_rows = affinity.shape[0]
    vector_count = left_weights.shape[1]

    def compute_pair():
        return (row_product(affinity, right_weights), col_product(affinity, left_weights))

    def skip_pair():
        zero_part = jnp.zeros((block_rows, vector_count), jnp.float32)
        return (zero_part, zero_part)

    return lax.cond(owned, compute_pair, skip_pair)


def butterfly(axis, summed_rows, block):
    size = lax.axis_size(axis)
    if size & (size - 1):
        return jnp.concatenate(
            [
                lax.psum(block[:summed_rows], axis),
                lax.all_gather(block[summed_rows:], axis, tiled=True),
            ]
        )
    index = lax.axis_index(axis)
    step = 1
    while step < size:
        route = [(i, i ^ step) for i in range(size)]
        other = lax.ppermute(block, axis, route)
        summed = block[:summed_rows] + other[:summed_rows]
        mine = block[summed_rows:]
        theirs = other[summed_rows:]
        upper = (index // step) % 2 == 1
        gathered = jnp.where(
            upper, jnp.concatenate([theirs, mine]), jnp.concatenate([mine, theirs])
        )
        block = jnp.concatenate([summed, gathered])
        step *= 2
    return block


def as_rows(vector, lanes=128):
    pad = (-vector.shape[0]) % lanes
    return jnp.pad(vector, (0, pad)).reshape(-1, lanes)


def hdot(left, right):
    return jnp.dot(left, right, precision=lax.Precision.HIGHEST, preferred_element_type=jnp.float32)


def factor_kernel(gram_ref, inverse_ref):
    size = gram_ref.shape[0]
    rows = lax.broadcasted_iota(jnp.int32, (size, size), 0)
    cols = lax.broadcasted_iota(jnp.int32, (size, size), 1)
    eye = jnp.where(rows == cols, 1.0, 0.0).astype(jnp.float32)

    def step(j, carry):
        remaining, inverse = carry
        column = jnp.sum(jnp.where(cols == j, remaining, 0.0), axis=1, keepdims=True)
        pivot = jnp.sum(jnp.where(rows[:, :1] == j, column, 0.0), axis=0, keepdims=True)
        scale = lax.rsqrt(pivot)
        factor_column = jnp.where(rows[:, :1] >= j, column * scale, 0.0)
        factor_row = jnp.sum(jnp.where(rows == j, remaining, 0.0), axis=0, keepdims=True)
        factor_row = jnp.where(cols[:1] >= j, factor_row * scale, 0.0)
        remaining = remaining - factor_column * factor_row
        inverse_row = jnp.sum(jnp.where(rows == j, inverse, 0.0), axis=0, keepdims=True) * scale
        inverse = jnp.where(rows == j, inverse_row, inverse)
        below = jnp.where(rows[:, :1] > j, factor_column, 0.0)
        inverse = inverse - below * inverse_row
        return remaining, inverse

    _, inverse = lax.fori_loop(0, size, step, (gram_ref[...], eye))
    inverse_ref[...] = inverse


def factor_inverse(gram_matrix):
    return pl.pallas_call(
        factor_kernel, out_shape=jax.ShapeDtypeStruct(gram_matrix.shape, jnp.float32)
    )(gram_matrix)


def orthonormal(product, vertex_valence, total_rows, fetch_offsets=()):
    block_rows, vector_count = product.shape
    walk = product / vertex_valence[:, None]
    partner_walks = [shifted(walk, "wide", -offset) for offset in fetch_offsets]
    centre = jnp.mean(walk, axis=0)
    centred = walk - centre
    local_gram = hdot(centred.T, centred)
    local_drift = jnp.sum(centred, axis=0)
    summed = jnp.concatenate(
        [
            as_rows(local_gram.reshape(-1)),
            as_rows(jnp.concatenate([jnp.sum(product, axis=0), jnp.sum(vertex_valence)[None]])),
        ]
    )
    summed_rows = summed.shape[0]
    block = jnp.concatenate([summed, as_rows(jnp.concatenate([centre, local_drift]))])
    gather_width = block.shape[0] - summed_rows
    for axis in ("narrow", "wide"):
        block = butterfly(axis, summed_rows, block)
    totals = block[:summed_rows].reshape(-1)
    gram_sum = totals[: vector_count * vector_count].reshape(vector_count, vector_count)
    column_sums = totals[vector_count * vector_count : vector_count * vector_count + vector_count]
    total_degree_sum = totals[vector_count * vector_count + vector_count]
    gathered = block[summed_rows:].reshape(-1, gather_width * 128)
    mean_walk = column_sums / total_degree_sum
    centres = gathered[:, :vector_count] - mean_walk
    drifts = gathered[:, vector_count:]
    cross = hdot(centres.T, drifts)
    gram_matrix = (gram_sum + cross + cross.T + block_rows * hdot(centres.T, centres)) / total_rows
    displaced_entries = jnp.concatenate([walk] + partner_walks) - mean_walk
    inverse_factor = factor_inverse(gram_matrix)
    bases = hdot(displaced_entries, inverse_factor.T)
    return [bases[i * block_rows : (i + 1) * block_rows] for i in range(1 + len(partner_walks))]


def on_device(embeddings, start, neighbours):
    wide_count = lax.axis_size("wide")
    lane_count = lax.axis_size("narrow")
    broad_index = lax.axis_index("wide")
    lane_index = lax.axis_index("narrow")
    far_reach = wide_count // 2 - 1
    fetch_offsets, pair_plan = difference_plan(wide_count, far_reach)
    unit_block = normalize_rows(embeddings)
    block_rows = unit_block.shape[0]
    total_rows = block_rows * wide_count * lane_count

    def block_at(offset):
        return (broad_index + offset) % wide_count * lane_count + lane_index

    owned_list = []
    for left, right in pair_plan:
        own_row = lax.dynamic_slice_in_dim(neighbours, block_at(left), 1, 0)[0]
        owned_list.append(jnp.any(own_row == block_at(right)))

    unit_width = unit_block.shape[1]
    vector_count = start.shape[1]
    packed = jnp.concatenate([unit_block, as_rows(start.reshape(-1), unit_width)])
    units = {0: packed}
    for offset in fetch_offsets:
        units[offset] = shifted(packed, "wide", -offset)

    self_mask = lax.broadcasted_iota(
        jnp.int32, (block_rows, block_rows), 0
    ) == lax.broadcasted_iota(jnp.int32, (block_rows, block_rows), 1)
    near_tile = jnp.where(
        self_mask, jnp.zeros((), jnp.bfloat16), scores_tile(unit_block, unit_block)
    )

    zero_part = jnp.zeros((block_rows, vector_count), jnp.float32)
    zero_sum = jnp.zeros((block_rows,), jnp.float32)
    parts = {offset: zero_part for offset in units}
    sums = {offset: zero_sum for offset in units}
    tiles = []
    for (left, right), owned in zip(pair_plan, owned_list):
        affinity, row_part, row_sum, col_part, col_sum = first_pass(
            owned, units[left], units[right], block_rows, vector_count
        )
        tiles.append(affinity)
        parts[left] = parts[left] + row_part
        sums[left] = sums[left] + row_sum
        parts[right] = parts[right] + col_part
        sums[right] = sums[right] + col_sum

    product = row_product(near_tile, start) + parts[0]
    vertex_valence = jnp.sum(near_tile, axis=1, dtype=jnp.float32) + sums[0]
    part_size = block_rows * vector_count
    for offset in fetch_offsets:
        sent = jnp.concatenate([as_rows(parts[offset].reshape(-1)), as_rows(sums[offset])])
        returned = shifted(sent, "wide", offset).reshape(-1)
        product = product + returned[:part_size].reshape(block_rows, vector_count)
        vertex_valence = vertex_valence + returned[part_size : part_size + block_rows]
    bases = orthonormal(product, vertex_valence, total_rows, fetch_offsets if ITERS > 1 else ())

    for iteration in range(1, ITERS):
        weights = {0: bases[0].astype(jnp.bfloat16)}
        for position, offset in enumerate(fetch_offsets):
            weights[offset] = bases[position + 1].astype(jnp.bfloat16)
        current = weights[0]
        parts = {offset: zero_part for offset in units}
        for (left, right), owned, affinity in zip(pair_plan, owned_list, tiles):
            row_part, col_part = later_pass(owned, affinity, weights[left], weights[right])
            parts[left] = parts[left] + row_part
            parts[right] = parts[right] + col_part
        product = row_product(near_tile, current) + parts[0]
        for offset in fetch_offsets:
            product = product + shifted(parts[offset], "wide", offset)
        last = iteration == ITERS - 1
        bases = orthonormal(product, vertex_valence, total_rows, () if last else fetch_offsets)
    return (bases[0], vertex_valence / block_rows)


def solution(mesh):
    in_specs = (P(("wide", "narrow"), None), P(("wide", "narrow"), None), P())
    out_specs = (P(("wide", "narrow"), None), P(("wide", "narrow")))
    return jax.shard_map(
        on_device, mesh=mesh, in_specs=in_specs, out_specs=out_specs, check_vma=False
    )
```

```python
from functools import partial
import itertools
import math

import jax
import jax.numpy as jnp
from jax import lax
from jax.sharding import PartitionSpec as P
from jax.experimental import pallas as pl

ITERS = 2


kernel_width_factor = 0.05


def shifted(block, axis, distance):
    devices = range(lax.axis_size(axis))
    route = [((i - distance) % len(devices), i) for i in devices]
    return lax.ppermute(block, axis, route)


def ring_gap(offset, span):
    offset %= span
    return min(offset, span - offset)


def difference_plan(span, far_reach):
    candidates = sorted(range(1, span), key=lambda s: (ring_gap(s, span), s))
    for count in range(1, span):
        best = None
        for chosen in itertools.combinations(candidates, count):
            points = (0,) + chosen
            plan = {}
            for a, b in itertools.permutations(points, 2):
                gap = (b - a) % span
                if 1 <= gap <= far_reach and gap not in plan:
                    plan[gap] = (a, b)
            if len(plan) == far_reach:
                cost = sum(ring_gap(s, span) for s in chosen)
                if best is None or cost < best[0]:
                    best = (cost, chosen, plan)
        if best is not None:
            return list(best[1]), [best[2][gap] for gap in range(1, far_reach + 1)]
    raise ValueError("no plan")


def normalize_rows(values):
    values_wide = values.astype(jnp.float32)
    scaling = lax.rsqrt(jnp.mean(values_wide * values_wide, axis=-1, keepdims=True) + 1e-06)
    return (values_wide * scaling / math.sqrt(values_wide.shape[-1])).astype(jnp.bfloat16)


def scores_tile(leftside_block, right_block):
    kernel_entries = lax.dot_general(
        leftside_block, right_block, (((1,), (1,)), ((), ())), preferred_element_type=jnp.float32
    )
    return jnp.exp(kernel_entries / kernel_width_factor).astype(jnp.bfloat16)


def row_product(affinity, weights):
    return jnp.dot(affinity, weights, preferred_element_type=jnp.float32)


def col_product(affinity, weights):
    return lax.dot_general(
        affinity, weights, (((0,), (0,)), ((), ())), preferred_element_type=jnp.float32
    )


def first_pass(owned, left_unit, right_unit, left_weights, right_weights):
    block_rows = left_unit.shape[0]
    vector_count = left_weights.shape[1]

    def compute_pair():
        affinity = scores_tile(left_unit, right_unit)
        return (
            affinity,
            row_product(affinity, right_weights),
            jnp.sum(affinity, axis=1, dtype=jnp.float32),
            col_product(affinity, left_weights),
            jnp.sum(affinity, axis=0, dtype=jnp.float32),
        )

    def skip_pair():
        zero_part = jnp.zeros((block_rows, vector_count), jnp.float32)
        zero_sum = jnp.zeros((block_rows,), jnp.float32)
        return (
            jnp.zeros((block_rows, block_rows), jnp.bfloat16),
            zero_part,
            zero_sum,
            zero_part,
            zero_sum,
        )

    return lax.cond(owned, compute_pair, skip_pair)


def later_pass(owned, affinity, left_weights, right_weights):
    block_rows = affinity.shape[0]
    vector_count = left_weights.shape[1]

    def compute_pair():
        return (row_product(affinity, right_weights), col_product(affinity, left_weights))

    def skip_pair():
        zero_part = jnp.zeros((block_rows, vector_count), jnp.float32)
        return (zero_part, zero_part)

    return lax.cond(owned, compute_pair, skip_pair)


def butterfly(axis, summed_rows, block):
    size = lax.axis_size(axis)
    if size & (size - 1):
        return jnp.concatenate(
            [
                lax.psum(block[:summed_rows], axis),
                lax.all_gather(block[summed_rows:], axis, tiled=True),
            ]
        )
    index = lax.axis_index(axis)
    step = 1
    while step < size:
        route = [(i, i ^ step) for i in range(size)]
        other = lax.ppermute(block, axis, route)
        summed = block[:summed_rows] + other[:summed_rows]
        mine = block[summed_rows:]
        theirs = other[summed_rows:]
        upper = (index // step) % 2 == 1
        gathered = jnp.where(
            upper, jnp.concatenate([theirs, mine]), jnp.concatenate([mine, theirs])
        )
        block = jnp.concatenate([summed, gathered])
        step *= 2
    return block


def as_rows(vector, lanes=128):
    pad = (-vector.shape[0]) % lanes
    return jnp.pad(vector, (0, pad)).reshape(-1, lanes)


def hdot(left, right):
    return jnp.dot(left, right, precision=lax.Precision.HIGHEST, preferred_element_type=jnp.float32)


def factor_kernel(gram_ref, inverse_ref):
    size = gram_ref.shape[0]
    rows = lax.broadcasted_iota(jnp.int32, (size, size), 0)
    cols = lax.broadcasted_iota(jnp.int32, (size, size), 1)
    eye = jnp.where(rows == cols, 1.0, 0.0).astype(jnp.float32)

    def step(j, carry):
        remaining, inverse = carry
        column = jnp.sum(jnp.where(cols == j, remaining, 0.0), axis=1, keepdims=True)
        pivot = jnp.sum(jnp.where(rows[:, :1] == j, column, 0.0), axis=0, keepdims=True)
        scale = lax.rsqrt(pivot)
        factor_column = jnp.where(rows[:, :1] >= j, column * scale, 0.0)
        factor_row = jnp.sum(jnp.where(rows == j, remaining, 0.0), axis=0, keepdims=True)
        factor_row = jnp.where(cols[:1] >= j, factor_row * scale, 0.0)
        remaining = remaining - factor_column * factor_row
        inverse_row = jnp.sum(jnp.where(rows == j, inverse, 0.0), axis=0, keepdims=True) * scale
        inverse = jnp.where(rows == j, inverse_row, inverse)
        below = jnp.where(rows[:, :1] > j, factor_column, 0.0)
        inverse = inverse - below * inverse_row
        return remaining, inverse

    _, inverse = lax.fori_loop(0, size, step, (gram_ref[...], eye))
    inverse_ref[...] = inverse


def factor_inverse(gram_matrix):
    return pl.pallas_call(
        factor_kernel, out_shape=jax.ShapeDtypeStruct(gram_matrix.shape, jnp.float32)
    )(gram_matrix)


def orthonormal(product, vertex_valence, total_rows, fetch_offsets=()):
    block_rows, vector_count = product.shape
    walk = product / vertex_valence[:, None]
    partner_walks = [shifted(walk, "wide", -offset) for offset in fetch_offsets]
    centre = jnp.mean(walk, axis=0)
    centred = walk - centre
    local_gram = hdot(centred.T, centred)
    local_drift = jnp.sum(centred, axis=0)
    summed = jnp.concatenate(
        [
            as_rows(local_gram.reshape(-1)),
            as_rows(jnp.concatenate([jnp.sum(product, axis=0), jnp.sum(vertex_valence)[None]])),
        ]
    )
    summed_rows = summed.shape[0]
    block = jnp.concatenate([summed, as_rows(jnp.concatenate([centre, local_drift]))])
    gather_width = block.shape[0] - summed_rows
    for axis in ("narrow", "wide"):
        block = butterfly(axis, summed_rows, block)
    totals = block[:summed_rows].reshape(-1)
    gram_sum = totals[: vector_count * vector_count].reshape(vector_count, vector_count)
    column_sums = totals[vector_count * vector_count : vector_count * vector_count + vector_count]
    total_degree_sum = totals[vector_count * vector_count + vector_count]
    gathered = block[summed_rows:].reshape(-1, gather_width * 128)
    mean_walk = column_sums / total_degree_sum
    centres = gathered[:, :vector_count] - mean_walk
    drifts = gathered[:, vector_count:]
    cross = hdot(centres.T, drifts)
    gram_matrix = (gram_sum + cross + cross.T + block_rows * hdot(centres.T, centres)) / total_rows
    displaced_entries = jnp.concatenate([walk] + partner_walks) - mean_walk
    inverse_factor = factor_inverse(gram_matrix)
    bases = hdot(displaced_entries, inverse_factor.T)
    return [bases[i * block_rows : (i + 1) * block_rows] for i in range(1 + len(partner_walks))]


def on_device(embeddings, start, neighbours):
    wide_count = lax.axis_size("wide")
    lane_count = lax.axis_size("narrow")
    broad_index = lax.axis_index("wide")
    lane_index = lax.axis_index("narrow")
    far_reach = wide_count // 2 - 1
    fetch_offsets, pair_plan = difference_plan(wide_count, far_reach)
    unit_block = normalize_rows(embeddings)
    block_rows = unit_block.shape[0]
    total_rows = block_rows * wide_count * lane_count

    def block_at(offset):
        return (broad_index + offset) % wide_count * lane_count + lane_index

    owned_list = []
    for left, right in pair_plan:
        own_row = lax.dynamic_slice_in_dim(neighbours, block_at(left), 1, 0)[0]
        owned_list.append(jnp.any(own_row == block_at(right)))

    vector_count = start.shape[1]
    units = {0: unit_block}
    weights = {0: start}
    for offset in fetch_offsets:
        units[offset] = normalize_rows(shifted(embeddings, "wide", -offset))
        weights[offset] = shifted(start, "wide", -offset)

    self_mask = lax.broadcasted_iota(
        jnp.int32, (block_rows, block_rows), 0
    ) == lax.broadcasted_iota(jnp.int32, (block_rows, block_rows), 1)
    near_tile = jnp.where(
        self_mask, jnp.zeros((), jnp.bfloat16), scores_tile(unit_block, unit_block)
    )

    zero_part = jnp.zeros((block_rows, vector_count), jnp.float32)
    zero_sum = jnp.zeros((block_rows,), jnp.float32)
    parts = {offset: zero_part for offset in units}
    sums = {offset: zero_sum for offset in units}
    tiles = []
    for (left, right), owned in zip(pair_plan, owned_list):
        affinity, row_part, row_sum, col_part, col_sum = first_pass(
            owned, units[left], units[right], weights[left], weights[right]
        )
        tiles.append(affinity)
        parts[left] = parts[left] + row_part
        sums[left] = sums[left] + row_sum
        parts[right] = parts[right] + col_part
        sums[right] = sums[right] + col_sum

    product = row_product(near_tile, start) + parts[0]
    vertex_valence = jnp.sum(near_tile, axis=1, dtype=jnp.float32) + sums[0]
    part_size = block_rows * vector_count
    for offset in fetch_offsets:
        sent = jnp.concatenate([as_rows(parts[offset].reshape(-1)), as_rows(sums[offset])])
        returned = shifted(sent, "wide", offset).reshape(-1)
        product = product + returned[:part_size].reshape(block_rows, vector_count)
        vertex_valence = vertex_valence + returned[part_size : part_size + block_rows]
    bases = orthonormal(product, vertex_valence, total_rows, fetch_offsets if ITERS > 1 else ())

    for iteration in range(1, ITERS):
        weights = {0: bases[0].astype(jnp.bfloat16)}
        for position, offset in enumerate(fetch_offsets):
            weights[offset] = bases[position + 1].astype(jnp.bfloat16)
        current = weights[0]
        parts = {offset: zero_part for offset in units}
        for (left, right), owned, affinity in zip(pair_plan, owned_list, tiles):
            row_part, col_part = later_pass(owned, affinity, weights[left], weights[right])
            parts[left] = parts[left] + row_part
            parts[right] = parts[right] + col_part
        product = row_product(near_tile, current) + parts[0]
        for offset in fetch_offsets:
            product = product + shifted(parts[offset], "wide", offset)
        last = iteration == ITERS - 1
        bases = orthonormal(product, vertex_valence, total_rows, () if last else fetch_offsets)
    return (bases[0], vertex_valence / block_rows)


def solution(mesh):
    in_specs = (P(("wide", "narrow"), None), P(("wide", "narrow"), None), P())
    out_specs = (P(("wide", "narrow"), None), P(("wide", "narrow")))
    return jax.shard_map(
        on_device, mesh=mesh, in_specs=in_specs, out_specs=out_specs, check_vma=False
    )
```

```python
from functools import partial
import itertools
import math

import jax
import jax.numpy as jnp
from jax import lax
from jax.sharding import PartitionSpec as P
from jax.experimental import pallas as pl

ITERS = 2


kernel_width_factor = 0.05


def shifted(block, axis, distance):
    devices = range(lax.axis_size(axis))
    route = [((i - distance) % len(devices), i) for i in devices]
    return lax.ppermute(block, axis, route)


def ring_gap(offset, span):
    offset %= span
    return min(offset, span - offset)


def difference_plan(span, far_reach):
    candidates = sorted(range(1, span), key=lambda s: (ring_gap(s, span), s))
    for count in range(1, span):
        best = None
        for chosen in itertools.combinations(candidates, count):
            points = (0,) + chosen
            plan = {}
            for a, b in itertools.permutations(points, 2):
                gap = (b - a) % span
                if 1 <= gap <= far_reach and gap not in plan:
                    plan[gap] = (a, b)
            if len(plan) == far_reach:
                cost = sum(ring_gap(s, span) for s in chosen)
                if best is None or cost < best[0]:
                    best = (cost, chosen, plan)
        if best is not None:
            return list(best[1]), [best[2][gap] for gap in range(1, far_reach + 1)]
    raise ValueError("no plan")


def normalize_rows(values):
    values_wide = values.astype(jnp.float32)
    scaling = lax.rsqrt(jnp.mean(values_wide * values_wide, axis=-1, keepdims=True) + 1e-06)
    return (values_wide * scaling / math.sqrt(values_wide.shape[-1])).astype(jnp.bfloat16)


def scores_tile(leftside_block, right_block):
    kernel_entries = lax.dot_general(
        leftside_block, right_block, (((1,), (1,)), ((), ())), preferred_element_type=jnp.float32
    )
    return jnp.exp(kernel_entries / kernel_width_factor).astype(jnp.bfloat16)


def row_product(affinity, weights):
    return jnp.dot(affinity, weights, preferred_element_type=jnp.float32)


def col_product(affinity, weights):
    return lax.dot_general(
        affinity, weights, (((0,), (0,)), ((), ())), preferred_element_type=jnp.float32
    )


def first_pass(owned, left_unit, right_unit, left_weights, right_weights):
    block_rows = left_unit.shape[0]
    vector_count = left_weights.shape[1]

    def compute_pair():
        affinity = scores_tile(left_unit, right_unit)
        return (
            affinity,
            row_product(affinity, right_weights),
            jnp.sum(affinity, axis=1, dtype=jnp.float32),
            col_product(affinity, left_weights),
            jnp.sum(affinity, axis=0, dtype=jnp.float32),
        )

    def skip_pair():
        zero_part = jnp.zeros((block_rows, vector_count), jnp.float32)
        zero_sum = jnp.zeros((block_rows,), jnp.float32)
        return (
            jnp.zeros((block_rows, block_rows), jnp.bfloat16),
            zero_part,
            zero_sum,
            zero_part,
            zero_sum,
        )

    return lax.cond(owned, compute_pair, skip_pair)


def later_pass(owned, affinity, left_weights, right_weights):
    block_rows = affinity.shape[0]
    vector_count = left_weights.shape[1]

    def compute_pair():
        return (row_product(affinity, right_weights), col_product(affinity, left_weights))

    def skip_pair():
        zero_part = jnp.zeros((block_rows, vector_count), jnp.float32)
        return (zero_part, zero_part)

    return lax.cond(owned, compute_pair, skip_pair)


def butterfly(axis, summed_rows, block):
    size = lax.axis_size(axis)
    if size & (size - 1):
        return jnp.concatenate(
            [
                lax.psum(block[:summed_rows], axis),
                lax.all_gather(block[summed_rows:], axis, tiled=True),
            ]
        )
    index = lax.axis_index(axis)
    step = 1
    while step < size:
        route = [(i, i ^ step) for i in range(size)]
        other = lax.ppermute(block, axis, route)
        summed = block[:summed_rows] + other[:summed_rows]
        mine = block[summed_rows:]
        theirs = other[summed_rows:]
        upper = (index // step) % 2 == 1
        gathered = jnp.where(
            upper, jnp.concatenate([theirs, mine]), jnp.concatenate([mine, theirs])
        )
        block = jnp.concatenate([summed, gathered])
        step *= 2
    return block


def as_rows(vector, lanes=128):
    pad = (-vector.shape[0]) % lanes
    return jnp.pad(vector, (0, pad)).reshape(-1, lanes)


def hdot(left, right):
    return jnp.dot(left, right, precision=lax.Precision.HIGHEST, preferred_element_type=jnp.float32)


def factor_kernel(gram_ref, inverse_ref):
    size = gram_ref.shape[0]
    rows = lax.broadcasted_iota(jnp.int32, (size, size), 0)
    cols = lax.broadcasted_iota(jnp.int32, (size, size), 1)
    eye = jnp.where(rows == cols, 1.0, 0.0).astype(jnp.float32)

    def step(j, carry):
        remaining, inverse = carry
        column = jnp.sum(jnp.where(cols == j, remaining, 0.0), axis=1, keepdims=True)
        pivot = jnp.sum(jnp.where(rows[:, :1] == j, column, 0.0), axis=0, keepdims=True)
        scale = lax.rsqrt(pivot)
        factor_column = jnp.where(rows[:, :1] >= j, column * scale, 0.0)
        factor_row = jnp.sum(jnp.where(rows == j, remaining, 0.0), axis=0, keepdims=True)
        factor_row = jnp.where(cols[:1] >= j, factor_row * scale, 0.0)
        remaining = remaining - factor_column * factor_row
        inverse_row = jnp.sum(jnp.where(rows == j, inverse, 0.0), axis=0, keepdims=True) * scale
        inverse = jnp.where(rows == j, inverse_row, inverse)
        below = jnp.where(rows[:, :1] > j, factor_column, 0.0)
        inverse = inverse - below * inverse_row
        return remaining, inverse

    _, inverse = lax.fori_loop(0, size, step, (gram_ref[...], eye))
    inverse_ref[...] = inverse


def factor_inverse(gram_matrix):
    return pl.pallas_call(
        factor_kernel, out_shape=jax.ShapeDtypeStruct(gram_matrix.shape, jnp.float32)
    )(gram_matrix)


def orthonormal(product, vertex_valence, total_rows, fetch_offsets=()):
    block_rows, vector_count = product.shape
    walk = product / vertex_valence[:, None]
    partner_walks = [shifted(walk, "wide", -offset) for offset in fetch_offsets]
    centre = jnp.mean(walk, axis=0)
    centred = walk - centre
    local_gram = hdot(centred.T, centred)
    local_drift = jnp.sum(centred, axis=0)
    summed = jnp.concatenate(
        [
            as_rows(local_gram.reshape(-1)),
            as_rows(jnp.concatenate([jnp.sum(product, axis=0), jnp.sum(vertex_valence)[None]])),
        ]
    )
    summed_rows = summed.shape[0]
    block = jnp.concatenate([summed, as_rows(jnp.concatenate([centre, local_drift]))])
    gather_width = block.shape[0] - summed_rows
    for axis in ("narrow", "wide"):
        block = butterfly(axis, summed_rows, block)
    totals = block[:summed_rows].reshape(-1)
    gram_sum = totals[: vector_count * vector_count].reshape(vector_count, vector_count)
    column_sums = totals[vector_count * vector_count : vector_count * vector_count + vector_count]
    total_degree_sum = totals[vector_count * vector_count + vector_count]
    gathered = block[summed_rows:].reshape(-1, gather_width * 128)
    mean_walk = column_sums / total_degree_sum
    centres = gathered[:, :vector_count] - mean_walk
    drifts = gathered[:, vector_count:]
    cross = hdot(centres.T, drifts)
    gram_matrix = (gram_sum + cross + cross.T + block_rows * hdot(centres.T, centres)) / total_rows
    displaced_entries = jnp.concatenate([walk] + partner_walks) - mean_walk
    inverse_factor = factor_inverse(gram_matrix)
    bases = hdot(displaced_entries, inverse_factor.T)
    return [bases[i * block_rows : (i + 1) * block_rows] for i in range(1 + len(partner_walks))]


def on_device(embeddings, start, neighbours):
    wide_count = lax.axis_size("wide")
    lane_count = lax.axis_size("narrow")
    broad_index = lax.axis_index("wide")
    lane_index = lax.axis_index("narrow")
    far_reach = wide_count // 2 - 1
    fetch_offsets, pair_plan = difference_plan(wide_count, far_reach)
    unit_block = normalize_rows(embeddings)
    block_rows = unit_block.shape[0]
    total_rows = block_rows * wide_count * lane_count

    def block_at(offset):
        return (broad_index + offset) % wide_count * lane_count + lane_index

    owned_list = []
    for left, right in pair_plan:
        own_row = lax.dynamic_slice_in_dim(neighbours, block_at(left), 1, 0)[0]
        owned_list.append(jnp.any(own_row == block_at(right)))

    vector_count = start.shape[1]
    units = {0: unit_block}
    weights = {0: start}
    for offset in fetch_offsets:
        units[offset] = shifted(unit_block, "wide", -offset)
        weights[offset] = shifted(start, "wide", -offset)

    self_mask = lax.broadcasted_iota(
        jnp.int32, (block_rows, block_rows), 0
    ) == lax.broadcasted_iota(jnp.int32, (block_rows, block_rows), 1)
    near_tile = jnp.where(
        self_mask, jnp.zeros((), jnp.bfloat16), scores_tile(unit_block, unit_block)
    )

    zero_part = jnp.zeros((block_rows, vector_count), jnp.float32)
    zero_sum = jnp.zeros((block_rows,), jnp.float32)
    parts = {offset: zero_part for offset in units}
    sums = {offset: zero_sum for offset in units}
    tiles = []
    for (left, right), owned in zip(pair_plan, owned_list):
        affinity, row_part, row_sum, col_part, col_sum = first_pass(
            owned, units[left], units[right], weights[left], weights[right]
        )
        tiles.append(affinity)
        parts[left] = parts[left] + row_part
        sums[left] = sums[left] + row_sum
        parts[right] = parts[right] + col_part
        sums[right] = sums[right] + col_sum

    product = row_product(near_tile, start) + parts[0]
    vertex_valence = jnp.sum(near_tile, axis=1, dtype=jnp.float32) + sums[0]
    part_size = block_rows * vector_count
    for offset in fetch_offsets:
        sent = jnp.concatenate([as_rows(parts[offset].reshape(-1)), as_rows(sums[offset])])
        returned = shifted(sent, "wide", offset).reshape(-1)
        product = product + returned[:part_size].reshape(block_rows, vector_count)
        vertex_valence = vertex_valence + returned[part_size : part_size + block_rows]
    bases = orthonormal(product, vertex_valence, total_rows, fetch_offsets if ITERS > 1 else ())

    for iteration in range(1, ITERS):
        weights = {0: bases[0].astype(jnp.bfloat16)}
        for position, offset in enumerate(fetch_offsets):
            weights[offset] = bases[position + 1].astype(jnp.bfloat16)
        current = weights[0]
        parts = {offset: zero_part for offset in units}
        for (left, right), owned, affinity in zip(pair_plan, owned_list, tiles):
            row_part, col_part = later_pass(owned, affinity, weights[left], weights[right])
            parts[left] = parts[left] + row_part
            parts[right] = parts[right] + col_part
        product = row_product(near_tile, current) + parts[0]
        for offset in fetch_offsets:
            product = product + shifted(parts[offset], "wide", offset)
        last = iteration == ITERS - 1
        bases = orthonormal(product, vertex_valence, total_rows, () if last else fetch_offsets)
    return (bases[0], vertex_valence / block_rows)


def solution(mesh):
    in_specs = (P(("wide", "narrow"), None), P(("wide", "narrow"), None), P())
    out_specs = (P(("wide", "narrow"), None), P(("wide", "narrow")))
    return jax.shard_map(
        on_device, mesh=mesh, in_specs=in_specs, out_specs=out_specs, check_vma=False
    )
```

```python
from functools import partial
import itertools
import math

import jax
import jax.numpy as jnp
from jax import lax
from jax.sharding import PartitionSpec as P
from jax.experimental import pallas as pl

ITERS = 2


kernel_width_factor = 0.05


def shifted(block, axis, distance):
    devices = range(lax.axis_size(axis))
    route = [((i - distance) % len(devices), i) for i in devices]
    return lax.ppermute(block, axis, route)


def ring_gap(offset, span):
    offset %= span
    return min(offset, span - offset)


def difference_plan(span, far_reach):
    candidates = sorted(range(1, span), key=lambda s: (ring_gap(s, span), s))
    for count in range(1, span):
        best = None
        for chosen in itertools.combinations(candidates, count):
            points = (0,) + chosen
            plan = {}
            for a, b in itertools.permutations(points, 2):
                gap = (b - a) % span
                if 1 <= gap <= far_reach and gap not in plan:
                    plan[gap] = (a, b)
            if len(plan) == far_reach:
                cost = sum(ring_gap(s, span) for s in chosen)
                if best is None or cost < best[0]:
                    best = (cost, chosen, plan)
        if best is not None:
            return list(best[1]), [best[2][gap] for gap in range(1, far_reach + 1)]
    raise ValueError("no plan")


def normalize_rows(values):
    values_wide = values.astype(jnp.float32)
    scaling = lax.rsqrt(jnp.mean(values_wide * values_wide, axis=-1, keepdims=True) + 1e-06)
    return (values_wide * scaling / math.sqrt(values_wide.shape[-1])).astype(jnp.bfloat16)


def scores_tile(leftside_block, right_block):
    kernel_entries = lax.dot_general(
        leftside_block, right_block, (((1,), (1,)), ((), ())), preferred_element_type=jnp.float32
    )
    return jnp.exp(kernel_entries / kernel_width_factor).astype(jnp.bfloat16)


def row_product(affinity, weights):
    return jnp.dot(affinity, weights, preferred_element_type=jnp.float32)


def col_product(affinity, weights):
    return lax.dot_general(
        affinity, weights, (((0,), (0,)), ((), ())), preferred_element_type=jnp.float32
    )


def first_pass(owned, left_unit, right_unit, left_weights, right_weights):
    block_rows = left_unit.shape[0]
    vector_count = left_weights.shape[1]

    def compute_pair():
        affinity = scores_tile(left_unit, right_unit)
        return (
            affinity,
            row_product(affinity, right_weights),
            jnp.sum(affinity, axis=1, dtype=jnp.float32),
            col_product(affinity, left_weights),
            jnp.sum(affinity, axis=0, dtype=jnp.float32),
        )

    def skip_pair():
        zero_part = jnp.zeros((block_rows, vector_count), jnp.float32)
        zero_sum = jnp.zeros((block_rows,), jnp.float32)
        return (
            jnp.zeros((block_rows, block_rows), jnp.bfloat16),
            zero_part,
            zero_sum,
            zero_part,
            zero_sum,
        )

    return lax.cond(owned, compute_pair, skip_pair)


def later_pass(owned, affinity, left_weights, right_weights):
    block_rows = affinity.shape[0]
    vector_count = left_weights.shape[1]

    def compute_pair():
        return (row_product(affinity, right_weights), col_product(affinity, left_weights))

    def skip_pair():
        zero_part = jnp.zeros((block_rows, vector_count), jnp.float32)
        return (zero_part, zero_part)

    return lax.cond(owned, compute_pair, skip_pair)


def butterfly(axis, summed_rows, block):
    size = lax.axis_size(axis)
    if size & (size - 1):
        return jnp.concatenate(
            [
                lax.psum(block[:summed_rows], axis),
                lax.all_gather(block[summed_rows:], axis, tiled=True),
            ]
        )
    index = lax.axis_index(axis)
    step = 1
    while step < size:
        route = [(i, i ^ step) for i in range(size)]
        other = lax.ppermute(block, axis, route)
        summed = block[:summed_rows] + other[:summed_rows]
        mine = block[summed_rows:]
        theirs = other[summed_rows:]
        upper = (index // step) % 2 == 1
        gathered = jnp.where(
            upper, jnp.concatenate([theirs, mine]), jnp.concatenate([mine, theirs])
        )
        block = jnp.concatenate([summed, gathered])
        step *= 2
    return block


def as_rows(vector, lanes=128):
    pad = (-vector.shape[0]) % lanes
    return jnp.pad(vector, (0, pad)).reshape(-1, lanes)


def hdot(left, right):
    return jnp.dot(left, right, precision=lax.Precision.HIGHEST, preferred_element_type=jnp.float32)


def factor_kernel(gram_ref, inverse_ref):
    size = gram_ref.shape[0]
    rows = lax.broadcasted_iota(jnp.int32, (size, size), 0)
    cols = lax.broadcasted_iota(jnp.int32, (size, size), 1)
    eye = jnp.where(rows == cols, 1.0, 0.0).astype(jnp.float32)

    def step(j, carry):
        remaining, inverse = carry
        column = jnp.sum(jnp.where(cols == j, remaining, 0.0), axis=1, keepdims=True)
        pivot = jnp.sum(jnp.where(rows[:, :1] == j, column, 0.0), axis=0, keepdims=True)
        scale = lax.rsqrt(pivot)
        factor_column = jnp.where(rows[:, :1] >= j, column * scale, 0.0)
        factor_row = jnp.sum(jnp.where(rows == j, remaining, 0.0), axis=0, keepdims=True)
        factor_row = jnp.where(cols[:1] >= j, factor_row * scale, 0.0)
        remaining = remaining - factor_column * factor_row
        inverse_row = jnp.sum(jnp.where(rows == j, inverse, 0.0), axis=0, keepdims=True) * scale
        inverse = jnp.where(rows == j, inverse_row, inverse)
        below = jnp.where(rows[:, :1] > j, factor_column, 0.0)
        inverse = inverse - below * inverse_row
        return remaining, inverse

    _, inverse = lax.fori_loop(0, size, step, (gram_ref[...], eye))
    inverse_ref[...] = inverse


def factor_inverse(gram_matrix):
    return pl.pallas_call(
        factor_kernel, out_shape=jax.ShapeDtypeStruct(gram_matrix.shape, jnp.float32)
    )(gram_matrix)


def orthonormal(product, vertex_valence, total_rows, fetch_offsets=()):
    block_rows, vector_count = product.shape
    walk = product / vertex_valence[:, None]
    partner_walks = [shifted(walk, "wide", -offset) for offset in fetch_offsets]
    centre = jnp.mean(walk, axis=0)
    centred = walk - centre
    local_gram = hdot(centred.T, centred)
    local_drift = jnp.sum(centred, axis=0)
    summed = jnp.concatenate(
        [
            as_rows(local_gram.reshape(-1)),
            as_rows(jnp.concatenate([jnp.sum(product, axis=0), jnp.sum(vertex_valence)[None]])),
        ]
    )
    summed_rows = summed.shape[0]
    block = jnp.concatenate([summed, as_rows(jnp.concatenate([centre, local_drift]))])
    gather_width = block.shape[0] - summed_rows
    for axis in ("narrow", "wide"):
        block = butterfly(axis, summed_rows, block)
    totals = block[:summed_rows].reshape(-1)
    gram_sum = totals[: vector_count * vector_count].reshape(vector_count, vector_count)
    column_sums = totals[vector_count * vector_count : vector_count * vector_count + vector_count]
    total_degree_sum = totals[vector_count * vector_count + vector_count]
    gathered = block[summed_rows:].reshape(-1, gather_width * 128)
    mean_walk = column_sums / total_degree_sum
    centres = gathered[:, :vector_count] - mean_walk
    drifts = gathered[:, vector_count:]
    cross = hdot(centres.T, drifts)
    gram_matrix = (gram_sum + cross + cross.T + block_rows * hdot(centres.T, centres)) / total_rows
    displaced_entries = jnp.concatenate([walk] + partner_walks) - mean_walk
    inverse_factor = factor_inverse(gram_matrix)
    bases = hdot(displaced_entries, inverse_factor.T)
    return [bases[i * block_rows : (i + 1) * block_rows] for i in range(1 + len(partner_walks))]


def on_device(embeddings, start, neighbours):
    wide_count = lax.axis_size("wide")
    lane_count = lax.axis_size("narrow")
    broad_index = lax.axis_index("wide")
    lane_index = lax.axis_index("narrow")
    far_reach = wide_count // 2 - 1
    fetch_offsets, pair_plan = difference_plan(wide_count, far_reach)
    unit_block = normalize_rows(embeddings)
    block_rows = unit_block.shape[0]
    total_rows = block_rows * wide_count * lane_count

    def block_at(offset):
        return (broad_index + offset) % wide_count * lane_count + lane_index

    owned_list = []
    for left, right in pair_plan:
        own_row = lax.dynamic_slice_in_dim(neighbours, block_at(left), 1, 0)[0]
        owned_list.append(jnp.any(own_row == block_at(right)))

    vector_count = start.shape[1]
    units = {0: unit_block}
    weights = {0: start}
    for offset in fetch_offsets:
        if offset == fetch_offsets[-1]:
            units[offset] = normalize_rows(shifted(embeddings, "wide", -offset))
        else:
            units[offset] = shifted(unit_block, "wide", -offset)
        weights[offset] = shifted(start, "wide", -offset)

    self_mask = lax.broadcasted_iota(
        jnp.int32, (block_rows, block_rows), 0
    ) == lax.broadcasted_iota(jnp.int32, (block_rows, block_rows), 1)
    near_tile = jnp.where(
        self_mask, jnp.zeros((), jnp.bfloat16), scores_tile(unit_block, unit_block)
    )

    zero_part = jnp.zeros((block_rows, vector_count), jnp.float32)
    zero_sum = jnp.zeros((block_rows,), jnp.float32)
    parts = {offset: zero_part for offset in units}
    sums = {offset: zero_sum for offset in units}
    tiles = []
    for (left, right), owned in zip(pair_plan, owned_list):
        affinity, row_part, row_sum, col_part, col_sum = first_pass(
            owned, units[left], units[right], weights[left], weights[right]
        )
        tiles.append(affinity)
        parts[left] = parts[left] + row_part
        sums[left] = sums[left] + row_sum
        parts[right] = parts[right] + col_part
        sums[right] = sums[right] + col_sum

    product = row_product(near_tile, start) + parts[0]
    vertex_valence = jnp.sum(near_tile, axis=1, dtype=jnp.float32) + sums[0]
    part_size = block_rows * vector_count
    for offset in fetch_offsets:
        sent = jnp.concatenate([as_rows(parts[offset].reshape(-1)), as_rows(sums[offset])])
        returned = shifted(sent, "wide", offset).reshape(-1)
        product = product + returned[:part_size].reshape(block_rows, vector_count)
        vertex_valence = vertex_valence + returned[part_size : part_size + block_rows]
    bases = orthonormal(product, vertex_valence, total_rows, fetch_offsets if ITERS > 1 else ())

    for iteration in range(1, ITERS):
        weights = {0: bases[0].astype(jnp.bfloat16)}
        for position, offset in enumerate(fetch_offsets):
            weights[offset] = bases[position + 1].astype(jnp.bfloat16)
        current = weights[0]
        parts = {offset: zero_part for offset in units}
        for (left, right), owned, affinity in zip(pair_plan, owned_list, tiles):
            row_part, col_part = later_pass(owned, affinity, weights[left], weights[right])
            parts[left] = parts[left] + row_part
            parts[right] = parts[right] + col_part
        product = row_product(near_tile, current) + parts[0]
        for offset in fetch_offsets:
            product = product + shifted(parts[offset], "wide", offset)
        last = iteration == ITERS - 1
        bases = orthonormal(product, vertex_valence, total_rows, () if last else fetch_offsets)
    return (bases[0], vertex_valence / block_rows)


def solution(mesh):
    in_specs = (P(("wide", "narrow"), None), P(("wide", "narrow"), None), P())
    out_specs = (P(("wide", "narrow"), None), P(("wide", "narrow")))
    return jax.shard_map(
        on_device, mesh=mesh, in_specs=in_specs, out_specs=out_specs, check_vma=False
    )
```

```python
from functools import partial
import itertools
import math

import jax
import jax.numpy as jnp
from jax import lax
from jax.sharding import PartitionSpec as P
from jax.experimental import pallas as pl

ITERS = 2


kernel_width_factor = 0.05


def shifted(block, axis, distance):
    devices = range(lax.axis_size(axis))
    route = [((i - distance) % len(devices), i) for i in devices]
    return lax.ppermute(block, axis, route)


def ring_gap(offset, span):
    offset %= span
    return min(offset, span - offset)


def difference_plan(span, far_reach):
    candidates = sorted(range(1, span), key=lambda s: (ring_gap(s, span), s))
    for count in range(1, span):
        best = None
        for chosen in itertools.combinations(candidates, count):
            points = (0,) + chosen
            plan = {}
            for a, b in itertools.permutations(points, 2):
                gap = (b - a) % span
                if 1 <= gap <= far_reach and gap not in plan:
                    plan[gap] = (a, b)
            if len(plan) == far_reach:
                cost = sum(ring_gap(s, span) for s in chosen)
                if best is None or cost < best[0]:
                    best = (cost, chosen, plan)
        if best is not None:
            return list(best[1]), [best[2][gap] for gap in range(1, far_reach + 1)]
    raise ValueError("no plan")


def normalize_rows(values):
    values_wide = values.astype(jnp.float32)
    scaling = lax.rsqrt(jnp.mean(values_wide * values_wide, axis=-1, keepdims=True) + 1e-06)
    return (values_wide * scaling / math.sqrt(values_wide.shape[-1])).astype(jnp.bfloat16)


def scores_tile(leftside_block, right_block):
    kernel_entries = lax.dot_general(
        leftside_block, right_block, (((1,), (1,)), ((), ())), preferred_element_type=jnp.float32
    )
    return jnp.exp(kernel_entries / kernel_width_factor).astype(jnp.bfloat16)


def row_product(affinity, weights):
    return jnp.dot(affinity, weights, preferred_element_type=jnp.float32)


def col_product(affinity, weights):
    return lax.dot_general(
        affinity, weights, (((0,), (0,)), ((), ())), preferred_element_type=jnp.float32
    )


def first_pass(owned, left_unit, right_unit, left_weights, right_weights):
    block_rows = left_unit.shape[0]
    vector_count = left_weights.shape[1]

    def compute_pair():
        affinity = scores_tile(left_unit, right_unit)
        return (
            affinity,
            row_product(affinity, right_weights),
            jnp.sum(affinity, axis=1, dtype=jnp.float32),
            col_product(affinity, left_weights),
            jnp.sum(affinity, axis=0, dtype=jnp.float32),
        )

    def skip_pair():
        zero_part = jnp.zeros((block_rows, vector_count), jnp.float32)
        zero_sum = jnp.zeros((block_rows,), jnp.float32)
        return (
            jnp.zeros((block_rows, block_rows), jnp.bfloat16),
            zero_part,
            zero_sum,
            zero_part,
            zero_sum,
        )

    return lax.cond(owned, compute_pair, skip_pair)


def later_pass(owned, affinity, left_weights, right_weights):
    block_rows = affinity.shape[0]
    vector_count = left_weights.shape[1]

    def compute_pair():
        return (row_product(affinity, right_weights), col_product(affinity, left_weights))

    def skip_pair():
        zero_part = jnp.zeros((block_rows, vector_count), jnp.float32)
        return (zero_part, zero_part)

    return lax.cond(owned, compute_pair, skip_pair)


def butterfly(axis, summed_rows, block):
    size = lax.axis_size(axis)
    if size & (size - 1):
        return jnp.concatenate(
            [
                lax.psum(block[:summed_rows], axis),
                lax.all_gather(block[summed_rows:], axis, tiled=True),
            ]
        )
    index = lax.axis_index(axis)
    step = 1
    while step < size:
        route = [(i, i ^ step) for i in range(size)]
        other = lax.ppermute(block, axis, route)
        summed = block[:summed_rows] + other[:summed_rows]
        mine = block[summed_rows:]
        theirs = other[summed_rows:]
        upper = (index // step) % 2 == 1
        gathered = jnp.where(
            upper, jnp.concatenate([theirs, mine]), jnp.concatenate([mine, theirs])
        )
        block = jnp.concatenate([summed, gathered])
        step *= 2
    return block


def as_rows(vector, lanes=128):
    pad = (-vector.shape[0]) % lanes
    return jnp.pad(vector, (0, pad)).reshape(-1, lanes)


def hdot(left, right):
    return jnp.dot(left, right, precision=lax.Precision.HIGHEST, preferred_element_type=jnp.float32)


def factor_kernel(gram_ref, inverse_ref):
    size = gram_ref.shape[0]
    rows = lax.broadcasted_iota(jnp.int32, (size, size), 0)
    cols = lax.broadcasted_iota(jnp.int32, (size, size), 1)
    eye = jnp.where(rows == cols, 1.0, 0.0).astype(jnp.float32)

    def step(j, carry):
        remaining, inverse = carry
        column = jnp.sum(jnp.where(cols == j, remaining, 0.0), axis=1, keepdims=True)
        pivot = jnp.sum(jnp.where(rows[:, :1] == j, column, 0.0), axis=0, keepdims=True)
        scale = lax.rsqrt(pivot)
        factor_column = jnp.where(rows[:, :1] >= j, column * scale, 0.0)
        factor_row = jnp.sum(jnp.where(rows == j, remaining, 0.0), axis=0, keepdims=True)
        factor_row = jnp.where(cols[:1] >= j, factor_row * scale, 0.0)
        remaining = remaining - factor_column * factor_row
        inverse_row = jnp.sum(jnp.where(rows == j, inverse, 0.0), axis=0, keepdims=True) * scale
        inverse = jnp.where(rows == j, inverse_row, inverse)
        below = jnp.where(rows[:, :1] > j, factor_column, 0.0)
        inverse = inverse - below * inverse_row
        return remaining, inverse

    _, inverse = lax.fori_loop(0, size, step, (gram_ref[...], eye))
    inverse_ref[...] = inverse


def factor_inverse(gram_matrix):
    return pl.pallas_call(
        factor_kernel, out_shape=jax.ShapeDtypeStruct(gram_matrix.shape, jnp.float32)
    )(gram_matrix)


def orthonormal(product, vertex_valence, total_rows, fetch_offsets=()):
    block_rows, vector_count = product.shape
    walk = product / vertex_valence[:, None]
    partner_walks = [shifted(walk, "wide", -offset) for offset in fetch_offsets]
    centre = jnp.mean(walk, axis=0)
    centred = walk - centre
    local_gram = hdot(centred.T, centred)
    local_drift = jnp.sum(centred, axis=0)
    summed = jnp.concatenate(
        [
            as_rows(local_gram.reshape(-1)),
            as_rows(jnp.concatenate([jnp.sum(product, axis=0), jnp.sum(vertex_valence)[None]])),
        ]
    )
    summed_rows = summed.shape[0]
    block = jnp.concatenate([summed, as_rows(jnp.concatenate([centre, local_drift]))])
    gather_width = block.shape[0] - summed_rows
    for axis in ("narrow", "wide"):
        block = butterfly(axis, summed_rows, block)
    totals = block[:summed_rows].reshape(-1)
    gram_sum = totals[: vector_count * vector_count].reshape(vector_count, vector_count)
    column_sums = totals[vector_count * vector_count : vector_count * vector_count + vector_count]
    total_degree_sum = totals[vector_count * vector_count + vector_count]
    gathered = block[summed_rows:].reshape(-1, gather_width * 128)
    mean_walk = column_sums / total_degree_sum
    centres = gathered[:, :vector_count] - mean_walk
    drifts = gathered[:, vector_count:]
    cross = hdot(centres.T, drifts)
    gram_matrix = (gram_sum + cross + cross.T + block_rows * hdot(centres.T, centres)) / total_rows
    displaced_entries = jnp.concatenate([walk] + partner_walks) - mean_walk
    inverse_factor = factor_inverse(gram_matrix)
    bases = hdot(displaced_entries, inverse_factor.T)
    return [bases[i * block_rows : (i + 1) * block_rows] for i in range(1 + len(partner_walks))]


def on_device(embeddings, start, neighbours):
    wide_count = lax.axis_size("wide")
    lane_count = lax.axis_size("narrow")
    broad_index = lax.axis_index("wide")
    lane_index = lax.axis_index("narrow")
    far_reach = wide_count // 2 - 1
    fetch_offsets, pair_plan = difference_plan(wide_count, far_reach)
    unit_block = normalize_rows(embeddings)
    block_rows = unit_block.shape[0]
    total_rows = block_rows * wide_count * lane_count

    def block_at(offset):
        return (broad_index + offset) % wide_count * lane_count + lane_index

    owned_list = []
    for left, right in pair_plan:
        own_row = lax.dynamic_slice_in_dim(neighbours, block_at(left), 1, 0)[0]
        owned_list.append(jnp.any(own_row == block_at(right)))

    vector_count = start.shape[1]
    units = {0: unit_block}
    weights = {0: start}
    unit_width = unit_block.shape[1]
    weight_rows = as_rows(start.reshape(-1), unit_width)
    for offset in fetch_offsets:
        raw = offset == fetch_offsets[-1]
        rows = embeddings if raw else unit_block
        arrived = shifted(jnp.concatenate([rows, weight_rows]), "wide", -offset)
        units[offset] = normalize_rows(arrived[:block_rows]) if raw else arrived[:block_rows]
        weights[offset] = (
            arrived[block_rows:].reshape(-1)[: block_rows * vector_count].reshape(block_rows, vector_count)
        )

    self_mask = lax.broadcasted_iota(
        jnp.int32, (block_rows, block_rows), 0
    ) == lax.broadcasted_iota(jnp.int32, (block_rows, block_rows), 1)
    near_tile = jnp.where(
        self_mask, jnp.zeros((), jnp.bfloat16), scores_tile(unit_block, unit_block)
    )

    zero_part = jnp.zeros((block_rows, vector_count), jnp.float32)
    zero_sum = jnp.zeros((block_rows,), jnp.float32)
    parts = {offset: zero_part for offset in units}
    sums = {offset: zero_sum for offset in units}
    tiles = []
    for (left, right), owned in zip(pair_plan, owned_list):
        affinity, row_part, row_sum, col_part, col_sum = first_pass(
            owned, units[left], units[right], weights[left], weights[right]
        )
        tiles.append(affinity)
        parts[left] = parts[left] + row_part
        sums[left] = sums[left] + row_sum
        parts[right] = parts[right] + col_part
        sums[right] = sums[right] + col_sum

    product = row_product(near_tile, start) + parts[0]
    vertex_valence = jnp.sum(near_tile, axis=1, dtype=jnp.float32) + sums[0]
    part_size = block_rows * vector_count
    for offset in fetch_offsets:
        sent = jnp.concatenate([as_rows(parts[offset].reshape(-1)), as_rows(sums[offset])])
        returned = shifted(sent, "wide", offset).reshape(-1)
        product = product + returned[:part_size].reshape(block_rows, vector_count)
        vertex_valence = vertex_valence + returned[part_size : part_size + block_rows]
    bases = orthonormal(product, vertex_valence, total_rows, fetch_offsets if ITERS > 1 else ())

    for iteration in range(1, ITERS):
        weights = {0: bases[0].astype(jnp.bfloat16)}
        for position, offset in enumerate(fetch_offsets):
            weights[offset] = bases[position + 1].astype(jnp.bfloat16)
        current = weights[0]
        parts = {offset: zero_part for offset in units}
        for (left, right), owned, affinity in zip(pair_plan, owned_list, tiles):
            row_part, col_part = later_pass(owned, affinity, weights[left], weights[right])
            parts[left] = parts[left] + row_part
            parts[right] = parts[right] + col_part
        product = row_product(near_tile, current) + parts[0]
        for offset in fetch_offsets:
            product = product + shifted(parts[offset], "wide", offset)
        last = iteration == ITERS - 1
        bases = orthonormal(product, vertex_valence, total_rows, () if last else fetch_offsets)
    return (bases[0], vertex_valence / block_rows)


def solution(mesh):
    in_specs = (P(("wide", "narrow"), None), P(("wide", "narrow"), None), P())
    out_specs = (P(("wide", "narrow"), None), P(("wide", "narrow")))
    return jax.shard_map(
        on_device, mesh=mesh, in_specs=in_specs, out_specs=out_specs, check_vma=False
    )
```

```python
from functools import partial
import itertools
import math

import jax
import jax.numpy as jnp
from jax import lax
from jax.sharding import PartitionSpec as P
from jax.experimental import pallas as pl

ITERS = 2


kernel_width_factor = 0.05


def shifted(block, axis, distance):
    devices = range(lax.axis_size(axis))
    route = [((i - distance) % len(devices), i) for i in devices]
    return lax.ppermute(block, axis, route)


def ring_gap(offset, span):
    offset %= span
    return min(offset, span - offset)


def difference_plan(span, far_reach):
    candidates = sorted(range(1, span), key=lambda s: (ring_gap(s, span), s))
    for count in range(1, span):
        best = None
        for chosen in itertools.combinations(candidates, count):
            points = (0,) + chosen
            plan = {}
            for a, b in itertools.permutations(points, 2):
                gap = (b - a) % span
                if 1 <= gap <= far_reach and gap not in plan:
                    plan[gap] = (a, b)
            if len(plan) == far_reach:
                cost = sum(ring_gap(s, span) for s in chosen)
                if best is None or cost < best[0]:
                    best = (cost, chosen, plan)
        if best is not None:
            return list(best[1]), [best[2][gap] for gap in range(1, far_reach + 1)]
    raise ValueError("no plan")


def normalize_rows(values):
    values_wide = values.astype(jnp.float32)
    scaling = lax.rsqrt(jnp.mean(values_wide * values_wide, axis=-1, keepdims=True) + 1e-06)
    return (values_wide * scaling / math.sqrt(values_wide.shape[-1])).astype(jnp.bfloat16)


def scores_tile(leftside_block, right_block):
    kernel_entries = lax.dot_general(
        leftside_block, right_block, (((1,), (1,)), ((), ())), preferred_element_type=jnp.float32
    )
    return jnp.exp(kernel_entries / kernel_width_factor).astype(jnp.bfloat16)


def row_product(affinity, weights):
    return jnp.dot(affinity, weights, preferred_element_type=jnp.float32)


def col_product(affinity, weights):
    return lax.dot_general(
        affinity, weights, (((0,), (0,)), ((), ())), preferred_element_type=jnp.float32
    )


def first_pass(owned, left_unit, right_unit, left_weights, right_weights):
    block_rows = left_unit.shape[0]
    vector_count = left_weights.shape[1]

    def compute_pair():
        affinity = scores_tile(left_unit, right_unit)
        return (
            affinity,
            row_product(affinity, right_weights),
            jnp.sum(affinity, axis=1, dtype=jnp.float32),
            col_product(affinity, left_weights),
            jnp.sum(affinity, axis=0, dtype=jnp.float32),
        )

    def skip_pair():
        zero_part = jnp.zeros((block_rows, vector_count), jnp.float32)
        zero_sum = jnp.zeros((block_rows,), jnp.float32)
        return (
            jnp.zeros((block_rows, block_rows), jnp.bfloat16),
            zero_part,
            zero_sum,
            zero_part,
            zero_sum,
        )

    return lax.cond(owned, compute_pair, skip_pair)


def early_pass(owned, left_unit, right_unit, near_weights, near_is_right):
    block_rows = left_unit.shape[0]
    vector_count = near_weights.shape[1]

    def compute_pair():
        affinity = scores_tile(left_unit, right_unit)
        if near_is_right:
            part = row_product(affinity, near_weights)
        else:
            part = col_product(affinity, near_weights)
        return (
            affinity,
            part,
            jnp.sum(affinity, axis=1, dtype=jnp.float32),
            jnp.sum(affinity, axis=0, dtype=jnp.float32),
        )

    def skip_pair():
        zero_sum = jnp.zeros((block_rows,), jnp.float32)
        return (
            jnp.zeros((block_rows, block_rows), jnp.bfloat16),
            jnp.zeros((block_rows, vector_count), jnp.float32),
            zero_sum,
            zero_sum,
        )

    return lax.cond(owned, compute_pair, skip_pair)


def deferred_pass(owned, affinity, far_weights, far_is_right):
    block_rows = affinity.shape[0]
    vector_count = far_weights.shape[1]

    def compute_pair():
        if far_is_right:
            return row_product(affinity, far_weights)
        return col_product(affinity, far_weights)

    return lax.cond(
        owned, compute_pair, lambda: jnp.zeros((block_rows, vector_count), jnp.float32)
    )


def later_pass(owned, affinity, left_weights, right_weights):
    block_rows = affinity.shape[0]
    vector_count = left_weights.shape[1]

    def compute_pair():
        return (row_product(affinity, right_weights), col_product(affinity, left_weights))

    def skip_pair():
        zero_part = jnp.zeros((block_rows, vector_count), jnp.float32)
        return (zero_part, zero_part)

    return lax.cond(owned, compute_pair, skip_pair)


def butterfly(axis, summed_rows, block):
    size = lax.axis_size(axis)
    if size & (size - 1):
        return jnp.concatenate(
            [
                lax.psum(block[:summed_rows], axis),
                lax.all_gather(block[summed_rows:], axis, tiled=True),
            ]
        )
    index = lax.axis_index(axis)
    step = 1
    while step < size:
        route = [(i, i ^ step) for i in range(size)]
        other = lax.ppermute(block, axis, route)
        summed = block[:summed_rows] + other[:summed_rows]
        mine = block[summed_rows:]
        theirs = other[summed_rows:]
        upper = (index // step) % 2 == 1
        gathered = jnp.where(
            upper, jnp.concatenate([theirs, mine]), jnp.concatenate([mine, theirs])
        )
        block = jnp.concatenate([summed, gathered])
        step *= 2
    return block


def as_rows(vector, lanes=128):
    pad = (-vector.shape[0]) % lanes
    return jnp.pad(vector, (0, pad)).reshape(-1, lanes)


def hdot(left, right):
    return jnp.dot(left, right, precision=lax.Precision.HIGHEST, preferred_element_type=jnp.float32)


def factor_kernel(gram_ref, inverse_ref):
    size = gram_ref.shape[0]
    rows = lax.broadcasted_iota(jnp.int32, (size, size), 0)
    cols = lax.broadcasted_iota(jnp.int32, (size, size), 1)
    eye = jnp.where(rows == cols, 1.0, 0.0).astype(jnp.float32)

    def step(j, carry):
        remaining, inverse = carry
        column = jnp.sum(jnp.where(cols == j, remaining, 0.0), axis=1, keepdims=True)
        pivot = jnp.sum(jnp.where(rows[:, :1] == j, column, 0.0), axis=0, keepdims=True)
        scale = lax.rsqrt(pivot)
        factor_column = jnp.where(rows[:, :1] >= j, column * scale, 0.0)
        factor_row = jnp.sum(jnp.where(rows == j, remaining, 0.0), axis=0, keepdims=True)
        factor_row = jnp.where(cols[:1] >= j, factor_row * scale, 0.0)
        remaining = remaining - factor_column * factor_row
        inverse_row = jnp.sum(jnp.where(rows == j, inverse, 0.0), axis=0, keepdims=True) * scale
        inverse = jnp.where(rows == j, inverse_row, inverse)
        below = jnp.where(rows[:, :1] > j, factor_column, 0.0)
        inverse = inverse - below * inverse_row
        return remaining, inverse

    _, inverse = lax.fori_loop(0, size, step, (gram_ref[...], eye))
    inverse_ref[...] = inverse


def factor_inverse(gram_matrix):
    return pl.pallas_call(
        factor_kernel, out_shape=jax.ShapeDtypeStruct(gram_matrix.shape, jnp.float32)
    )(gram_matrix)


def orthonormal(product, vertex_valence, total_rows, fetch_offsets=()):
    block_rows, vector_count = product.shape
    walk = product / vertex_valence[:, None]
    partner_walks = [shifted(walk, "wide", -offset) for offset in fetch_offsets]
    centre = jnp.mean(walk, axis=0)
    centred = walk - centre
    local_gram = hdot(centred.T, centred)
    local_drift = jnp.sum(centred, axis=0)
    summed = jnp.concatenate(
        [
            as_rows(local_gram.reshape(-1)),
            as_rows(jnp.concatenate([jnp.sum(product, axis=0), jnp.sum(vertex_valence)[None]])),
        ]
    )
    summed_rows = summed.shape[0]
    block = jnp.concatenate([summed, as_rows(jnp.concatenate([centre, local_drift]))])
    gather_width = block.shape[0] - summed_rows
    for axis in ("narrow", "wide"):
        block = butterfly(axis, summed_rows, block)
    totals = block[:summed_rows].reshape(-1)
    gram_sum = totals[: vector_count * vector_count].reshape(vector_count, vector_count)
    column_sums = totals[vector_count * vector_count : vector_count * vector_count + vector_count]
    total_degree_sum = totals[vector_count * vector_count + vector_count]
    gathered = block[summed_rows:].reshape(-1, gather_width * 128)
    mean_walk = column_sums / total_degree_sum
    centres = gathered[:, :vector_count] - mean_walk
    drifts = gathered[:, vector_count:]
    cross = hdot(centres.T, drifts)
    gram_matrix = (gram_sum + cross + cross.T + block_rows * hdot(centres.T, centres)) / total_rows
    displaced_entries = jnp.concatenate([walk] + partner_walks) - mean_walk
    inverse_factor = factor_inverse(gram_matrix)
    bases = hdot(displaced_entries, inverse_factor.T)
    return [bases[i * block_rows : (i + 1) * block_rows] for i in range(1 + len(partner_walks))]


def on_device(embeddings, start, neighbours):
    wide_count = lax.axis_size("wide")
    lane_count = lax.axis_size("narrow")
    broad_index = lax.axis_index("wide")
    lane_index = lax.axis_index("narrow")
    far_reach = wide_count // 2 - 1
    fetch_offsets, pair_plan = difference_plan(wide_count, far_reach)
    unit_block = normalize_rows(embeddings)
    block_rows = unit_block.shape[0]
    total_rows = block_rows * wide_count * lane_count

    def block_at(offset):
        return (broad_index + offset) % wide_count * lane_count + lane_index

    owned_list = []
    for left, right in pair_plan:
        own_row = lax.dynamic_slice_in_dim(neighbours, block_at(left), 1, 0)[0]
        owned_list.append(jnp.any(own_row == block_at(right)))

    vector_count = start.shape[1]
    units = {0: unit_block}
    weights = {0: start}
    for offset in fetch_offsets:
        if offset == fetch_offsets[-1]:
            units[offset] = normalize_rows(shifted(embeddings, "wide", -offset))
        else:
            units[offset] = shifted(unit_block, "wide", -offset)
        weights[offset] = shifted(start, "wide", -offset)

    self_mask = lax.broadcasted_iota(
        jnp.int32, (block_rows, block_rows), 0
    ) == lax.broadcasted_iota(jnp.int32, (block_rows, block_rows), 1)
    near_tile = jnp.where(
        self_mask, jnp.zeros((), jnp.bfloat16), scores_tile(unit_block, unit_block)
    )

    zero_part = jnp.zeros((block_rows, vector_count), jnp.float32)
    zero_sum = jnp.zeros((block_rows,), jnp.float32)
    parts = {offset: zero_part for offset in units}
    sums = {offset: zero_sum for offset in units}
    early = fetch_offsets[-1]
    early_ids = [i for i, pair in enumerate(pair_plan) if set(pair) <= {0, early}]
    tiles = [None] * len(pair_plan)
    early_results = []
    for i in early_ids:
        left, right = pair_plan[i]
        near_is_right = right == 0
        near_weights = weights[0]
        early_results.append(
            early_pass(owned_list[i], units[left], units[right], near_weights, near_is_right)
        )
    if early_ids:
        late_offsets = [offset for offset in fetch_offsets if offset != early]
        late_units, late_weights, early_results = lax.optimization_barrier(
            ([units[o] for o in late_offsets], [weights[o] for o in late_offsets], early_results)
        )
        for position, offset in enumerate(late_offsets):
            units[offset] = late_units[position]
            weights[offset] = late_weights[position]
    for i, (affinity, part, row_sum, col_sum) in zip(early_ids, early_results):
        left, right = pair_plan[i]
        near_is_right = right == 0
        tiles[i] = affinity
        far = left if near_is_right else right
        far_part = deferred_pass(owned_list[i], affinity, weights[far], not near_is_right)
        if near_is_right:
            row_part, col_part = part, far_part
        else:
            row_part, col_part = far_part, part
        parts[left] = parts[left] + row_part
        sums[left] = sums[left] + row_sum
        parts[right] = parts[right] + col_part
        sums[right] = sums[right] + col_sum
    for i, ((left, right), owned) in enumerate(zip(pair_plan, owned_list)):
        if i in early_ids:
            continue
        affinity, row_part, row_sum, col_part, col_sum = first_pass(
            owned, units[left], units[right], weights[left], weights[right]
        )
        tiles[i] = affinity
        parts[left] = parts[left] + row_part
        sums[left] = sums[left] + row_sum
        parts[right] = parts[right] + col_part
        sums[right] = sums[right] + col_sum

    product = row_product(near_tile, start) + parts[0]
    vertex_valence = jnp.sum(near_tile, axis=1, dtype=jnp.float32) + sums[0]
    part_size = block_rows * vector_count
    for offset in fetch_offsets:
        sent = jnp.concatenate([as_rows(parts[offset].reshape(-1)), as_rows(sums[offset])])
        returned = shifted(sent, "wide", offset).reshape(-1)
        product = product + returned[:part_size].reshape(block_rows, vector_count)
        vertex_valence = vertex_valence + returned[part_size : part_size + block_rows]
    bases = orthonormal(product, vertex_valence, total_rows, fetch_offsets if ITERS > 1 else ())

    for iteration in range(1, ITERS):
        weights = {0: bases[0].astype(jnp.bfloat16)}
        for position, offset in enumerate(fetch_offsets):
            weights[offset] = bases[position + 1].astype(jnp.bfloat16)
        current = weights[0]
        parts = {offset: zero_part for offset in units}
        for (left, right), owned, affinity in zip(pair_plan, owned_list, tiles):
            row_part, col_part = later_pass(owned, affinity, weights[left], weights[right])
            parts[left] = parts[left] + row_part
            parts[right] = parts[right] + col_part
        product = row_product(near_tile, current) + parts[0]
        for offset in fetch_offsets:
            product = product + shifted(parts[offset], "wide", offset)
        last = iteration == ITERS - 1
        bases = orthonormal(product, vertex_valence, total_rows, () if last else fetch_offsets)
    return (bases[0], vertex_valence / block_rows)


def solution(mesh):
    in_specs = (P(("wide", "narrow"), None), P(("wide", "narrow"), None), P())
    out_specs = (P(("wide", "narrow"), None), P(("wide", "narrow")))
    return jax.shard_map(
        on_device, mesh=mesh, in_specs=in_specs, out_specs=out_specs, check_vma=False
    )
```

```python
from functools import partial
import itertools
import math

import jax
import jax.numpy as jnp
from jax import lax
from jax.sharding import PartitionSpec as P
from jax.experimental import pallas as pl

ITERS = 2


kernel_width_factor = 0.05


def shifted(block, axis, distance):
    devices = range(lax.axis_size(axis))
    route = [((i - distance) % len(devices), i) for i in devices]
    return lax.ppermute(block, axis, route)


def ring_gap(offset, span):
    offset %= span
    return min(offset, span - offset)


def difference_plan(span, far_reach):
    candidates = sorted(range(1, span), key=lambda s: (ring_gap(s, span), s))
    for count in range(1, span):
        best = None
        for chosen in itertools.combinations(candidates, count):
            points = (0,) + chosen
            plan = {}
            for a, b in itertools.permutations(points, 2):
                gap = (b - a) % span
                if 1 <= gap <= far_reach and gap not in plan:
                    plan[gap] = (a, b)
            if len(plan) == far_reach:
                cost = sum(ring_gap(s, span) for s in chosen)
                if best is None or cost < best[0]:
                    best = (cost, chosen, plan)
        if best is not None:
            return list(best[1]), [best[2][gap] for gap in range(1, far_reach + 1)]
    raise ValueError("no plan")


def normalize_rows(values):
    values_wide = values.astype(jnp.float32)
    scaling = lax.rsqrt(jnp.mean(values_wide * values_wide, axis=-1, keepdims=True) + 1e-06)
    return (values_wide * scaling / math.sqrt(values_wide.shape[-1])).astype(jnp.bfloat16)


def scores_tile(leftside_block, right_block):
    kernel_entries = lax.dot_general(
        leftside_block, right_block, (((1,), (1,)), ((), ())), preferred_element_type=jnp.float32
    )
    return jnp.exp(kernel_entries / kernel_width_factor).astype(jnp.bfloat16)


def row_product(affinity, weights):
    return jnp.dot(affinity, weights, preferred_element_type=jnp.float32)


def col_product(affinity, weights):
    return lax.dot_general(
        affinity, weights, (((0,), (0,)), ((), ())), preferred_element_type=jnp.float32
    )


def first_pass(owned, left_unit, right_unit, left_weights, right_weights):
    block_rows = left_unit.shape[0]
    vector_count = left_weights.shape[1]

    def compute_pair():
        affinity = scores_tile(left_unit, right_unit)
        return (
            affinity,
            row_product(affinity, right_weights),
            jnp.sum(affinity, axis=1, dtype=jnp.float32),
            col_product(affinity, left_weights),
            jnp.sum(affinity, axis=0, dtype=jnp.float32),
        )

    def skip_pair():
        zero_part = jnp.zeros((block_rows, vector_count), jnp.float32)
        zero_sum = jnp.zeros((block_rows,), jnp.float32)
        return (
            jnp.zeros((block_rows, block_rows), jnp.bfloat16),
            zero_part,
            zero_sum,
            zero_part,
            zero_sum,
        )

    return lax.cond(owned, compute_pair, skip_pair)


def early_pass(owned, left_unit, right_unit, near_weights, near_is_right):
    block_rows = left_unit.shape[0]
    vector_count = near_weights.shape[1]

    def compute_pair():
        affinity = scores_tile(left_unit, right_unit)
        if near_is_right:
            part = row_product(affinity, near_weights)
        else:
            part = col_product(affinity, near_weights)
        return (
            affinity,
            part,
            jnp.sum(affinity, axis=1, dtype=jnp.float32),
            jnp.sum(affinity, axis=0, dtype=jnp.float32),
        )

    def skip_pair():
        zero_sum = jnp.zeros((block_rows,), jnp.float32)
        return (
            jnp.zeros((block_rows, block_rows), jnp.bfloat16),
            jnp.zeros((block_rows, vector_count), jnp.float32),
            zero_sum,
            zero_sum,
        )

    return lax.cond(owned, compute_pair, skip_pair)


def deferred_pass(owned, affinity, far_weights, far_is_right):
    block_rows = affinity.shape[0]
    vector_count = far_weights.shape[1]

    def compute_pair():
        if far_is_right:
            return row_product(affinity, far_weights)
        return col_product(affinity, far_weights)

    return lax.cond(
        owned, compute_pair, lambda: jnp.zeros((block_rows, vector_count), jnp.float32)
    )


def column_chunk(owned, left_unit, right_chunk, left_weights, right_weights_chunk):
    block_rows = left_unit.shape[0]
    chunk_rows = right_chunk.shape[0]
    vector_count = left_weights.shape[1]

    def compute_pair():
        affinity = scores_tile(left_unit, right_chunk)
        return (
            affinity,
            row_product(affinity, right_weights_chunk),
            jnp.sum(affinity, axis=1, dtype=jnp.float32),
            col_product(affinity, left_weights),
            jnp.sum(affinity, axis=0, dtype=jnp.float32),
        )

    def skip_pair():
        return (
            jnp.zeros((block_rows, chunk_rows), jnp.bfloat16),
            jnp.zeros((block_rows, vector_count), jnp.float32),
            jnp.zeros((block_rows,), jnp.float32),
            jnp.zeros((chunk_rows, vector_count), jnp.float32),
            jnp.zeros((chunk_rows,), jnp.float32),
        )

    return lax.cond(owned, compute_pair, skip_pair)


def later_pass(owned, affinity, left_weights, right_weights):
    block_rows = affinity.shape[0]
    vector_count = left_weights.shape[1]

    def compute_pair():
        return (row_product(affinity, right_weights), col_product(affinity, left_weights))

    def skip_pair():
        zero_part = jnp.zeros((block_rows, vector_count), jnp.float32)
        return (zero_part, zero_part)

    return lax.cond(owned, compute_pair, skip_pair)


def butterfly(axis, summed_rows, block):
    size = lax.axis_size(axis)
    if size & (size - 1):
        return jnp.concatenate(
            [
                lax.psum(block[:summed_rows], axis),
                lax.all_gather(block[summed_rows:], axis, tiled=True),
            ]
        )
    index = lax.axis_index(axis)
    step = 1
    while step < size:
        route = [(i, i ^ step) for i in range(size)]
        other = lax.ppermute(block, axis, route)
        summed = block[:summed_rows] + other[:summed_rows]
        mine = block[summed_rows:]
        theirs = other[summed_rows:]
        upper = (index // step) % 2 == 1
        gathered = jnp.where(
            upper, jnp.concatenate([theirs, mine]), jnp.concatenate([mine, theirs])
        )
        block = jnp.concatenate([summed, gathered])
        step *= 2
    return block


def as_rows(vector, lanes=128):
    pad = (-vector.shape[0]) % lanes
    return jnp.pad(vector, (0, pad)).reshape(-1, lanes)


def hdot(left, right):
    return jnp.dot(left, right, precision=lax.Precision.HIGHEST, preferred_element_type=jnp.float32)


def factor_kernel(gram_ref, inverse_ref):
    size = gram_ref.shape[0]
    rows = lax.broadcasted_iota(jnp.int32, (size, size), 0)
    cols = lax.broadcasted_iota(jnp.int32, (size, size), 1)
    eye = jnp.where(rows == cols, 1.0, 0.0).astype(jnp.float32)

    def step(j, carry):
        remaining, inverse = carry
        column = jnp.sum(jnp.where(cols == j, remaining, 0.0), axis=1, keepdims=True)
        pivot = jnp.sum(jnp.where(rows[:, :1] == j, column, 0.0), axis=0, keepdims=True)
        scale = lax.rsqrt(pivot)
        factor_column = jnp.where(rows[:, :1] >= j, column * scale, 0.0)
        factor_row = jnp.sum(jnp.where(rows == j, remaining, 0.0), axis=0, keepdims=True)
        factor_row = jnp.where(cols[:1] >= j, factor_row * scale, 0.0)
        remaining = remaining - factor_column * factor_row
        inverse_row = jnp.sum(jnp.where(rows == j, inverse, 0.0), axis=0, keepdims=True) * scale
        inverse = jnp.where(rows == j, inverse_row, inverse)
        below = jnp.where(rows[:, :1] > j, factor_column, 0.0)
        inverse = inverse - below * inverse_row
        return remaining, inverse

    _, inverse = lax.fori_loop(0, size, step, (gram_ref[...], eye))
    inverse_ref[...] = inverse


def factor_inverse(gram_matrix):
    return pl.pallas_call(
        factor_kernel, out_shape=jax.ShapeDtypeStruct(gram_matrix.shape, jnp.float32)
    )(gram_matrix)


def orthonormal(product, vertex_valence, total_rows, fetch_offsets=()):
    block_rows, vector_count = product.shape
    walk = product / vertex_valence[:, None]
    partner_walks = [shifted(walk, "wide", -offset) for offset in fetch_offsets]
    centre = jnp.mean(walk, axis=0)
    centred = walk - centre
    local_gram = hdot(centred.T, centred)
    local_drift = jnp.sum(centred, axis=0)
    summed = jnp.concatenate(
        [
            as_rows(local_gram.reshape(-1)),
            as_rows(jnp.concatenate([jnp.sum(product, axis=0), jnp.sum(vertex_valence)[None]])),
        ]
    )
    summed_rows = summed.shape[0]
    block = jnp.concatenate([summed, as_rows(jnp.concatenate([centre, local_drift]))])
    gather_width = block.shape[0] - summed_rows
    for axis in ("narrow", "wide"):
        block = butterfly(axis, summed_rows, block)
    totals = block[:summed_rows].reshape(-1)
    gram_sum = totals[: vector_count * vector_count].reshape(vector_count, vector_count)
    column_sums = totals[vector_count * vector_count : vector_count * vector_count + vector_count]
    total_degree_sum = totals[vector_count * vector_count + vector_count]
    gathered = block[summed_rows:].reshape(-1, gather_width * 128)
    mean_walk = column_sums / total_degree_sum
    centres = gathered[:, :vector_count] - mean_walk
    drifts = gathered[:, vector_count:]
    cross = hdot(centres.T, drifts)
    gram_matrix = (gram_sum + cross + cross.T + block_rows * hdot(centres.T, centres)) / total_rows
    displaced_entries = jnp.concatenate([walk] + partner_walks) - mean_walk
    inverse_factor = factor_inverse(gram_matrix)
    bases = hdot(displaced_entries, inverse_factor.T)
    return [bases[i * block_rows : (i + 1) * block_rows] for i in range(1 + len(partner_walks))]


def on_device(embeddings, start, neighbours):
    wide_count = lax.axis_size("wide")
    lane_count = lax.axis_size("narrow")
    broad_index = lax.axis_index("wide")
    lane_index = lax.axis_index("narrow")
    far_reach = wide_count // 2 - 1
    fetch_offsets, pair_plan = difference_plan(wide_count, far_reach)
    unit_block = normalize_rows(embeddings)
    block_rows = unit_block.shape[0]
    total_rows = block_rows * wide_count * lane_count

    def block_at(offset):
        return (broad_index + offset) % wide_count * lane_count + lane_index

    owned_list = []
    for left, right in pair_plan:
        own_row = lax.dynamic_slice_in_dim(neighbours, block_at(left), 1, 0)[0]
        owned_list.append(jnp.any(own_row == block_at(right)))

    vector_count = start.shape[1]
    units = {0: unit_block}
    weights = {0: start}
    halves = {}
    half_rows = block_rows // 2
    for offset in fetch_offsets:
        if offset == fetch_offsets[-1]:
            units[offset] = normalize_rows(shifted(embeddings, "wide", -offset))
        else:
            halves[offset] = [
                shifted(unit_block[:half_rows], "wide", -offset),
                shifted(unit_block[half_rows:], "wide", -offset),
            ]
            units[offset] = None
        weights[offset] = shifted(start, "wide", -offset)

    self_mask = lax.broadcasted_iota(
        jnp.int32, (block_rows, block_rows), 0
    ) == lax.broadcasted_iota(jnp.int32, (block_rows, block_rows), 1)
    near_tile = jnp.where(
        self_mask, jnp.zeros((), jnp.bfloat16), scores_tile(unit_block, unit_block)
    )

    zero_part = jnp.zeros((block_rows, vector_count), jnp.float32)
    zero_sum = jnp.zeros((block_rows,), jnp.float32)
    parts = {offset: zero_part for offset in units}
    sums = {offset: zero_sum for offset in units}
    early = fetch_offsets[-1]
    early_ids = [i for i, pair in enumerate(pair_plan) if set(pair) <= {0, early}]
    tiles = [None] * len(pair_plan)
    early_results = []
    for i in early_ids:
        left, right = pair_plan[i]
        near_is_right = right == 0
        near_weights = weights[0]
        early_results.append(
            early_pass(owned_list[i], units[left], units[right], near_weights, near_is_right)
        )
    late_offsets = [offset for offset in fetch_offsets if offset != early]
    split_ids = [
        i
        for i, (left, right) in enumerate(pair_plan)
        if i not in early_ids and right in halves and left not in halves
    ]
    chunk_results = {}

    def run_chunk(i, h):
        left, right = pair_plan[i]
        rows = slice(h * half_rows, (h + 1) * half_rows)
        return column_chunk(
            owned_list[i], units[left], halves[right][h], weights[left], weights[right][rows]
        )

    for i in split_ids:
        chunk_results[(i, 0)] = run_chunk(i, 0)
    if early_ids or split_ids:
        late_halves, late_weights, early_results, first_chunks = lax.optimization_barrier(
            (
                [halves[o][1] for o in late_offsets if o in halves],
                [weights[o] for o in late_offsets],
                early_results,
                [chunk_results[(i, 0)] for i in split_ids],
            )
        )
        for position, offset in enumerate([o for o in late_offsets if o in halves]):
            halves[offset][1] = late_halves[position]
        for position, offset in enumerate(late_offsets):
            weights[offset] = late_weights[position]
        for position, i in enumerate(split_ids):
            chunk_results[(i, 0)] = first_chunks[position]
    for offset in halves:
        units[offset] = jnp.concatenate(halves[offset])
    for i in split_ids:
        chunk_results[(i, 1)] = run_chunk(i, 1)
        left, right = pair_plan[i]
        first, second = chunk_results[(i, 0)], chunk_results[(i, 1)]
        tiles[i] = jnp.concatenate([first[0], second[0]], axis=1)
        parts[left] = parts[left] + first[1] + second[1]
        sums[left] = sums[left] + first[2] + second[2]
        parts[right] = parts[right] + jnp.concatenate([first[3], second[3]])
        sums[right] = sums[right] + jnp.concatenate([first[4], second[4]])
    for i, (affinity, part, row_sum, col_sum) in zip(early_ids, early_results):
        left, right = pair_plan[i]
        near_is_right = right == 0
        tiles[i] = affinity
        far = left if near_is_right else right
        far_part = deferred_pass(owned_list[i], affinity, weights[far], not near_is_right)
        if near_is_right:
            row_part, col_part = part, far_part
        else:
            row_part, col_part = far_part, part
        parts[left] = parts[left] + row_part
        sums[left] = sums[left] + row_sum
        parts[right] = parts[right] + col_part
        sums[right] = sums[right] + col_sum
    for i, ((left, right), owned) in enumerate(zip(pair_plan, owned_list)):
        if i in early_ids or i in split_ids:
            continue
        affinity, row_part, row_sum, col_part, col_sum = first_pass(
            owned, units[left], units[right], weights[left], weights[right]
        )
        tiles[i] = affinity
        parts[left] = parts[left] + row_part
        sums[left] = sums[left] + row_sum
        parts[right] = parts[right] + col_part
        sums[right] = sums[right] + col_sum

    product = row_product(near_tile, start) + parts[0]
    vertex_valence = jnp.sum(near_tile, axis=1, dtype=jnp.float32) + sums[0]
    part_size = block_rows * vector_count
    for offset in fetch_offsets:
        sent = jnp.concatenate([as_rows(parts[offset].reshape(-1)), as_rows(sums[offset])])
        returned = shifted(sent, "wide", offset).reshape(-1)
        product = product + returned[:part_size].reshape(block_rows, vector_count)
        vertex_valence = vertex_valence + returned[part_size : part_size + block_rows]
    bases = orthonormal(product, vertex_valence, total_rows, fetch_offsets if ITERS > 1 else ())

    for iteration in range(1, ITERS):
        weights = {0: bases[0].astype(jnp.bfloat16)}
        for position, offset in enumerate(fetch_offsets):
            weights[offset] = bases[position + 1].astype(jnp.bfloat16)
        current = weights[0]
        parts = {offset: zero_part for offset in units}
        for (left, right), owned, affinity in zip(pair_plan, owned_list, tiles):
            row_part, col_part = later_pass(owned, affinity, weights[left], weights[right])
            parts[left] = parts[left] + row_part
            parts[right] = parts[right] + col_part
        product = row_product(near_tile, current) + parts[0]
        for offset in fetch_offsets:
            product = product + shifted(parts[offset], "wide", offset)
        last = iteration == ITERS - 1
        bases = orthonormal(product, vertex_valence, total_rows, () if last else fetch_offsets)
    return (bases[0], vertex_valence / block_rows)


def solution(mesh):
    in_specs = (P(("wide", "narrow"), None), P(("wide", "narrow"), None), P())
    out_specs = (P(("wide", "narrow"), None), P(("wide", "narrow")))
    return jax.shard_map(
        on_device, mesh=mesh, in_specs=in_specs, out_specs=out_specs, check_vma=False
    )
```

```python
from functools import partial
import itertools
import math

import jax
import jax.numpy as jnp
from jax import lax
from jax.sharding import PartitionSpec as P
from jax.experimental import pallas as pl

ITERS = 2
FETCH_PIECES = 2


kernel_width_factor = 0.05


def shifted(block, axis, distance):
    devices = range(lax.axis_size(axis))
    route = [((i - distance) % len(devices), i) for i in devices]
    return lax.ppermute(block, axis, route)


def ring_gap(offset, span):
    offset %= span
    return min(offset, span - offset)


def difference_plan(span, far_reach):
    candidates = sorted(range(1, span), key=lambda s: (ring_gap(s, span), s))
    for count in range(1, span):
        best = None
        for chosen in itertools.combinations(candidates, count):
            points = (0,) + chosen
            plan = {}
            for a, b in itertools.permutations(points, 2):
                gap = (b - a) % span
                if 1 <= gap <= far_reach and gap not in plan:
                    plan[gap] = (a, b)
            if len(plan) == far_reach:
                cost = sum(ring_gap(s, span) for s in chosen)
                if best is None or cost < best[0]:
                    best = (cost, chosen, plan)
        if best is not None:
            return list(best[1]), [best[2][gap] for gap in range(1, far_reach + 1)]
    raise ValueError("no plan")


def normalize_rows(values):
    values_wide = values.astype(jnp.float32)
    scaling = lax.rsqrt(jnp.mean(values_wide * values_wide, axis=-1, keepdims=True) + 1e-06)
    return (values_wide * scaling / math.sqrt(values_wide.shape[-1])).astype(jnp.bfloat16)


def scores_tile(leftside_block, right_block):
    kernel_entries = lax.dot_general(
        leftside_block, right_block, (((1,), (1,)), ((), ())), preferred_element_type=jnp.float32
    )
    return jnp.exp(kernel_entries / kernel_width_factor).astype(jnp.bfloat16)


def row_product(affinity, weights):
    return jnp.dot(affinity, weights, preferred_element_type=jnp.float32)


def col_product(affinity, weights):
    return lax.dot_general(
        affinity, weights, (((0,), (0,)), ((), ())), preferred_element_type=jnp.float32
    )


def first_pass(owned, left_unit, right_unit, left_weights, right_weights):
    block_rows = left_unit.shape[0]
    vector_count = left_weights.shape[1]

    def compute_pair():
        affinity = scores_tile(left_unit, right_unit)
        return (
            affinity,
            row_product(affinity, right_weights),
            jnp.sum(affinity, axis=1, dtype=jnp.float32),
            col_product(affinity, left_weights),
            jnp.sum(affinity, axis=0, dtype=jnp.float32),
        )

    def skip_pair():
        zero_part = jnp.zeros((block_rows, vector_count), jnp.float32)
        zero_sum = jnp.zeros((block_rows,), jnp.float32)
        return (
            jnp.zeros((block_rows, block_rows), jnp.bfloat16),
            zero_part,
            zero_sum,
            zero_part,
            zero_sum,
        )

    return lax.cond(owned, compute_pair, skip_pair)


def early_pass(owned, left_unit, right_unit, near_weights, near_is_right):
    block_rows = left_unit.shape[0]
    vector_count = near_weights.shape[1]

    def compute_pair():
        affinity = scores_tile(left_unit, right_unit)
        if near_is_right:
            part = row_product(affinity, near_weights)
        else:
            part = col_product(affinity, near_weights)
        return (
            affinity,
            part,
            jnp.sum(affinity, axis=1, dtype=jnp.float32),
            jnp.sum(affinity, axis=0, dtype=jnp.float32),
        )

    def skip_pair():
        zero_sum = jnp.zeros((block_rows,), jnp.float32)
        return (
            jnp.zeros((block_rows, block_rows), jnp.bfloat16),
            jnp.zeros((block_rows, vector_count), jnp.float32),
            zero_sum,
            zero_sum,
        )

    return lax.cond(owned, compute_pair, skip_pair)


def deferred_pass(owned, affinity, far_weights, far_is_right):
    block_rows = affinity.shape[0]
    vector_count = far_weights.shape[1]

    def compute_pair():
        if far_is_right:
            return row_product(affinity, far_weights)
        return col_product(affinity, far_weights)

    return lax.cond(
        owned, compute_pair, lambda: jnp.zeros((block_rows, vector_count), jnp.float32)
    )


def later_pass(owned, affinity, left_weights, right_weights):
    block_rows = affinity.shape[0]
    vector_count = left_weights.shape[1]

    def compute_pair():
        return (row_product(affinity, right_weights), col_product(affinity, left_weights))

    def skip_pair():
        zero_part = jnp.zeros((block_rows, vector_count), jnp.float32)
        return (zero_part, zero_part)

    return lax.cond(owned, compute_pair, skip_pair)


def butterfly(axis, summed_rows, block):
    size = lax.axis_size(axis)
    if size & (size - 1):
        return jnp.concatenate(
            [
                lax.psum(block[:summed_rows], axis),
                lax.all_gather(block[summed_rows:], axis, tiled=True),
            ]
        )
    index = lax.axis_index(axis)
    step = 1
    while step < size:
        route = [(i, i ^ step) for i in range(size)]
        other = lax.ppermute(block, axis, route)
        summed = block[:summed_rows] + other[:summed_rows]
        mine = block[summed_rows:]
        theirs = other[summed_rows:]
        upper = (index // step) % 2 == 1
        gathered = jnp.where(
            upper, jnp.concatenate([theirs, mine]), jnp.concatenate([mine, theirs])
        )
        block = jnp.concatenate([summed, gathered])
        step *= 2
    return block


def as_rows(vector, lanes=128):
    pad = (-vector.shape[0]) % lanes
    return jnp.pad(vector, (0, pad)).reshape(-1, lanes)


def hdot(left, right):
    return jnp.dot(left, right, precision=lax.Precision.HIGHEST, preferred_element_type=jnp.float32)


def factor_kernel(gram_ref, inverse_ref):
    size = gram_ref.shape[0]
    rows = lax.broadcasted_iota(jnp.int32, (size, size), 0)
    cols = lax.broadcasted_iota(jnp.int32, (size, size), 1)
    eye = jnp.where(rows == cols, 1.0, 0.0).astype(jnp.float32)

    def step(j, carry):
        remaining, inverse = carry
        column = jnp.sum(jnp.where(cols == j, remaining, 0.0), axis=1, keepdims=True)
        pivot = jnp.sum(jnp.where(rows[:, :1] == j, column, 0.0), axis=0, keepdims=True)
        scale = lax.rsqrt(pivot)
        factor_column = jnp.where(rows[:, :1] >= j, column * scale, 0.0)
        factor_row = jnp.sum(jnp.where(rows == j, remaining, 0.0), axis=0, keepdims=True)
        factor_row = jnp.where(cols[:1] >= j, factor_row * scale, 0.0)
        remaining = remaining - factor_column * factor_row
        inverse_row = jnp.sum(jnp.where(rows == j, inverse, 0.0), axis=0, keepdims=True) * scale
        inverse = jnp.where(rows == j, inverse_row, inverse)
        below = jnp.where(rows[:, :1] > j, factor_column, 0.0)
        inverse = inverse - below * inverse_row
        return remaining, inverse

    _, inverse = lax.fori_loop(0, size, step, (gram_ref[...], eye))
    inverse_ref[...] = inverse


def factor_inverse(gram_matrix):
    return pl.pallas_call(
        factor_kernel, out_shape=jax.ShapeDtypeStruct(gram_matrix.shape, jnp.float32)
    )(gram_matrix)


def orthonormal(product, vertex_valence, total_rows, fetch_offsets=()):
    block_rows, vector_count = product.shape
    walk = product / vertex_valence[:, None]
    partner_walks = [shifted(walk, "wide", -offset) for offset in fetch_offsets]
    centre = jnp.mean(walk, axis=0)
    centred = walk - centre
    local_gram = hdot(centred.T, centred)
    local_drift = jnp.sum(centred, axis=0)
    summed = jnp.concatenate(
        [
            as_rows(local_gram.reshape(-1)),
            as_rows(jnp.concatenate([jnp.sum(product, axis=0), jnp.sum(vertex_valence)[None]])),
        ]
    )
    summed_rows = summed.shape[0]
    block = jnp.concatenate([summed, as_rows(jnp.concatenate([centre, local_drift]))])
    gather_width = block.shape[0] - summed_rows
    for axis in ("narrow", "wide"):
        block = butterfly(axis, summed_rows, block)
    totals = block[:summed_rows].reshape(-1)
    gram_sum = totals[: vector_count * vector_count].reshape(vector_count, vector_count)
    column_sums = totals[vector_count * vector_count : vector_count * vector_count + vector_count]
    total_degree_sum = totals[vector_count * vector_count + vector_count]
    gathered = block[summed_rows:].reshape(-1, gather_width * 128)
    mean_walk = column_sums / total_degree_sum
    centres = gathered[:, :vector_count] - mean_walk
    drifts = gathered[:, vector_count:]
    cross = hdot(centres.T, drifts)
    gram_matrix = (gram_sum + cross + cross.T + block_rows * hdot(centres.T, centres)) / total_rows
    displaced_entries = jnp.concatenate([walk] + partner_walks) - mean_walk
    inverse_factor = factor_inverse(gram_matrix)
    bases = hdot(displaced_entries, inverse_factor.T)
    return [bases[i * block_rows : (i + 1) * block_rows] for i in range(1 + len(partner_walks))]


def on_device(embeddings, start, neighbours):
    wide_count = lax.axis_size("wide")
    lane_count = lax.axis_size("narrow")
    broad_index = lax.axis_index("wide")
    lane_index = lax.axis_index("narrow")
    far_reach = wide_count // 2 - 1
    fetch_offsets, pair_plan = difference_plan(wide_count, far_reach)
    unit_block = normalize_rows(embeddings)
    block_rows = unit_block.shape[0]
    total_rows = block_rows * wide_count * lane_count

    def block_at(offset):
        return (broad_index + offset) % wide_count * lane_count + lane_index

    owned_list = []
    for left, right in pair_plan:
        own_row = lax.dynamic_slice_in_dim(neighbours, block_at(left), 1, 0)[0]
        owned_list.append(jnp.any(own_row == block_at(right)))

    vector_count = start.shape[1]
    units = {0: unit_block}
    weights = {0: start}
    piece_rows = block_rows // FETCH_PIECES
    for offset in fetch_offsets:
        rows = embeddings if offset == fetch_offsets[-1] else unit_block
        pieces = [
            shifted(rows[i * piece_rows : (i + 1) * piece_rows], "wide", -offset)
            for i in range(FETCH_PIECES)
        ]
        arrived = jnp.concatenate(pieces)
        units[offset] = normalize_rows(arrived) if offset == fetch_offsets[-1] else arrived
        weights[offset] = shifted(start, "wide", -offset)

    self_mask = lax.broadcasted_iota(
        jnp.int32, (block_rows, block_rows), 0
    ) == lax.broadcasted_iota(jnp.int32, (block_rows, block_rows), 1)
    near_tile = jnp.where(
        self_mask, jnp.zeros((), jnp.bfloat16), scores_tile(unit_block, unit_block)
    )

    zero_part = jnp.zeros((block_rows, vector_count), jnp.float32)
    zero_sum = jnp.zeros((block_rows,), jnp.float32)
    parts = {offset: zero_part for offset in units}
    sums = {offset: zero_sum for offset in units}
    early = fetch_offsets[-1]
    early_ids = [i for i, pair in enumerate(pair_plan) if set(pair) <= {0, early}]
    tiles = [None] * len(pair_plan)
    early_results = []
    for i in early_ids:
        left, right = pair_plan[i]
        near_is_right = right == 0
        near_weights = weights[0]
        early_results.append(
            early_pass(owned_list[i], units[left], units[right], near_weights, near_is_right)
        )
    if early_ids:
        late_offsets = [offset for offset in fetch_offsets if offset != early]
        late_units, late_weights, early_results = lax.optimization_barrier(
            ([units[o] for o in late_offsets], [weights[o] for o in late_offsets], early_results)
        )
        for position, offset in enumerate(late_offsets):
            units[offset] = late_units[position]
            weights[offset] = late_weights[position]
    for i, (affinity, part, row_sum, col_sum) in zip(early_ids, early_results):
        left, right = pair_plan[i]
        near_is_right = right == 0
        tiles[i] = affinity
        far = left if near_is_right else right
        far_part = deferred_pass(owned_list[i], affinity, weights[far], not near_is_right)
        if near_is_right:
            row_part, col_part = part, far_part
        else:
            row_part, col_part = far_part, part
        parts[left] = parts[left] + row_part
        sums[left] = sums[left] + row_sum
        parts[right] = parts[right] + col_part
        sums[right] = sums[right] + col_sum
    for i, ((left, right), owned) in enumerate(zip(pair_plan, owned_list)):
        if i in early_ids:
            continue
        affinity, row_part, row_sum, col_part, col_sum = first_pass(
            owned, units[left], units[right], weights[left], weights[right]
        )
        tiles[i] = affinity
        parts[left] = parts[left] + row_part
        sums[left] = sums[left] + row_sum
        parts[right] = parts[right] + col_part
        sums[right] = sums[right] + col_sum

    product = row_product(near_tile, start) + parts[0]
    vertex_valence = jnp.sum(near_tile, axis=1, dtype=jnp.float32) + sums[0]
    part_size = block_rows * vector_count
    for offset in fetch_offsets:
        sent = jnp.concatenate([as_rows(parts[offset].reshape(-1)), as_rows(sums[offset])])
        returned = shifted(sent, "wide", offset).reshape(-1)
        product = product + returned[:part_size].reshape(block_rows, vector_count)
        vertex_valence = vertex_valence + returned[part_size : part_size + block_rows]
    bases = orthonormal(product, vertex_valence, total_rows, fetch_offsets if ITERS > 1 else ())

    for iteration in range(1, ITERS):
        weights = {0: bases[0].astype(jnp.bfloat16)}
        for position, offset in enumerate(fetch_offsets):
            weights[offset] = bases[position + 1].astype(jnp.bfloat16)
        current = weights[0]
        parts = {offset: zero_part for offset in units}
        for (left, right), owned, affinity in zip(pair_plan, owned_list, tiles):
            row_part, col_part = later_pass(owned, affinity, weights[left], weights[right])
            parts[left] = parts[left] + row_part
            parts[right] = parts[right] + col_part
        product = row_product(near_tile, current) + parts[0]
        for offset in fetch_offsets:
            product = product + shifted(parts[offset], "wide", offset)
        last = iteration == ITERS - 1
        bases = orthonormal(product, vertex_valence, total_rows, () if last else fetch_offsets)
    return (bases[0], vertex_valence / block_rows)


def solution(mesh):
    in_specs = (P(("wide", "narrow"), None), P(("wide", "narrow"), None), P())
    out_specs = (P(("wide", "narrow"), None), P(("wide", "narrow")))
    return jax.shard_map(
        on_device, mesh=mesh, in_specs=in_specs, out_specs=out_specs, check_vma=False
    )
```

```python
from functools import partial
import itertools
import math

import jax
import jax.numpy as jnp
from jax import lax
from jax.sharding import PartitionSpec as P
from jax.experimental import pallas as pl

ITERS = 2


kernel_width_factor = 0.05


def shifted(block, axis, distance):
    devices = range(lax.axis_size(axis))
    route = [((i - distance) % len(devices), i) for i in devices]
    return lax.ppermute(block, axis, route)


def ring_gap(offset, span):
    offset %= span
    return min(offset, span - offset)


def difference_plan(span, far_reach):
    candidates = sorted(range(1, span), key=lambda s: (ring_gap(s, span), s))
    for count in range(1, span):
        best = None
        for chosen in itertools.combinations(candidates, count):
            points = (0,) + chosen
            plan = {}
            for a, b in itertools.permutations(points, 2):
                gap = (b - a) % span
                if 1 <= gap <= far_reach and gap not in plan:
                    plan[gap] = (a, b)
            if len(plan) == far_reach:
                cost = sum(ring_gap(s, span) for s in chosen)
                if best is None or cost < best[0]:
                    best = (cost, chosen, plan)
        if best is not None:
            return list(best[1]), [best[2][gap] for gap in range(1, far_reach + 1)]
    raise ValueError("no plan")


def normalize_rows(values):
    values_wide = values.astype(jnp.float32)
    scaling = lax.rsqrt(jnp.mean(values_wide * values_wide, axis=-1, keepdims=True) + 1e-06)
    return (values_wide * scaling / math.sqrt(values_wide.shape[-1])).astype(jnp.bfloat16)


def scores_tile(leftside_block, right_block):
    kernel_entries = lax.dot_general(
        leftside_block, right_block, (((1,), (1,)), ((), ())), preferred_element_type=jnp.float32
    )
    return jnp.exp(kernel_entries / kernel_width_factor).astype(jnp.bfloat16)


def row_product(affinity, weights):
    return jnp.dot(affinity, weights, preferred_element_type=jnp.float32)


def col_product(affinity, weights):
    return lax.dot_general(
        affinity, weights, (((0,), (0,)), ((), ())), preferred_element_type=jnp.float32
    )


def first_pass(owned, left_unit, right_unit, left_weights, right_weights):
    block_rows = left_unit.shape[0]
    vector_count = left_weights.shape[1]

    def compute_pair():
        affinity = scores_tile(left_unit, right_unit)
        return (
            affinity,
            row_product(affinity, right_weights),
            jnp.sum(affinity, axis=1, dtype=jnp.float32),
            col_product(affinity, left_weights),
            jnp.sum(affinity, axis=0, dtype=jnp.float32),
        )

    def skip_pair():
        zero_part = jnp.zeros((block_rows, vector_count), jnp.float32)
        zero_sum = jnp.zeros((block_rows,), jnp.float32)
        return (
            jnp.zeros((block_rows, block_rows), jnp.bfloat16),
            zero_part,
            zero_sum,
            zero_part,
            zero_sum,
        )

    return lax.cond(owned, compute_pair, skip_pair)


def early_pass(owned, left_unit, right_unit, near_weights, near_is_right):
    block_rows = left_unit.shape[0]
    vector_count = near_weights.shape[1]

    def compute_pair():
        affinity = scores_tile(left_unit, right_unit)
        if near_is_right:
            part = row_product(affinity, near_weights)
        else:
            part = col_product(affinity, near_weights)
        return (
            affinity,
            part,
            jnp.sum(affinity, axis=1, dtype=jnp.float32),
            jnp.sum(affinity, axis=0, dtype=jnp.float32),
        )

    def skip_pair():
        zero_sum = jnp.zeros((block_rows,), jnp.float32)
        return (
            jnp.zeros((block_rows, block_rows), jnp.bfloat16),
            jnp.zeros((block_rows, vector_count), jnp.float32),
            zero_sum,
            zero_sum,
        )

    return lax.cond(owned, compute_pair, skip_pair)


def deferred_pass(owned, affinity, far_weights, far_is_right):
    block_rows = affinity.shape[0]
    vector_count = far_weights.shape[1]

    def compute_pair():
        if far_is_right:
            return row_product(affinity, far_weights)
        return col_product(affinity, far_weights)

    return lax.cond(
        owned, compute_pair, lambda: jnp.zeros((block_rows, vector_count), jnp.float32)
    )


def column_chunk(owned, left_unit, right_chunk, left_weights, right_weights_chunk):
    block_rows = left_unit.shape[0]
    chunk_rows = right_chunk.shape[0]
    vector_count = left_weights.shape[1]

    def compute_pair():
        affinity = scores_tile(left_unit, right_chunk)
        return (
            affinity,
            row_product(affinity, right_weights_chunk),
            jnp.sum(affinity, axis=1, dtype=jnp.float32),
            col_product(affinity, left_weights),
            jnp.sum(affinity, axis=0, dtype=jnp.float32),
        )

    def skip_pair():
        return (
            jnp.zeros((block_rows, chunk_rows), jnp.bfloat16),
            jnp.zeros((block_rows, vector_count), jnp.float32),
            jnp.zeros((block_rows,), jnp.float32),
            jnp.zeros((chunk_rows, vector_count), jnp.float32),
            jnp.zeros((chunk_rows,), jnp.float32),
        )

    return lax.cond(owned, compute_pair, skip_pair)


def later_pass(owned, affinity, left_weights, right_weights):
    block_rows = affinity.shape[0]
    vector_count = left_weights.shape[1]

    def compute_pair():
        return (row_product(affinity, right_weights), col_product(affinity, left_weights))

    def skip_pair():
        zero_part = jnp.zeros((block_rows, vector_count), jnp.float32)
        return (zero_part, zero_part)

    return lax.cond(owned, compute_pair, skip_pair)


def butterfly(axis, summed_rows, block):
    size = lax.axis_size(axis)
    if size & (size - 1):
        return jnp.concatenate(
            [
                lax.psum(block[:summed_rows], axis),
                lax.all_gather(block[summed_rows:], axis, tiled=True),
            ]
        )
    index = lax.axis_index(axis)
    step = 1
    while step < size:
        route = [(i, i ^ step) for i in range(size)]
        other = lax.ppermute(block, axis, route)
        summed = block[:summed_rows] + other[:summed_rows]
        mine = block[summed_rows:]
        theirs = other[summed_rows:]
        upper = (index // step) % 2 == 1
        gathered = jnp.where(
            upper, jnp.concatenate([theirs, mine]), jnp.concatenate([mine, theirs])
        )
        block = jnp.concatenate([summed, gathered])
        step *= 2
    return block


def as_rows(vector, lanes=128):
    pad = (-vector.shape[0]) % lanes
    return jnp.pad(vector, (0, pad)).reshape(-1, lanes)


def hdot(left, right):
    return jnp.dot(left, right, precision=lax.Precision.HIGHEST, preferred_element_type=jnp.float32)


def factor_kernel(gram_ref, inverse_ref):
    size = gram_ref.shape[0]
    rows = lax.broadcasted_iota(jnp.int32, (size, size), 0)
    cols = lax.broadcasted_iota(jnp.int32, (size, size), 1)
    eye = jnp.where(rows == cols, 1.0, 0.0).astype(jnp.float32)

    def step(j, carry):
        remaining, inverse = carry
        column = jnp.sum(jnp.where(cols == j, remaining, 0.0), axis=1, keepdims=True)
        pivot = jnp.sum(jnp.where(rows[:, :1] == j, column, 0.0), axis=0, keepdims=True)
        scale = lax.rsqrt(pivot)
        factor_column = jnp.where(rows[:, :1] >= j, column * scale, 0.0)
        factor_row = jnp.sum(jnp.where(rows == j, remaining, 0.0), axis=0, keepdims=True)
        factor_row = jnp.where(cols[:1] >= j, factor_row * scale, 0.0)
        remaining = remaining - factor_column * factor_row
        inverse_row = jnp.sum(jnp.where(rows == j, inverse, 0.0), axis=0, keepdims=True) * scale
        inverse = jnp.where(rows == j, inverse_row, inverse)
        below = jnp.where(rows[:, :1] > j, factor_column, 0.0)
        inverse = inverse - below * inverse_row
        return remaining, inverse

    _, inverse = lax.fori_loop(0, size, step, (gram_ref[...], eye))
    inverse_ref[...] = inverse


def factor_inverse(gram_matrix):
    return pl.pallas_call(
        factor_kernel, out_shape=jax.ShapeDtypeStruct(gram_matrix.shape, jnp.float32)
    )(gram_matrix)


def orthonormal(product, vertex_valence, total_rows, fetch_offsets=()):
    block_rows, vector_count = product.shape
    walk = product / vertex_valence[:, None]
    partner_walks = [shifted(walk, "wide", -offset) for offset in fetch_offsets]
    centre = jnp.mean(walk, axis=0)
    centred = walk - centre
    local_gram = hdot(centred.T, centred)
    local_drift = jnp.sum(centred, axis=0)
    summed = jnp.concatenate(
        [
            as_rows(local_gram.reshape(-1)),
            as_rows(jnp.concatenate([jnp.sum(product, axis=0), jnp.sum(vertex_valence)[None]])),
        ]
    )
    summed_rows = summed.shape[0]
    block = jnp.concatenate([summed, as_rows(jnp.concatenate([centre, local_drift]))])
    gather_width = block.shape[0] - summed_rows
    for axis in ("narrow", "wide"):
        block = butterfly(axis, summed_rows, block)
    totals = block[:summed_rows].reshape(-1)
    gram_sum = totals[: vector_count * vector_count].reshape(vector_count, vector_count)
    column_sums = totals[vector_count * vector_count : vector_count * vector_count + vector_count]
    total_degree_sum = totals[vector_count * vector_count + vector_count]
    gathered = block[summed_rows:].reshape(-1, gather_width * 128)
    mean_walk = column_sums / total_degree_sum
    centres = gathered[:, :vector_count] - mean_walk
    drifts = gathered[:, vector_count:]
    cross = hdot(centres.T, drifts)
    gram_matrix = (gram_sum + cross + cross.T + block_rows * hdot(centres.T, centres)) / total_rows
    displaced_entries = jnp.concatenate([walk] + partner_walks) - mean_walk
    inverse_factor = factor_inverse(gram_matrix)
    bases = hdot(displaced_entries, inverse_factor.T)
    return [bases[i * block_rows : (i + 1) * block_rows] for i in range(1 + len(partner_walks))]


def on_device(embeddings, start, neighbours):
    wide_count = lax.axis_size("wide")
    lane_count = lax.axis_size("narrow")
    broad_index = lax.axis_index("wide")
    lane_index = lax.axis_index("narrow")
    far_reach = wide_count // 2 - 1
    fetch_offsets, pair_plan = difference_plan(wide_count, far_reach)
    unit_block = normalize_rows(embeddings)
    block_rows = unit_block.shape[0]
    total_rows = block_rows * wide_count * lane_count

    def block_at(offset):
        return (broad_index + offset) % wide_count * lane_count + lane_index

    owned_list = []
    for left, right in pair_plan:
        own_row = lax.dynamic_slice_in_dim(neighbours, block_at(left), 1, 0)[0]
        owned_list.append(jnp.any(own_row == block_at(right)))

    vector_count = start.shape[1]
    units = {0: unit_block}
    weights = {0: start}
    halves = {}
    half_rows = block_rows // 2
    for offset in fetch_offsets:
        if offset == fetch_offsets[-1]:
            units[offset] = jnp.concatenate(
                [
                    normalize_rows(shifted(embeddings[:half_rows], "wide", -offset)),
                    normalize_rows(shifted(embeddings[half_rows:], "wide", -offset)),
                ]
            )
        else:
            halves[offset] = [
                shifted(unit_block[:half_rows], "wide", -offset),
                shifted(unit_block[half_rows:], "wide", -offset),
            ]
            units[offset] = None
        weights[offset] = shifted(start, "wide", -offset)

    self_mask = lax.broadcasted_iota(
        jnp.int32, (block_rows, block_rows), 0
    ) == lax.broadcasted_iota(jnp.int32, (block_rows, block_rows), 1)
    near_tile = jnp.where(
        self_mask, jnp.zeros((), jnp.bfloat16), scores_tile(unit_block, unit_block)
    )

    zero_part = jnp.zeros((block_rows, vector_count), jnp.float32)
    zero_sum = jnp.zeros((block_rows,), jnp.float32)
    parts = {offset: zero_part for offset in units}
    sums = {offset: zero_sum for offset in units}
    early = fetch_offsets[-1]
    early_ids = [i for i, pair in enumerate(pair_plan) if set(pair) <= {0, early}]
    tiles = [None] * len(pair_plan)
    early_results = []
    for i in early_ids:
        left, right = pair_plan[i]
        near_is_right = right == 0
        near_weights = weights[0]
        early_results.append(
            early_pass(owned_list[i], units[left], units[right], near_weights, near_is_right)
        )
    late_offsets = [offset for offset in fetch_offsets if offset != early]
    split_ids = [
        i
        for i, (left, right) in enumerate(pair_plan)
        if i not in early_ids and right in halves and left not in halves
    ]
    chunk_results = {}

    def run_chunk(i, h):
        left, right = pair_plan[i]
        rows = slice(h * half_rows, (h + 1) * half_rows)
        return column_chunk(
            owned_list[i], units[left], halves[right][h], weights[left], weights[right][rows]
        )

    for i in split_ids:
        chunk_results[(i, 0)] = run_chunk(i, 0)
    if early_ids or split_ids:
        late_halves, late_weights, early_results, first_chunks = lax.optimization_barrier(
            (
                [halves[o][1] for o in late_offsets if o in halves],
                [weights[o] for o in late_offsets],
                early_results,
                [chunk_results[(i, 0)] for i in split_ids],
            )
        )
        for position, offset in enumerate([o for o in late_offsets if o in halves]):
            halves[offset][1] = late_halves[position]
        for position, offset in enumerate(late_offsets):
            weights[offset] = late_weights[position]
        for position, i in enumerate(split_ids):
            chunk_results[(i, 0)] = first_chunks[position]
    for offset in halves:
        units[offset] = jnp.concatenate(halves[offset])
    for i in split_ids:
        chunk_results[(i, 1)] = run_chunk(i, 1)
        left, right = pair_plan[i]
        first, second = chunk_results[(i, 0)], chunk_results[(i, 1)]
        tiles[i] = jnp.concatenate([first[0], second[0]], axis=1)
        parts[left] = parts[left] + first[1] + second[1]
        sums[left] = sums[left] + first[2] + second[2]
        parts[right] = parts[right] + jnp.concatenate([first[3], second[3]])
        sums[right] = sums[right] + jnp.concatenate([first[4], second[4]])
    for i, (affinity, part, row_sum, col_sum) in zip(early_ids, early_results):
        left, right = pair_plan[i]
        near_is_right = right == 0
        tiles[i] = affinity
        far = left if near_is_right else right
        far_part = deferred_pass(owned_list[i], affinity, weights[far], not near_is_right)
        if near_is_right:
            row_part, col_part = part, far_part
        else:
            row_part, col_part = far_part, part
        parts[left] = parts[left] + row_part
        sums[left] = sums[left] + row_sum
        parts[right] = parts[right] + col_part
        sums[right] = sums[right] + col_sum
    for i, ((left, right), owned) in enumerate(zip(pair_plan, owned_list)):
        if i in early_ids or i in split_ids:
            continue
        affinity, row_part, row_sum, col_part, col_sum = first_pass(
            owned, units[left], units[right], weights[left], weights[right]
        )
        tiles[i] = affinity
        parts[left] = parts[left] + row_part
        sums[left] = sums[left] + row_sum
        parts[right] = parts[right] + col_part
        sums[right] = sums[right] + col_sum

    product = row_product(near_tile, start) + parts[0]
    vertex_valence = jnp.sum(near_tile, axis=1, dtype=jnp.float32) + sums[0]
    part_size = block_rows * vector_count
    for offset in fetch_offsets:
        sent = jnp.concatenate([as_rows(parts[offset].reshape(-1)), as_rows(sums[offset])])
        returned = shifted(sent, "wide", offset).reshape(-1)
        product = product + returned[:part_size].reshape(block_rows, vector_count)
        vertex_valence = vertex_valence + returned[part_size : part_size + block_rows]
    bases = orthonormal(product, vertex_valence, total_rows, fetch_offsets if ITERS > 1 else ())

    for iteration in range(1, ITERS):
        weights = {0: bases[0].astype(jnp.bfloat16)}
        for position, offset in enumerate(fetch_offsets):
            weights[offset] = bases[position + 1].astype(jnp.bfloat16)
        current = weights[0]
        parts = {offset: zero_part for offset in units}
        for (left, right), owned, affinity in zip(pair_plan, owned_list, tiles):
            row_part, col_part = later_pass(owned, affinity, weights[left], weights[right])
            parts[left] = parts[left] + row_part
            parts[right] = parts[right] + col_part
        product = row_product(near_tile, current) + parts[0]
        for offset in fetch_offsets:
            product = product + shifted(parts[offset], "wide", offset)
        last = iteration == ITERS - 1
        bases = orthonormal(product, vertex_valence, total_rows, () if last else fetch_offsets)
    return (bases[0], vertex_valence / block_rows)


def solution(mesh):
    in_specs = (P(("wide", "narrow"), None), P(("wide", "narrow"), None), P())
    out_specs = (P(("wide", "narrow"), None), P(("wide", "narrow")))
    return jax.shard_map(
        on_device, mesh=mesh, in_specs=in_specs, out_specs=out_specs, check_vma=False
    )
```

```python
from functools import partial
import itertools
import math

import jax
import jax.numpy as jnp
from jax import lax
from jax.sharding import PartitionSpec as P
from jax.experimental import pallas as pl

ITERS = 2


kernel_width_factor = 0.05


def shifted(block, axis, distance):
    devices = range(lax.axis_size(axis))
    route = [((i - distance) % len(devices), i) for i in devices]
    return lax.ppermute(block, axis, route)


def ring_gap(offset, span):
    offset %= span
    return min(offset, span - offset)


def difference_plan(span, far_reach):
    candidates = sorted(range(1, span), key=lambda s: (ring_gap(s, span), s))
    for count in range(1, span):
        best = None
        for chosen in itertools.combinations(candidates, count):
            points = (0,) + chosen
            plan = {}
            for a, b in itertools.permutations(points, 2):
                gap = (b - a) % span
                if 1 <= gap <= far_reach and gap not in plan:
                    plan[gap] = (a, b)
            if len(plan) == far_reach:
                cost = sum(ring_gap(s, span) for s in chosen)
                if best is None or cost < best[0]:
                    best = (cost, chosen, plan)
        if best is not None:
            return list(best[1]), [best[2][gap] for gap in range(1, far_reach + 1)]
    raise ValueError("no plan")


def normalize_rows(values):
    values_wide = values.astype(jnp.float32)
    scaling = lax.rsqrt(jnp.mean(values_wide * values_wide, axis=-1, keepdims=True) + 1e-06)
    return (values_wide * scaling / math.sqrt(values_wide.shape[-1])).astype(jnp.bfloat16)


def scores_tile(leftside_block, right_block):
    kernel_entries = lax.dot_general(
        leftside_block, right_block, (((1,), (1,)), ((), ())), preferred_element_type=jnp.float32
    )
    return jnp.exp(kernel_entries / kernel_width_factor).astype(jnp.bfloat16)


def row_product(affinity, weights):
    return jnp.dot(affinity, weights, preferred_element_type=jnp.float32)


def col_product(affinity, weights):
    return lax.dot_general(
        affinity, weights, (((0,), (0,)), ((), ())), preferred_element_type=jnp.float32
    )


def first_pass(owned, left_unit, right_unit, left_weights, right_weights):
    block_rows = left_unit.shape[0]
    vector_count = left_weights.shape[1]

    def compute_pair():
        affinity = scores_tile(left_unit, right_unit)
        return (
            affinity,
            row_product(affinity, right_weights),
            jnp.sum(affinity, axis=1, dtype=jnp.float32),
            col_product(affinity, left_weights),
            jnp.sum(affinity, axis=0, dtype=jnp.float32),
        )

    def skip_pair():
        zero_part = jnp.zeros((block_rows, vector_count), jnp.float32)
        zero_sum = jnp.zeros((block_rows,), jnp.float32)
        return (
            jnp.zeros((block_rows, block_rows), jnp.bfloat16),
            zero_part,
            zero_sum,
            zero_part,
            zero_sum,
        )

    return lax.cond(owned, compute_pair, skip_pair)


def early_pass(owned, left_unit, right_unit, near_weights, near_is_right):
    block_rows = left_unit.shape[0]
    vector_count = near_weights.shape[1]

    def compute_pair():
        affinity = scores_tile(left_unit, right_unit)
        if near_is_right:
            part = row_product(affinity, near_weights)
        else:
            part = col_product(affinity, near_weights)
        return (
            affinity,
            part,
            jnp.sum(affinity, axis=1, dtype=jnp.float32),
            jnp.sum(affinity, axis=0, dtype=jnp.float32),
        )

    def skip_pair():
        zero_sum = jnp.zeros((block_rows,), jnp.float32)
        return (
            jnp.zeros((block_rows, block_rows), jnp.bfloat16),
            jnp.zeros((block_rows, vector_count), jnp.float32),
            zero_sum,
            zero_sum,
        )

    return lax.cond(owned, compute_pair, skip_pair)


def deferred_pass(owned, affinity, far_weights, far_is_right):
    block_rows = affinity.shape[0]
    vector_count = far_weights.shape[1]

    def compute_pair():
        if far_is_right:
            return row_product(affinity, far_weights)
        return col_product(affinity, far_weights)

    return lax.cond(
        owned, compute_pair, lambda: jnp.zeros((block_rows, vector_count), jnp.float32)
    )


def column_chunk(owned, left_unit, right_chunk, left_weights, right_weights_chunk):
    block_rows = left_unit.shape[0]
    chunk_rows = right_chunk.shape[0]
    vector_count = left_weights.shape[1]

    def compute_pair():
        affinity = scores_tile(left_unit, right_chunk)
        return (
            affinity,
            row_product(affinity, right_weights_chunk),
            jnp.sum(affinity, axis=1, dtype=jnp.float32),
            col_product(affinity, left_weights),
            jnp.sum(affinity, axis=0, dtype=jnp.float32),
        )

    def skip_pair():
        return (
            jnp.zeros((block_rows, chunk_rows), jnp.bfloat16),
            jnp.zeros((block_rows, vector_count), jnp.float32),
            jnp.zeros((block_rows,), jnp.float32),
            jnp.zeros((chunk_rows, vector_count), jnp.float32),
            jnp.zeros((chunk_rows,), jnp.float32),
        )

    return lax.cond(owned, compute_pair, skip_pair)


def later_pass(owned, affinity, left_weights, right_weights):
    block_rows = affinity.shape[0]
    vector_count = left_weights.shape[1]

    def compute_pair():
        return (row_product(affinity, right_weights), col_product(affinity, left_weights))

    def skip_pair():
        zero_part = jnp.zeros((block_rows, vector_count), jnp.float32)
        return (zero_part, zero_part)

    return lax.cond(owned, compute_pair, skip_pair)


def butterfly(axis, summed_rows, block):
    size = lax.axis_size(axis)
    if size & (size - 1):
        return jnp.concatenate(
            [
                lax.psum(block[:summed_rows], axis),
                lax.all_gather(block[summed_rows:], axis, tiled=True),
            ]
        )
    index = lax.axis_index(axis)
    step = 1
    while step < size:
        route = [(i, i ^ step) for i in range(size)]
        other = lax.ppermute(block, axis, route)
        summed = block[:summed_rows] + other[:summed_rows]
        mine = block[summed_rows:]
        theirs = other[summed_rows:]
        upper = (index // step) % 2 == 1
        gathered = jnp.where(
            upper, jnp.concatenate([theirs, mine]), jnp.concatenate([mine, theirs])
        )
        block = jnp.concatenate([summed, gathered])
        step *= 2
    return block


def as_rows(vector, lanes=128):
    pad = (-vector.shape[0]) % lanes
    return jnp.pad(vector, (0, pad)).reshape(-1, lanes)


def hdot(left, right):
    return jnp.dot(left, right, precision=lax.Precision.HIGHEST, preferred_element_type=jnp.float32)


def factor_kernel(gram_ref, inverse_ref):
    size = gram_ref.shape[0]
    rows = lax.broadcasted_iota(jnp.int32, (size, size), 0)
    cols = lax.broadcasted_iota(jnp.int32, (size, size), 1)
    eye = jnp.where(rows == cols, 1.0, 0.0).astype(jnp.float32)

    def step(j, carry):
        remaining, inverse = carry
        column = jnp.sum(jnp.where(cols == j, remaining, 0.0), axis=1, keepdims=True)
        pivot = jnp.sum(jnp.where(rows[:, :1] == j, column, 0.0), axis=0, keepdims=True)
        scale = lax.rsqrt(pivot)
        factor_column = jnp.where(rows[:, :1] >= j, column * scale, 0.0)
        factor_row = jnp.sum(jnp.where(rows == j, remaining, 0.0), axis=0, keepdims=True)
        factor_row = jnp.where(cols[:1] >= j, factor_row * scale, 0.0)
        remaining = remaining - factor_column * factor_row
        inverse_row = jnp.sum(jnp.where(rows == j, inverse, 0.0), axis=0, keepdims=True) * scale
        inverse = jnp.where(rows == j, inverse_row, inverse)
        below = jnp.where(rows[:, :1] > j, factor_column, 0.0)
        inverse = inverse - below * inverse_row
        return remaining, inverse

    _, inverse = lax.fori_loop(0, size, step, (gram_ref[...], eye))
    inverse_ref[...] = inverse


def factor_inverse(gram_matrix):
    return pl.pallas_call(
        factor_kernel, out_shape=jax.ShapeDtypeStruct(gram_matrix.shape, jnp.float32)
    )(gram_matrix)


def orthonormal(product, vertex_valence, total_rows, fetch_offsets=()):
    block_rows, vector_count = product.shape
    walk = product / vertex_valence[:, None]
    partner_walks = [shifted(walk, "wide", -offset) for offset in fetch_offsets]
    centre = jnp.mean(walk, axis=0)
    centred = walk - centre
    local_gram = hdot(centred.T, centred)
    local_drift = jnp.sum(centred, axis=0)
    summed = jnp.concatenate(
        [
            as_rows(local_gram.reshape(-1)),
            as_rows(jnp.concatenate([jnp.sum(product, axis=0), jnp.sum(vertex_valence)[None]])),
        ]
    )
    summed_rows = summed.shape[0]
    block = jnp.concatenate([summed, as_rows(jnp.concatenate([centre, local_drift]))])
    gather_width = block.shape[0] - summed_rows
    for axis in ("wide", "narrow"):
        block = butterfly(axis, summed_rows, block)
    totals = block[:summed_rows].reshape(-1)
    gram_sum = totals[: vector_count * vector_count].reshape(vector_count, vector_count)
    column_sums = totals[vector_count * vector_count : vector_count * vector_count + vector_count]
    total_degree_sum = totals[vector_count * vector_count + vector_count]
    gathered = block[summed_rows:].reshape(-1, gather_width * 128)
    mean_walk = column_sums / total_degree_sum
    centres = gathered[:, :vector_count] - mean_walk
    drifts = gathered[:, vector_count:]
    cross = hdot(centres.T, drifts)
    gram_matrix = (gram_sum + cross + cross.T + block_rows * hdot(centres.T, centres)) / total_rows
    displaced_entries = jnp.concatenate([walk] + partner_walks) - mean_walk
    inverse_factor = factor_inverse(gram_matrix)
    bases = hdot(displaced_entries, inverse_factor.T)
    return [bases[i * block_rows : (i + 1) * block_rows] for i in range(1 + len(partner_walks))]


def on_device(embeddings, start, neighbours):
    wide_count = lax.axis_size("wide")
    lane_count = lax.axis_size("narrow")
    broad_index = lax.axis_index("wide")
    lane_index = lax.axis_index("narrow")
    far_reach = wide_count // 2 - 1
    fetch_offsets, pair_plan = difference_plan(wide_count, far_reach)
    unit_block = normalize_rows(embeddings)
    block_rows = unit_block.shape[0]
    total_rows = block_rows * wide_count * lane_count

    def block_at(offset):
        return (broad_index + offset) % wide_count * lane_count + lane_index

    owned_list = []
    for left, right in pair_plan:
        own_row = lax.dynamic_slice_in_dim(neighbours, block_at(left), 1, 0)[0]
        owned_list.append(jnp.any(own_row == block_at(right)))

    vector_count = start.shape[1]
    units = {0: unit_block}
    weights = {0: start}
    halves = {}
    half_rows = block_rows // 2
    for offset in fetch_offsets:
        if offset == fetch_offsets[-1]:
            units[offset] = normalize_rows(shifted(embeddings, "wide", -offset))
        else:
            halves[offset] = [
                shifted(unit_block[:half_rows], "wide", -offset),
                shifted(unit_block[half_rows:], "wide", -offset),
            ]
            units[offset] = None
        weights[offset] = shifted(start, "wide", -offset)

    self_mask = lax.broadcasted_iota(
        jnp.int32, (block_rows, block_rows), 0
    ) == lax.broadcasted_iota(jnp.int32, (block_rows, block_rows), 1)
    near_tile = jnp.where(
        self_mask, jnp.zeros((), jnp.bfloat16), scores_tile(unit_block, unit_block)
    )

    zero_part = jnp.zeros((block_rows, vector_count), jnp.float32)
    zero_sum = jnp.zeros((block_rows,), jnp.float32)
    parts = {offset: zero_part for offset in units}
    sums = {offset: zero_sum for offset in units}
    early = fetch_offsets[-1]
    early_ids = [i for i, pair in enumerate(pair_plan) if set(pair) <= {0, early}]
    tiles = [None] * len(pair_plan)
    early_results = []
    for i in early_ids:
        left, right = pair_plan[i]
        near_is_right = right == 0
        near_weights = weights[0]
        early_results.append(
            early_pass(owned_list[i], units[left], units[right], near_weights, near_is_right)
        )
    late_offsets = [offset for offset in fetch_offsets if offset != early]
    split_ids = [
        i
        for i, (left, right) in enumerate(pair_plan)
        if i not in early_ids and right in halves and left not in halves
    ]
    chunk_results = {}

    def run_chunk(i, h):
        left, right = pair_plan[i]
        rows = slice(h * half_rows, (h + 1) * half_rows)
        return column_chunk(
            owned_list[i], units[left], halves[right][h], weights[left], weights[right][rows]
        )

    for i in split_ids:
        chunk_results[(i, 0)] = run_chunk(i, 0)
    if early_ids or split_ids:
        late_halves, late_weights, early_results, first_chunks = lax.optimization_barrier(
            (
                [halves[o][1] for o in late_offsets if o in halves],
                [weights[o] for o in late_offsets],
                early_results,
                [chunk_results[(i, 0)] for i in split_ids],
            )
        )
        for position, offset in enumerate([o for o in late_offsets if o in halves]):
            halves[offset][1] = late_halves[position]
        for position, offset in enumerate(late_offsets):
            weights[offset] = late_weights[position]
        for position, i in enumerate(split_ids):
            chunk_results[(i, 0)] = first_chunks[position]
    for offset in halves:
        units[offset] = jnp.concatenate(halves[offset])
    for i in split_ids:
        chunk_results[(i, 1)] = run_chunk(i, 1)
        left, right = pair_plan[i]
        first, second = chunk_results[(i, 0)], chunk_results[(i, 1)]
        tiles[i] = jnp.concatenate([first[0], second[0]], axis=1)
        parts[left] = parts[left] + first[1] + second[1]
        sums[left] = sums[left] + first[2] + second[2]
        parts[right] = parts[right] + jnp.concatenate([first[3], second[3]])
        sums[right] = sums[right] + jnp.concatenate([first[4], second[4]])
    for i, (affinity, part, row_sum, col_sum) in zip(early_ids, early_results):
        left, right = pair_plan[i]
        near_is_right = right == 0
        tiles[i] = affinity
        far = left if near_is_right else right
        far_part = deferred_pass(owned_list[i], affinity, weights[far], not near_is_right)
        if near_is_right:
            row_part, col_part = part, far_part
        else:
            row_part, col_part = far_part, part
        parts[left] = parts[left] + row_part
        sums[left] = sums[left] + row_sum
        parts[right] = parts[right] + col_part
        sums[right] = sums[right] + col_sum
    for i, ((left, right), owned) in enumerate(zip(pair_plan, owned_list)):
        if i in early_ids or i in split_ids:
            continue
        affinity, row_part, row_sum, col_part, col_sum = first_pass(
            owned, units[left], units[right], weights[left], weights[right]
        )
        tiles[i] = affinity
        parts[left] = parts[left] + row_part
        sums[left] = sums[left] + row_sum
        parts[right] = parts[right] + col_part
        sums[right] = sums[right] + col_sum

    product = row_product(near_tile, start) + parts[0]
    vertex_valence = jnp.sum(near_tile, axis=1, dtype=jnp.float32) + sums[0]
    part_size = block_rows * vector_count
    for offset in fetch_offsets:
        sent = jnp.concatenate([as_rows(parts[offset].reshape(-1)), as_rows(sums[offset])])
        returned = shifted(sent, "wide", offset).reshape(-1)
        product = product + returned[:part_size].reshape(block_rows, vector_count)
        vertex_valence = vertex_valence + returned[part_size : part_size + block_rows]
    bases = orthonormal(product, vertex_valence, total_rows, fetch_offsets if ITERS > 1 else ())

    for iteration in range(1, ITERS):
        weights = {0: bases[0].astype(jnp.bfloat16)}
        for position, offset in enumerate(fetch_offsets):
            weights[offset] = bases[position + 1].astype(jnp.bfloat16)
        current = weights[0]
        parts = {offset: zero_part for offset in units}
        for (left, right), owned, affinity in zip(pair_plan, owned_list, tiles):
            row_part, col_part = later_pass(owned, affinity, weights[left], weights[right])
            parts[left] = parts[left] + row_part
            parts[right] = parts[right] + col_part
        product = row_product(near_tile, current) + parts[0]
        for offset in fetch_offsets:
            product = product + shifted(parts[offset], "wide", offset)
        last = iteration == ITERS - 1
        bases = orthonormal(product, vertex_valence, total_rows, () if last else fetch_offsets)
    return (bases[0], vertex_valence / block_rows)


def solution(mesh):
    in_specs = (P(("wide", "narrow"), None), P(("wide", "narrow"), None), P())
    out_specs = (P(("wide", "narrow"), None), P(("wide", "narrow")))
    return jax.shard_map(
        on_device, mesh=mesh, in_specs=in_specs, out_specs=out_specs, check_vma=False
    )
```

```python
from functools import partial
import itertools
import math

import jax
import jax.numpy as jnp
from jax import lax
from jax.sharding import PartitionSpec as P
from jax.experimental import pallas as pl

ITERS = 2


kernel_width_factor = 0.05


def shifted(block, axis, distance):
    devices = range(lax.axis_size(axis))
    route = [((i - distance) % len(devices), i) for i in devices]
    return lax.ppermute(block, axis, route)


def ring_gap(offset, span):
    offset %= span
    return min(offset, span - offset)


def difference_plan(span, far_reach):
    candidates = sorted(range(1, span), key=lambda s: (ring_gap(s, span), s))
    for count in range(1, span):
        best = None
        for chosen in itertools.combinations(candidates, count):
            points = (0,) + chosen
            plan = {}
            for a, b in itertools.permutations(points, 2):
                gap = (b - a) % span
                if 1 <= gap <= far_reach and gap not in plan:
                    plan[gap] = (a, b)
            if len(plan) == far_reach:
                cost = sum(ring_gap(s, span) for s in chosen)
                if best is None or cost < best[0]:
                    best = (cost, chosen, plan)
        if best is not None:
            return list(best[1]), [best[2][gap] for gap in range(1, far_reach + 1)]
    raise ValueError("no plan")


def normalize_rows(values):
    values_wide = values.astype(jnp.float32)
    scaling = lax.rsqrt(jnp.mean(values_wide * values_wide, axis=-1, keepdims=True) + 1e-06)
    return (values_wide * scaling / math.sqrt(values_wide.shape[-1])).astype(jnp.bfloat16)


def scores_tile(leftside_block, right_block):
    kernel_entries = lax.dot_general(
        leftside_block, right_block, (((1,), (1,)), ((), ())), preferred_element_type=jnp.float32
    )
    return jnp.exp(kernel_entries / kernel_width_factor).astype(jnp.bfloat16)


def row_product(affinity, weights):
    return jnp.dot(affinity, weights, preferred_element_type=jnp.float32)


def col_product(affinity, weights):
    return lax.dot_general(
        affinity, weights, (((0,), (0,)), ((), ())), preferred_element_type=jnp.float32
    )


def first_pass(owned, left_unit, right_unit, left_weights, right_weights):
    block_rows = left_unit.shape[0]
    vector_count = left_weights.shape[1]

    def compute_pair():
        affinity = scores_tile(left_unit, right_unit)
        return (
            affinity,
            row_product(affinity, right_weights),
            jnp.sum(affinity, axis=1, dtype=jnp.float32),
            col_product(affinity, left_weights),
            jnp.sum(affinity, axis=0, dtype=jnp.float32),
        )

    def skip_pair():
        zero_part = jnp.zeros((block_rows, vector_count), jnp.float32)
        zero_sum = jnp.zeros((block_rows,), jnp.float32)
        return (
            jnp.zeros((block_rows, block_rows), jnp.bfloat16),
            zero_part,
            zero_sum,
            zero_part,
            zero_sum,
        )

    return lax.cond(owned, compute_pair, skip_pair)


def early_pass(owned, left_unit, right_unit, near_weights, near_is_right):
    block_rows = left_unit.shape[0]
    vector_count = near_weights.shape[1]

    def compute_pair():
        affinity = scores_tile(left_unit, right_unit)
        if near_is_right:
            part = row_product(affinity, near_weights)
        else:
            part = col_product(affinity, near_weights)
        return (
            affinity,
            part,
            jnp.sum(affinity, axis=1, dtype=jnp.float32),
            jnp.sum(affinity, axis=0, dtype=jnp.float32),
        )

    def skip_pair():
        zero_sum = jnp.zeros((block_rows,), jnp.float32)
        return (
            jnp.zeros((block_rows, block_rows), jnp.bfloat16),
            jnp.zeros((block_rows, vector_count), jnp.float32),
            zero_sum,
            zero_sum,
        )

    return lax.cond(owned, compute_pair, skip_pair)


def deferred_pass(owned, affinity, far_weights, far_is_right):
    block_rows = affinity.shape[0]
    vector_count = far_weights.shape[1]

    def compute_pair():
        if far_is_right:
            return row_product(affinity, far_weights)
        return col_product(affinity, far_weights)

    return lax.cond(
        owned, compute_pair, lambda: jnp.zeros((block_rows, vector_count), jnp.float32)
    )


def column_chunk(owned, left_unit, right_chunk, left_weights, right_weights_chunk):
    block_rows = left_unit.shape[0]
    chunk_rows = right_chunk.shape[0]
    vector_count = left_weights.shape[1]

    def compute_pair():
        affinity = scores_tile(left_unit, right_chunk)
        return (
            affinity,
            row_product(affinity, right_weights_chunk),
            jnp.sum(affinity, axis=1, dtype=jnp.float32),
            col_product(affinity, left_weights),
            jnp.sum(affinity, axis=0, dtype=jnp.float32),
        )

    def skip_pair():
        return (
            jnp.zeros((block_rows, chunk_rows), jnp.bfloat16),
            jnp.zeros((block_rows, vector_count), jnp.float32),
            jnp.zeros((block_rows,), jnp.float32),
            jnp.zeros((chunk_rows, vector_count), jnp.float32),
            jnp.zeros((chunk_rows,), jnp.float32),
        )

    return lax.cond(owned, compute_pair, skip_pair)


def later_pass(owned, affinity, left_weights, right_weights):
    block_rows = affinity.shape[0]
    vector_count = left_weights.shape[1]

    def compute_pair():
        return (row_product(affinity, right_weights), col_product(affinity, left_weights))

    def skip_pair():
        zero_part = jnp.zeros((block_rows, vector_count), jnp.float32)
        return (zero_part, zero_part)

    return lax.cond(owned, compute_pair, skip_pair)


def butterfly(axis, summed_rows, block):
    size = lax.axis_size(axis)
    if size & (size - 1):
        return jnp.concatenate(
            [
                lax.psum(block[:summed_rows], axis),
                lax.all_gather(block[summed_rows:], axis, tiled=True),
            ]
        )
    index = lax.axis_index(axis)
    step = 1
    while step < size:
        route = [(i, i ^ step) for i in range(size)]
        other = lax.ppermute(block, axis, route)
        summed = block[:summed_rows] + other[:summed_rows]
        mine = block[summed_rows:]
        theirs = other[summed_rows:]
        upper = (index // step) % 2 == 1
        gathered = jnp.where(
            upper, jnp.concatenate([theirs, mine]), jnp.concatenate([mine, theirs])
        )
        block = jnp.concatenate([summed, gathered])
        step *= 2
    return block


def as_rows(vector, lanes=128):
    pad = (-vector.shape[0]) % lanes
    return jnp.pad(vector, (0, pad)).reshape(-1, lanes)


def hdot(left, right):
    return jnp.dot(left, right, precision=lax.Precision.HIGHEST, preferred_element_type=jnp.float32)


def factor_kernel(gram_ref, inverse_ref):
    size = gram_ref.shape[0]
    rows = lax.broadcasted_iota(jnp.int32, (size, size), 0)
    cols = lax.broadcasted_iota(jnp.int32, (size, size), 1)
    eye = jnp.where(rows == cols, 1.0, 0.0).astype(jnp.float32)

    def step(j, carry):
        remaining, inverse = carry
        pivot_row = jnp.sum(jnp.where(rows == j, remaining, 0.0), axis=0, keepdims=True)
        pivot = jnp.sum(jnp.where(cols[:1] == j, pivot_row, 0.0), axis=1, keepdims=True)
        column = jnp.sum(jnp.where(cols == j, remaining, 0.0), axis=1, keepdims=True)
        scale = lax.rsqrt(pivot)
        factor_column = jnp.where(rows[:, :1] >= j, column * scale, 0.0)
        factor_row = jnp.where(cols[:1] >= j, pivot_row * scale, 0.0)
        remaining = remaining - factor_column * factor_row
        inverse_row = jnp.sum(jnp.where(rows == j, inverse, 0.0), axis=0, keepdims=True) * scale
        inverse = jnp.where(rows == j, inverse_row, inverse)
        below = jnp.where(rows[:, :1] > j, factor_column, 0.0)
        inverse = inverse - below * inverse_row
        return remaining, inverse

    _, inverse = lax.fori_loop(0, size, step, (gram_ref[...], eye))
    inverse_ref[...] = inverse


def factor_inverse(gram_matrix):
    return pl.pallas_call(
        factor_kernel, out_shape=jax.ShapeDtypeStruct(gram_matrix.shape, jnp.float32)
    )(gram_matrix)


def orthonormal(product, vertex_valence, total_rows, fetch_offsets=()):
    block_rows, vector_count = product.shape
    walk = product / vertex_valence[:, None]
    partner_walks = [shifted(walk, "wide", -offset) for offset in fetch_offsets]
    centre = jnp.mean(walk, axis=0)
    centred = walk - centre
    local_gram = hdot(centred.T, centred)
    local_drift = jnp.sum(centred, axis=0)
    summed = jnp.concatenate(
        [
            as_rows(local_gram.reshape(-1)),
            as_rows(jnp.concatenate([jnp.sum(product, axis=0), jnp.sum(vertex_valence)[None]])),
        ]
    )
    summed_rows = summed.shape[0]
    block = jnp.concatenate([summed, as_rows(jnp.concatenate([centre, local_drift]))])
    gather_width = block.shape[0] - summed_rows
    for axis in ("narrow", "wide"):
        block = butterfly(axis, summed_rows, block)
    totals = block[:summed_rows].reshape(-1)
    gram_sum = totals[: vector_count * vector_count].reshape(vector_count, vector_count)
    column_sums = totals[vector_count * vector_count : vector_count * vector_count + vector_count]
    total_degree_sum = totals[vector_count * vector_count + vector_count]
    gathered = block[summed_rows:].reshape(-1, gather_width * 128)
    mean_walk = column_sums / total_degree_sum
    centres = gathered[:, :vector_count] - mean_walk
    drifts = gathered[:, vector_count:]
    cross = hdot(centres.T, drifts)
    gram_matrix = (gram_sum + cross + cross.T + block_rows * hdot(centres.T, centres)) / total_rows
    displaced_entries = jnp.concatenate([walk] + partner_walks) - mean_walk
    inverse_factor = factor_inverse(gram_matrix)
    bases = hdot(displaced_entries, inverse_factor.T)
    return [bases[i * block_rows : (i + 1) * block_rows] for i in range(1 + len(partner_walks))]


def on_device(embeddings, start, neighbours):
    wide_count = lax.axis_size("wide")
    lane_count = lax.axis_size("narrow")
    broad_index = lax.axis_index("wide")
    lane_index = lax.axis_index("narrow")
    far_reach = wide_count // 2 - 1
    fetch_offsets, pair_plan = difference_plan(wide_count, far_reach)
    unit_block = normalize_rows(embeddings)
    block_rows = unit_block.shape[0]
    total_rows = block_rows * wide_count * lane_count

    def block_at(offset):
        return (broad_index + offset) % wide_count * lane_count + lane_index

    owned_list = []
    for left, right in pair_plan:
        own_row = lax.dynamic_slice_in_dim(neighbours, block_at(left), 1, 0)[0]
        owned_list.append(jnp.any(own_row == block_at(right)))

    vector_count = start.shape[1]
    units = {0: unit_block}
    weights = {0: start}
    halves = {}
    half_rows = block_rows // 2
    for offset in fetch_offsets:
        if offset == fetch_offsets[-1]:
            units[offset] = normalize_rows(shifted(embeddings, "wide", -offset))
        else:
            halves[offset] = [
                shifted(unit_block[:half_rows], "wide", -offset),
                shifted(unit_block[half_rows:], "wide", -offset),
            ]
            units[offset] = None
        weights[offset] = shifted(start, "wide", -offset)

    self_mask = lax.broadcasted_iota(
        jnp.int32, (block_rows, block_rows), 0
    ) == lax.broadcasted_iota(jnp.int32, (block_rows, block_rows), 1)
    near_tile = jnp.where(
        self_mask, jnp.zeros((), jnp.bfloat16), scores_tile(unit_block, unit_block)
    )

    zero_part = jnp.zeros((block_rows, vector_count), jnp.float32)
    zero_sum = jnp.zeros((block_rows,), jnp.float32)
    parts = {offset: zero_part for offset in units}
    sums = {offset: zero_sum for offset in units}
    early = fetch_offsets[-1]
    early_ids = [i for i, pair in enumerate(pair_plan) if set(pair) <= {0, early}]
    tiles = [None] * len(pair_plan)
    early_results = []
    for i in early_ids:
        left, right = pair_plan[i]
        near_is_right = right == 0
        near_weights = weights[0]
        early_results.append(
            early_pass(owned_list[i], units[left], units[right], near_weights, near_is_right)
        )
    late_offsets = [offset for offset in fetch_offsets if offset != early]
    split_ids = [
        i
        for i, (left, right) in enumerate(pair_plan)
        if i not in early_ids and right in halves and left not in halves
    ]
    chunk_results = {}

    def run_chunk(i, h):
        left, right = pair_plan[i]
        rows = slice(h * half_rows, (h + 1) * half_rows)
        return column_chunk(
            owned_list[i], units[left], halves[right][h], weights[left], weights[right][rows]
        )

    for i in split_ids:
        chunk_results[(i, 0)] = run_chunk(i, 0)
    if early_ids or split_ids:
        late_halves, late_weights, early_results, first_chunks = lax.optimization_barrier(
            (
                [halves[o][1] for o in late_offsets if o in halves],
                [weights[o] for o in late_offsets],
                early_results,
                [chunk_results[(i, 0)] for i in split_ids],
            )
        )
        for position, offset in enumerate([o for o in late_offsets if o in halves]):
            halves[offset][1] = late_halves[position]
        for position, offset in enumerate(late_offsets):
            weights[offset] = late_weights[position]
        for position, i in enumerate(split_ids):
            chunk_results[(i, 0)] = first_chunks[position]
    for offset in halves:
        units[offset] = jnp.concatenate(halves[offset])
    for i in split_ids:
        chunk_results[(i, 1)] = run_chunk(i, 1)
        left, right = pair_plan[i]
        first, second = chunk_results[(i, 0)], chunk_results[(i, 1)]
        tiles[i] = jnp.concatenate([first[0], second[0]], axis=1)
        parts[left] = parts[left] + first[1] + second[1]
        sums[left] = sums[left] + first[2] + second[2]
        parts[right] = parts[right] + jnp.concatenate([first[3], second[3]])
        sums[right] = sums[right] + jnp.concatenate([first[4], second[4]])
    for i, (affinity, part, row_sum, col_sum) in zip(early_ids, early_results):
        left, right = pair_plan[i]
        near_is_right = right == 0
        tiles[i] = affinity
        far = left if near_is_right else right
        far_part = deferred_pass(owned_list[i], affinity, weights[far], not near_is_right)
        if near_is_right:
            row_part, col_part = part, far_part
        else:
            row_part, col_part = far_part, part
        parts[left] = parts[left] + row_part
        sums[left] = sums[left] + row_sum
        parts[right] = parts[right] + col_part
        sums[right] = sums[right] + col_sum
    for i, ((left, right), owned) in enumerate(zip(pair_plan, owned_list)):
        if i in early_ids or i in split_ids:
            continue
        affinity, row_part, row_sum, col_part, col_sum = first_pass(
            owned, units[left], units[right], weights[left], weights[right]
        )
        tiles[i] = affinity
        parts[left] = parts[left] + row_part
        sums[left] = sums[left] + row_sum
        parts[right] = parts[right] + col_part
        sums[right] = sums[right] + col_sum

    product = row_product(near_tile, start) + parts[0]
    vertex_valence = jnp.sum(near_tile, axis=1, dtype=jnp.float32) + sums[0]
    part_size = block_rows * vector_count
    for offset in fetch_offsets:
        sent = jnp.concatenate([as_rows(parts[offset].reshape(-1)), as_rows(sums[offset])])
        returned = shifted(sent, "wide", offset).reshape(-1)
        product = product + returned[:part_size].reshape(block_rows, vector_count)
        vertex_valence = vertex_valence + returned[part_size : part_size + block_rows]
    bases = orthonormal(product, vertex_valence, total_rows, fetch_offsets if ITERS > 1 else ())

    for iteration in range(1, ITERS):
        weights = {0: bases[0].astype(jnp.bfloat16)}
        for position, offset in enumerate(fetch_offsets):
            weights[offset] = bases[position + 1].astype(jnp.bfloat16)
        current = weights[0]
        parts = {offset: zero_part for offset in units}
        for (left, right), owned, affinity in zip(pair_plan, owned_list, tiles):
            row_part, col_part = later_pass(owned, affinity, weights[left], weights[right])
            parts[left] = parts[left] + row_part
            parts[right] = parts[right] + col_part
        product = row_product(near_tile, current) + parts[0]
        for offset in fetch_offsets:
            product = product + shifted(parts[offset], "wide", offset)
        last = iteration == ITERS - 1
        bases = orthonormal(product, vertex_valence, total_rows, () if last else fetch_offsets)
    return (bases[0], vertex_valence / block_rows)


def solution(mesh):
    in_specs = (P(("wide", "narrow"), None), P(("wide", "narrow"), None), P())
    out_specs = (P(("wide", "narrow"), None), P(("wide", "narrow")))
    return jax.shard_map(
        on_device, mesh=mesh, in_specs=in_specs, out_specs=out_specs, check_vma=False
    )
```

```python
from functools import partial
import itertools
import math

import jax
import jax.numpy as jnp
from jax import lax
from jax.sharding import PartitionSpec as P
from jax.experimental import pallas as pl

ITERS = 2


kernel_width_factor = 0.05


def shifted(block, axis, distance):
    devices = range(lax.axis_size(axis))
    route = [((i - distance) % len(devices), i) for i in devices]
    return lax.ppermute(block, axis, route)


def ring_gap(offset, span):
    offset %= span
    return min(offset, span - offset)


def difference_plan(span, far_reach):
    candidates = sorted(range(1, span), key=lambda s: (ring_gap(s, span), s))
    for count in range(1, span):
        best = None
        for chosen in itertools.combinations(candidates, count):
            points = (0,) + chosen
            plan = {}
            for a, b in itertools.permutations(points, 2):
                gap = (b - a) % span
                if 1 <= gap <= far_reach and gap not in plan:
                    plan[gap] = (a, b)
            if len(plan) == far_reach:
                cost = sum(ring_gap(s, span) for s in chosen)
                if best is None or cost < best[0]:
                    best = (cost, chosen, plan)
        if best is not None:
            return list(best[1]), [best[2][gap] for gap in range(1, far_reach + 1)]
    raise ValueError("no plan")


def normalize_rows(values):
    values_wide = values.astype(jnp.float32)
    scaling = lax.rsqrt(jnp.mean(values_wide * values_wide, axis=-1, keepdims=True) + 1e-06)
    return (values_wide * scaling / math.sqrt(values_wide.shape[-1])).astype(jnp.bfloat16)


def scores_tile(leftside_block, right_block):
    kernel_entries = lax.dot_general(
        leftside_block, right_block, (((1,), (1,)), ((), ())), preferred_element_type=jnp.float32
    )
    return jnp.exp(kernel_entries / kernel_width_factor).astype(jnp.bfloat16)


def row_product(affinity, weights):
    return jnp.dot(affinity, weights, preferred_element_type=jnp.float32)


def col_product(affinity, weights):
    return lax.dot_general(
        affinity, weights, (((0,), (0,)), ((), ())), preferred_element_type=jnp.float32
    )


def first_pass(owned, left_unit, right_unit, left_weights, right_weights):
    block_rows = left_unit.shape[0]
    vector_count = left_weights.shape[1]

    def compute_pair():
        affinity = scores_tile(left_unit, right_unit)
        return (
            affinity,
            row_product(affinity, right_weights),
            jnp.sum(affinity, axis=1, dtype=jnp.float32),
            col_product(affinity, left_weights),
            jnp.sum(affinity, axis=0, dtype=jnp.float32),
        )

    def skip_pair():
        zero_part = jnp.zeros((block_rows, vector_count), jnp.float32)
        zero_sum = jnp.zeros((block_rows,), jnp.float32)
        return (
            jnp.zeros((block_rows, block_rows), jnp.bfloat16),
            zero_part,
            zero_sum,
            zero_part,
            zero_sum,
        )

    return lax.cond(owned, compute_pair, skip_pair)


def early_pass(owned, left_unit, right_unit, near_weights, near_is_right):
    block_rows = left_unit.shape[0]
    vector_count = near_weights.shape[1]

    def compute_pair():
        affinity = scores_tile(left_unit, right_unit)
        if near_is_right:
            part = row_product(affinity, near_weights)
        else:
            part = col_product(affinity, near_weights)
        return (
            affinity,
            part,
            jnp.sum(affinity, axis=1, dtype=jnp.float32),
            jnp.sum(affinity, axis=0, dtype=jnp.float32),
        )

    def skip_pair():
        zero_sum = jnp.zeros((block_rows,), jnp.float32)
        return (
            jnp.zeros((block_rows, block_rows), jnp.bfloat16),
            jnp.zeros((block_rows, vector_count), jnp.float32),
            zero_sum,
            zero_sum,
        )

    return lax.cond(owned, compute_pair, skip_pair)


def deferred_pass(owned, affinity, far_weights, far_is_right):
    block_rows = affinity.shape[0]
    vector_count = far_weights.shape[1]

    def compute_pair():
        if far_is_right:
            return row_product(affinity, far_weights)
        return col_product(affinity, far_weights)

    return lax.cond(
        owned, compute_pair, lambda: jnp.zeros((block_rows, vector_count), jnp.float32)
    )


def column_chunk(owned, left_unit, right_chunk, left_weights, right_weights_chunk):
    block_rows = left_unit.shape[0]
    chunk_rows = right_chunk.shape[0]
    vector_count = left_weights.shape[1]

    def compute_pair():
        affinity = scores_tile(left_unit, right_chunk)
        return (
            affinity,
            row_product(affinity, right_weights_chunk),
            jnp.sum(affinity, axis=1, dtype=jnp.float32),
            col_product(affinity, left_weights),
            jnp.sum(affinity, axis=0, dtype=jnp.float32),
        )

    def skip_pair():
        return (
            jnp.zeros((block_rows, chunk_rows), jnp.bfloat16),
            jnp.zeros((block_rows, vector_count), jnp.float32),
            jnp.zeros((block_rows,), jnp.float32),
            jnp.zeros((chunk_rows, vector_count), jnp.float32),
            jnp.zeros((chunk_rows,), jnp.float32),
        )

    return lax.cond(owned, compute_pair, skip_pair)


def later_pass(owned, affinity, left_weights, right_weights):
    block_rows = affinity.shape[0]
    vector_count = left_weights.shape[1]

    def compute_pair():
        return (row_product(affinity, right_weights), col_product(affinity, left_weights))

    def skip_pair():
        zero_part = jnp.zeros((block_rows, vector_count), jnp.float32)
        return (zero_part, zero_part)

    return lax.cond(owned, compute_pair, skip_pair)


def butterfly(axis, summed_rows, block):
    size = lax.axis_size(axis)
    if size & (size - 1):
        return jnp.concatenate(
            [
                lax.psum(block[:summed_rows], axis),
                lax.all_gather(block[summed_rows:], axis, tiled=True),
            ]
        )
    index = lax.axis_index(axis)
    step = 1
    while step < size:
        route = [(i, i ^ step) for i in range(size)]
        other = lax.ppermute(block, axis, route)
        summed = block[:summed_rows] + other[:summed_rows]
        mine = block[summed_rows:]
        theirs = other[summed_rows:]
        upper = (index // step) % 2 == 1
        gathered = jnp.where(
            upper, jnp.concatenate([theirs, mine]), jnp.concatenate([mine, theirs])
        )
        block = jnp.concatenate([summed, gathered])
        step *= 2
    return block


def as_rows(vector, lanes=128):
    pad = (-vector.shape[0]) % lanes
    return jnp.pad(vector, (0, pad)).reshape(-1, lanes)


def hdot(left, right):
    return jnp.dot(left, right, precision=lax.Precision.HIGHEST, preferred_element_type=jnp.float32)


def factor_kernel(gram_ref, inverse_ref):
    size = gram_ref.shape[0]
    rows = lax.broadcasted_iota(jnp.int32, (size, 1), 0)
    cols = lax.broadcasted_iota(jnp.int32, (1, size), 1)
    eye = jnp.where(rows == cols, 1.0, 0.0).astype(jnp.float32)

    def pick_row(matrix, j):
        return jnp.sum(jnp.where(rows == j, matrix, 0.0), axis=0, keepdims=True)

    def pick_column(matrix, j):
        return jnp.sum(jnp.where(cols == j, matrix, 0.0), axis=1, keepdims=True)

    def invert(inverse, j, scale, factor_column):
        inverse_row = pick_row(inverse, j) * scale
        inverse = jnp.where(rows == j, inverse_row, inverse)
        return inverse - jnp.where(rows > j, factor_column, 0.0) * inverse_row

    def step(t, carry):
        remaining, inverse = carry
        j = 2 * t
        row0 = pick_row(remaining, j)
        row1 = pick_row(remaining, j + 1)
        column0 = pick_column(remaining, j)
        column1 = pick_column(remaining, j + 1)
        scale0 = lax.rsqrt(pick_column(row0, j))
        factor_column0 = jnp.where(rows >= j, column0 * scale0, 0.0)
        factor_row0 = jnp.where(cols >= j, row0 * scale0, 0.0)
        row1 = row1 - pick_row(factor_column0, j + 1) * factor_row0
        column1 = column1 - factor_column0 * pick_column(factor_row0, j + 1)
        scale1 = lax.rsqrt(pick_column(row1, j + 1))
        factor_column1 = jnp.where(rows >= j + 1, column1 * scale1, 0.0)
        factor_row1 = jnp.where(cols >= j + 1, row1 * scale1, 0.0)
        remaining = remaining - factor_column0 * factor_row0 - factor_column1 * factor_row1
        inverse = invert(inverse, j, scale0, factor_column0)
        inverse = invert(inverse, j + 1, scale1, factor_column1)
        return remaining, inverse

    _, inverse = lax.fori_loop(0, size // 2, step, (gram_ref[...], eye))
    inverse_ref[...] = inverse


def factor_inverse(gram_matrix):
    return pl.pallas_call(
        factor_kernel, out_shape=jax.ShapeDtypeStruct(gram_matrix.shape, jnp.float32)
    )(gram_matrix)


def orthonormal(product, vertex_valence, total_rows, fetch_offsets=()):
    block_rows, vector_count = product.shape
    walk = product / vertex_valence[:, None]
    partner_walks = [shifted(walk, "wide", -offset) for offset in fetch_offsets]
    centre = jnp.mean(walk, axis=0)
    centred = walk - centre
    local_gram = hdot(centred.T, centred)
    local_drift = jnp.sum(centred, axis=0)
    summed = jnp.concatenate(
        [
            as_rows(local_gram.reshape(-1)),
            as_rows(jnp.concatenate([jnp.sum(product, axis=0), jnp.sum(vertex_valence)[None]])),
        ]
    )
    summed_rows = summed.shape[0]
    block = jnp.concatenate([summed, as_rows(jnp.concatenate([centre, local_drift]))])
    gather_width = block.shape[0] - summed_rows
    for axis in ("narrow", "wide"):
        block = butterfly(axis, summed_rows, block)
    totals = block[:summed_rows].reshape(-1)
    gram_sum = totals[: vector_count * vector_count].reshape(vector_count, vector_count)
    column_sums = totals[vector_count * vector_count : vector_count * vector_count + vector_count]
    total_degree_sum = totals[vector_count * vector_count + vector_count]
    gathered = block[summed_rows:].reshape(-1, gather_width * 128)
    mean_walk = column_sums / total_degree_sum
    centres = gathered[:, :vector_count] - mean_walk
    drifts = gathered[:, vector_count:]
    cross = hdot(centres.T, drifts)
    gram_matrix = (gram_sum + cross + cross.T + block_rows * hdot(centres.T, centres)) / total_rows
    displaced_entries = jnp.concatenate([walk] + partner_walks) - mean_walk
    inverse_factor = factor_inverse(gram_matrix)
    bases = hdot(displaced_entries, inverse_factor.T)
    return [bases[i * block_rows : (i + 1) * block_rows] for i in range(1 + len(partner_walks))]


def on_device(embeddings, start, neighbours):
    wide_count = lax.axis_size("wide")
    lane_count = lax.axis_size("narrow")
    broad_index = lax.axis_index("wide")
    lane_index = lax.axis_index("narrow")
    far_reach = wide_count // 2 - 1
    fetch_offsets, pair_plan = difference_plan(wide_count, far_reach)
    unit_block = normalize_rows(embeddings)
    block_rows = unit_block.shape[0]
    total_rows = block_rows * wide_count * lane_count

    def block_at(offset):
        return (broad_index + offset) % wide_count * lane_count + lane_index

    owned_list = []
    for left, right in pair_plan:
        own_row = lax.dynamic_slice_in_dim(neighbours, block_at(left), 1, 0)[0]
        owned_list.append(jnp.any(own_row == block_at(right)))

    vector_count = start.shape[1]
    units = {0: unit_block}
    weights = {0: start}
    halves = {}
    half_rows = block_rows // 2
    for offset in fetch_offsets:
        if offset == fetch_offsets[-1]:
            units[offset] = normalize_rows(shifted(embeddings, "wide", -offset))
        else:
            halves[offset] = [
                shifted(unit_block[:half_rows], "wide", -offset),
                shifted(unit_block[half_rows:], "wide", -offset),
            ]
            units[offset] = None
        weights[offset] = shifted(start, "wide", -offset)

    self_mask = lax.broadcasted_iota(
        jnp.int32, (block_rows, block_rows), 0
    ) == lax.broadcasted_iota(jnp.int32, (block_rows, block_rows), 1)
    near_tile = jnp.where(
        self_mask, jnp.zeros((), jnp.bfloat16), scores_tile(unit_block, unit_block)
    )

    zero_part = jnp.zeros((block_rows, vector_count), jnp.float32)
    zero_sum = jnp.zeros((block_rows,), jnp.float32)
    parts = {offset: zero_part for offset in units}
    sums = {offset: zero_sum for offset in units}
    early = fetch_offsets[-1]
    early_ids = [i for i, pair in enumerate(pair_plan) if set(pair) <= {0, early}]
    tiles = [None] * len(pair_plan)
    early_results = []
    for i in early_ids:
        left, right = pair_plan[i]
        near_is_right = right == 0
        near_weights = weights[0]
        early_results.append(
            early_pass(owned_list[i], units[left], units[right], near_weights, near_is_right)
        )
    late_offsets = [offset for offset in fetch_offsets if offset != early]
    split_ids = [
        i
        for i, (left, right) in enumerate(pair_plan)
        if i not in early_ids and right in halves and left not in halves
    ]
    chunk_results = {}

    def run_chunk(i, h):
        left, right = pair_plan[i]
        rows = slice(h * half_rows, (h + 1) * half_rows)
        return column_chunk(
            owned_list[i], units[left], halves[right][h], weights[left], weights[right][rows]
        )

    for i in split_ids:
        chunk_results[(i, 0)] = run_chunk(i, 0)
    if early_ids or split_ids:
        late_halves, late_weights, early_results, first_chunks = lax.optimization_barrier(
            (
                [halves[o][1] for o in late_offsets if o in halves],
                [weights[o] for o in late_offsets],
                early_results,
                [chunk_results[(i, 0)] for i in split_ids],
            )
        )
        for position, offset in enumerate([o for o in late_offsets if o in halves]):
            halves[offset][1] = late_halves[position]
        for position, offset in enumerate(late_offsets):
            weights[offset] = late_weights[position]
        for position, i in enumerate(split_ids):
            chunk_results[(i, 0)] = first_chunks[position]
    for offset in halves:
        units[offset] = jnp.concatenate(halves[offset])
    for i in split_ids:
        chunk_results[(i, 1)] = run_chunk(i, 1)
        left, right = pair_plan[i]
        first, second = chunk_results[(i, 0)], chunk_results[(i, 1)]
        tiles[i] = jnp.concatenate([first[0], second[0]], axis=1)
        parts[left] = parts[left] + first[1] + second[1]
        sums[left] = sums[left] + first[2] + second[2]
        parts[right] = parts[right] + jnp.concatenate([first[3], second[3]])
        sums[right] = sums[right] + jnp.concatenate([first[4], second[4]])
    for i, (affinity, part, row_sum, col_sum) in zip(early_ids, early_results):
        left, right = pair_plan[i]
        near_is_right = right == 0
        tiles[i] = affinity
        far = left if near_is_right else right
        far_part = deferred_pass(owned_list[i], affinity, weights[far], not near_is_right)
        if near_is_right:
            row_part, col_part = part, far_part
        else:
            row_part, col_part = far_part, part
        parts[left] = parts[left] + row_part
        sums[left] = sums[left] + row_sum
        parts[right] = parts[right] + col_part
        sums[right] = sums[right] + col_sum
    for i, ((left, right), owned) in enumerate(zip(pair_plan, owned_list)):
        if i in early_ids or i in split_ids:
            continue
        affinity, row_part, row_sum, col_part, col_sum = first_pass(
            owned, units[left], units[right], weights[left], weights[right]
        )
        tiles[i] = affinity
        parts[left] = parts[left] + row_part
        sums[left] = sums[left] + row_sum
        parts[right] = parts[right] + col_part
        sums[right] = sums[right] + col_sum

    product = row_product(near_tile, start) + parts[0]
    vertex_valence = jnp.sum(near_tile, axis=1, dtype=jnp.float32) + sums[0]
    part_size = block_rows * vector_count
    for offset in fetch_offsets:
        sent = jnp.concatenate([as_rows(parts[offset].reshape(-1)), as_rows(sums[offset])])
        returned = shifted(sent, "wide", offset).reshape(-1)
        product = product + returned[:part_size].reshape(block_rows, vector_count)
        vertex_valence = vertex_valence + returned[part_size : part_size + block_rows]
    bases = orthonormal(product, vertex_valence, total_rows, fetch_offsets if ITERS > 1 else ())

    for iteration in range(1, ITERS):
        weights = {0: bases[0].astype(jnp.bfloat16)}
        for position, offset in enumerate(fetch_offsets):
            weights[offset] = bases[position + 1].astype(jnp.bfloat16)
        current = weights[0]
        parts = {offset: zero_part for offset in units}
        for (left, right), owned, affinity in zip(pair_plan, owned_list, tiles):
            row_part, col_part = later_pass(owned, affinity, weights[left], weights[right])
            parts[left] = parts[left] + row_part
            parts[right] = parts[right] + col_part
        product = row_product(near_tile, current) + parts[0]
        for offset in fetch_offsets:
            product = product + shifted(parts[offset], "wide", offset)
        last = iteration == ITERS - 1
        bases = orthonormal(product, vertex_valence, total_rows, () if last else fetch_offsets)
    return (bases[0], vertex_valence / block_rows)


def solution(mesh):
    in_specs = (P(("wide", "narrow"), None), P(("wide", "narrow"), None), P())
    out_specs = (P(("wide", "narrow"), None), P(("wide", "narrow")))
    return jax.shard_map(
        on_device, mesh=mesh, in_specs=in_specs, out_specs=out_specs, check_vma=False
    )
```

```python
from functools import partial
import itertools
import math

import jax
import jax.numpy as jnp
from jax import lax
from jax.sharding import PartitionSpec as P
from jax.experimental import pallas as pl

ITERS = 2


kernel_width_factor = 0.05


def shifted(block, axis, distance):
    devices = range(lax.axis_size(axis))
    route = [((i - distance) % len(devices), i) for i in devices]
    return lax.ppermute(block, axis, route)


def ring_gap(offset, span):
    offset %= span
    return min(offset, span - offset)


def difference_plan(span, far_reach):
    candidates = sorted(range(1, span), key=lambda s: (ring_gap(s, span), s))
    for count in range(1, span):
        best = None
        for chosen in itertools.combinations(candidates, count):
            points = (0,) + chosen
            plan = {}
            for a, b in itertools.permutations(points, 2):
                gap = (b - a) % span
                if 1 <= gap <= far_reach and gap not in plan:
                    plan[gap] = (a, b)
            if len(plan) == far_reach:
                cost = sum(ring_gap(s, span) for s in chosen)
                if best is None or cost < best[0]:
                    best = (cost, chosen, plan)
        if best is not None:
            return list(best[1]), [best[2][gap] for gap in range(1, far_reach + 1)]
    raise ValueError("no plan")


def normalize_rows(values):
    values_wide = values.astype(jnp.float32)
    scaling = lax.rsqrt(jnp.mean(values_wide * values_wide, axis=-1, keepdims=True) + 1e-06)
    return (values_wide * scaling / math.sqrt(values_wide.shape[-1])).astype(jnp.bfloat16)


def scores_tile(leftside_block, right_block):
    kernel_entries = lax.dot_general(
        leftside_block, right_block, (((1,), (1,)), ((), ())), preferred_element_type=jnp.float32
    )
    return jnp.exp(kernel_entries / kernel_width_factor).astype(jnp.bfloat16)


def row_product(affinity, weights):
    return jnp.dot(affinity, weights, preferred_element_type=jnp.float32)


def col_product(affinity, weights):
    return lax.dot_general(
        affinity, weights, (((0,), (0,)), ((), ())), preferred_element_type=jnp.float32
    )


def first_pass(owned, left_unit, right_unit, left_weights, right_weights):
    block_rows = left_unit.shape[0]
    vector_count = left_weights.shape[1]

    def compute_pair():
        affinity = scores_tile(left_unit, right_unit)
        return (
            affinity,
            row_product(affinity, right_weights),
            jnp.sum(affinity, axis=1, dtype=jnp.float32),
            col_product(affinity, left_weights),
            jnp.sum(affinity, axis=0, dtype=jnp.float32),
        )

    def skip_pair():
        zero_part = jnp.zeros((block_rows, vector_count), jnp.float32)
        zero_sum = jnp.zeros((block_rows,), jnp.float32)
        return (
            jnp.zeros((block_rows, block_rows), jnp.bfloat16),
            zero_part,
            zero_sum,
            zero_part,
            zero_sum,
        )

    return lax.cond(owned, compute_pair, skip_pair)


def early_pass(owned, left_unit, right_unit, near_weights, near_is_right):
    block_rows = left_unit.shape[0]
    vector_count = near_weights.shape[1]

    def compute_pair():
        affinity = scores_tile(left_unit, right_unit)
        if near_is_right:
            part = row_product(affinity, near_weights)
        else:
            part = col_product(affinity, near_weights)
        return (
            affinity,
            part,
            jnp.sum(affinity, axis=1, dtype=jnp.float32),
            jnp.sum(affinity, axis=0, dtype=jnp.float32),
        )

    def skip_pair():
        zero_sum = jnp.zeros((block_rows,), jnp.float32)
        return (
            jnp.zeros((block_rows, block_rows), jnp.bfloat16),
            jnp.zeros((block_rows, vector_count), jnp.float32),
            zero_sum,
            zero_sum,
        )

    return lax.cond(owned, compute_pair, skip_pair)


def deferred_pass(owned, affinity, far_weights, far_is_right):
    block_rows = affinity.shape[0]
    vector_count = far_weights.shape[1]

    def compute_pair():
        if far_is_right:
            return row_product(affinity, far_weights)
        return col_product(affinity, far_weights)

    return lax.cond(
        owned, compute_pair, lambda: jnp.zeros((block_rows, vector_count), jnp.float32)
    )


def column_chunk(owned, left_unit, right_chunk, left_weights, right_weights_chunk):
    block_rows = left_unit.shape[0]
    chunk_rows = right_chunk.shape[0]
    vector_count = left_weights.shape[1]

    def compute_pair():
        affinity = scores_tile(left_unit, right_chunk)
        return (
            affinity,
            row_product(affinity, right_weights_chunk),
            jnp.sum(affinity, axis=1, dtype=jnp.float32),
            col_product(affinity, left_weights),
            jnp.sum(affinity, axis=0, dtype=jnp.float32),
        )

    def skip_pair():
        return (
            jnp.zeros((block_rows, chunk_rows), jnp.bfloat16),
            jnp.zeros((block_rows, vector_count), jnp.float32),
            jnp.zeros((block_rows,), jnp.float32),
            jnp.zeros((chunk_rows, vector_count), jnp.float32),
            jnp.zeros((chunk_rows,), jnp.float32),
        )

    return lax.cond(owned, compute_pair, skip_pair)


def later_pass(owned, affinity, left_weights, right_weights):
    block_rows = affinity.shape[0]
    vector_count = left_weights.shape[1]

    def compute_pair():
        return (row_product(affinity, right_weights), col_product(affinity, left_weights))

    def skip_pair():
        zero_part = jnp.zeros((block_rows, vector_count), jnp.float32)
        return (zero_part, zero_part)

    return lax.cond(owned, compute_pair, skip_pair)


def butterfly(axis, summed_rows, block):
    size = lax.axis_size(axis)
    if size & (size - 1):
        return jnp.concatenate(
            [
                lax.psum(block[:summed_rows], axis),
                lax.all_gather(block[summed_rows:], axis, tiled=True),
            ]
        )
    index = lax.axis_index(axis)
    step = 1
    while step < size:
        route = [(i, i ^ step) for i in range(size)]
        other = lax.ppermute(block, axis, route)
        summed = block[:summed_rows] + other[:summed_rows]
        mine = block[summed_rows:]
        theirs = other[summed_rows:]
        upper = (index // step) % 2 == 1
        gathered = jnp.where(
            upper, jnp.concatenate([theirs, mine]), jnp.concatenate([mine, theirs])
        )
        block = jnp.concatenate([summed, gathered])
        step *= 2
    return block


def as_rows(vector, lanes=128):
    pad = (-vector.shape[0]) % lanes
    return jnp.pad(vector, (0, pad)).reshape(-1, lanes)


def hdot(left, right):
    return jnp.dot(left, right, precision=lax.Precision.HIGHEST, preferred_element_type=jnp.float32)


def factor_kernel(gram_ref, inverse_ref):
    size = gram_ref.shape[0]
    rows = lax.broadcasted_iota(jnp.int32, (size, size), 0)
    cols = lax.broadcasted_iota(jnp.int32, (size, size), 1)
    eye = jnp.where(rows == cols, 1.0, 0.0).astype(jnp.float32)

    def step(j, carry):
        remaining, inverse = carry
        pivot_row = jnp.sum(jnp.where(rows == j, remaining, 0.0), axis=0, keepdims=True)
        pivot = jnp.sum(jnp.where(cols[:1] == j, pivot_row, 0.0), axis=1, keepdims=True)
        column = jnp.sum(jnp.where(cols == j, remaining, 0.0), axis=1, keepdims=True)
        scale = lax.rsqrt(pivot)
        factor_column = jnp.where(rows[:, :1] >= j, column * scale, 0.0)
        factor_row = jnp.where(cols[:1] >= j, pivot_row * scale, 0.0)
        remaining = remaining - factor_column * factor_row
        inverse_row = jnp.sum(jnp.where(rows == j, inverse, 0.0), axis=0, keepdims=True) * scale
        inverse = jnp.where(rows == j, inverse_row, inverse)
        below = jnp.where(rows[:, :1] > j, factor_column, 0.0)
        inverse = inverse - below * inverse_row
        return remaining, inverse

    _, inverse = lax.fori_loop(0, size, step, (gram_ref[...], eye))
    inverse_ref[...] = inverse


def factor_inverse(gram_matrix):
    return pl.pallas_call(
        factor_kernel, out_shape=jax.ShapeDtypeStruct(gram_matrix.shape, jnp.float32)
    )(gram_matrix)


def orthonormal(product, vertex_valence, total_rows, fetch_offsets=()):
    block_rows, vector_count = product.shape
    walk = product / vertex_valence[:, None]
    partner_walks = [shifted(walk, "wide", -offset) for offset in fetch_offsets]
    centre = jnp.mean(walk, axis=0)
    centred = walk - centre
    local_gram = hdot(centred.T, centred)
    local_drift = jnp.sum(centred, axis=0)
    summed = jnp.concatenate(
        [
            as_rows(local_gram.reshape(-1)),
            as_rows(jnp.concatenate([jnp.sum(product, axis=0), jnp.sum(vertex_valence)[None]])),
        ]
    )
    summed_rows = summed.shape[0]
    block = jnp.concatenate([summed, as_rows(jnp.concatenate([centre, local_drift]))])
    gather_width = block.shape[0] - summed_rows
    for axis in ("narrow", "wide"):
        block = butterfly(axis, summed_rows, block)
    totals = block[:summed_rows].reshape(-1)
    gram_sum = totals[: vector_count * vector_count].reshape(vector_count, vector_count)
    column_sums = totals[vector_count * vector_count : vector_count * vector_count + vector_count]
    total_degree_sum = totals[vector_count * vector_count + vector_count]
    gathered = block[summed_rows:].reshape(-1, gather_width * 128)
    mean_walk = column_sums / total_degree_sum
    centres = gathered[:, :vector_count] - mean_walk
    drifts = gathered[:, vector_count:]
    cross = hdot(centres.T, drifts)
    gram_matrix = (gram_sum + cross + cross.T + block_rows * hdot(centres.T, centres)) / total_rows
    displaced_entries = jnp.concatenate([walk] + partner_walks) - mean_walk
    inverse_factor = factor_inverse(gram_matrix)
    bases = hdot(displaced_entries, inverse_factor.T)
    return [bases[i * block_rows : (i + 1) * block_rows] for i in range(1 + len(partner_walks))]


def on_device(embeddings, start, neighbours):
    wide_count = lax.axis_size("wide")
    lane_count = lax.axis_size("narrow")
    broad_index = lax.axis_index("wide")
    lane_index = lax.axis_index("narrow")
    far_reach = wide_count // 2 - 1
    fetch_offsets, pair_plan = difference_plan(wide_count, far_reach)
    unit_block = normalize_rows(embeddings)
    block_rows = unit_block.shape[0]
    total_rows = block_rows * wide_count * lane_count

    def block_at(offset):
        return (broad_index + offset) % wide_count * lane_count + lane_index

    owned_list = []
    for left, right in pair_plan:
        own_row = lax.dynamic_slice_in_dim(neighbours, block_at(left), 1, 0)[0]
        owned_list.append(jnp.any(own_row == block_at(right)))

    vector_count = start.shape[1]
    units = {0: unit_block}
    weights = {0: start}
    halves = {}
    half_rows = block_rows // 2
    for offset in fetch_offsets:
        if offset == fetch_offsets[-1]:
            units[offset] = normalize_rows(shifted(embeddings, "wide", -offset))
        else:
            halves[offset] = [
                shifted(unit_block[:half_rows], "wide", -offset),
                shifted(unit_block[half_rows:], "wide", -offset),
            ]
            units[offset] = None
        weights[offset] = shifted(start, "wide", -offset)

    self_mask = lax.broadcasted_iota(
        jnp.int32, (block_rows, block_rows), 0
    ) == lax.broadcasted_iota(jnp.int32, (block_rows, block_rows), 1)
    near_tile = jnp.where(
        self_mask, jnp.zeros((), jnp.bfloat16), scores_tile(unit_block, unit_block)
    )

    zero_part = jnp.zeros((block_rows, vector_count), jnp.float32)
    zero_sum = jnp.zeros((block_rows,), jnp.float32)
    parts = {offset: zero_part for offset in units}
    sums = {offset: zero_sum for offset in units}
    early = fetch_offsets[-1]
    early_ids = [i for i, pair in enumerate(pair_plan) if set(pair) <= {0, early}]
    tiles = [None] * len(pair_plan)
    early_results = []
    for i in early_ids:
        left, right = pair_plan[i]
        near_is_right = right == 0
        near_weights = weights[0]
        early_results.append(
            early_pass(owned_list[i], units[left], units[right], near_weights, near_is_right)
        )
    late_offsets = [offset for offset in fetch_offsets if offset != early]
    split_ids = [
        i
        for i, (left, right) in enumerate(pair_plan)
        if i not in early_ids and right in halves and left not in halves
    ]
    chunk_results = {}

    def run_chunk(i, h):
        left, right = pair_plan[i]
        rows = slice(h * half_rows, (h + 1) * half_rows)
        return column_chunk(
            owned_list[i], units[left], halves[right][h], weights[left], weights[right][rows]
        )

    for i in split_ids:
        chunk_results[(i, 0)] = run_chunk(i, 0)
    if early_ids or split_ids:
        late_halves, late_weights, early_results, first_chunks = lax.optimization_barrier(
            (
                [halves[o][1] for o in late_offsets if o in halves],
                [weights[o] for o in late_offsets],
                early_results,
                [chunk_results[(i, 0)] for i in split_ids],
            )
        )
        for position, offset in enumerate([o for o in late_offsets if o in halves]):
            halves[offset][1] = late_halves[position]
        for position, offset in enumerate(late_offsets):
            weights[offset] = late_weights[position]
        for position, i in enumerate(split_ids):
            chunk_results[(i, 0)] = first_chunks[position]
    for offset in halves:
        units[offset] = jnp.concatenate(halves[offset])
    for i in split_ids:
        chunk_results[(i, 1)] = run_chunk(i, 1)
        left, right = pair_plan[i]
        first, second = chunk_results[(i, 0)], chunk_results[(i, 1)]
        tiles[i] = jnp.concatenate([first[0], second[0]], axis=1)
        parts[left] = parts[left] + first[1] + second[1]
        sums[left] = sums[left] + first[2] + second[2]
        parts[right] = parts[right] + jnp.concatenate([first[3], second[3]])
        sums[right] = sums[right] + jnp.concatenate([first[4], second[4]])
    for i, (affinity, part, row_sum, col_sum) in zip(early_ids, early_results):
        left, right = pair_plan[i]
        near_is_right = right == 0
        tiles[i] = affinity
        far = left if near_is_right else right
        far_part = deferred_pass(owned_list[i], affinity, weights[far], not near_is_right)
        if near_is_right:
            row_part, col_part = part, far_part
        else:
            row_part, col_part = far_part, part
        parts[left] = parts[left] + row_part
        sums[left] = sums[left] + row_sum
        parts[right] = parts[right] + col_part
        sums[right] = sums[right] + col_sum
    for i, ((left, right), owned) in enumerate(zip(pair_plan, owned_list)):
        if i in early_ids or i in split_ids:
            continue
        affinity, row_part, row_sum, col_part, col_sum = first_pass(
            owned, units[left], units[right], weights[left], weights[right]
        )
        tiles[i] = affinity
        parts[left] = parts[left] + row_part
        sums[left] = sums[left] + row_sum
        parts[right] = parts[right] + col_part
        sums[right] = sums[right] + col_sum

    product = row_product(near_tile, start) + parts[0]
    vertex_valence = jnp.sum(near_tile, axis=1, dtype=jnp.float32) + sums[0]
    part_size = block_rows * vector_count
    for offset in fetch_offsets:
        sent = jnp.concatenate([as_rows(parts[offset].reshape(-1)), as_rows(sums[offset])])
        returned = shifted(sent, "wide", offset).reshape(-1)
        product = product + returned[:part_size].reshape(block_rows, vector_count)
        vertex_valence = vertex_valence + returned[part_size : part_size + block_rows]
    bases = orthonormal(product, vertex_valence, total_rows, fetch_offsets if ITERS > 1 else ())

    for iteration in range(1, ITERS):
        weights = {0: bases[0].astype(jnp.bfloat16)}
        for position, offset in enumerate(fetch_offsets):
            weights[offset] = bases[position + 1].astype(jnp.bfloat16)
        current = weights[0]
        parts = {offset: zero_part for offset in units}
        first_return = fetch_offsets[0]
        order = sorted(range(len(pair_plan)), key=lambda i: first_return not in pair_plan[i])
        for i in order:
            left, right = pair_plan[i]
            row_part, col_part = later_pass(owned_list[i], tiles[i], weights[left], weights[right])
            parts[left] = parts[left] + row_part
            parts[right] = parts[right] + col_part
        product = row_product(near_tile, current) + parts[0]
        for offset in fetch_offsets:
            product = product + shifted(parts[offset], "wide", offset)
        last = iteration == ITERS - 1
        bases = orthonormal(product, vertex_valence, total_rows, () if last else fetch_offsets)
    return (bases[0], vertex_valence / block_rows)


def solution(mesh):
    in_specs = (P(("wide", "narrow"), None), P(("wide", "narrow"), None), P())
    out_specs = (P(("wide", "narrow"), None), P(("wide", "narrow")))
    return jax.shard_map(
        on_device, mesh=mesh, in_specs=in_specs, out_specs=out_specs, check_vma=False
    )
```

```python
from functools import partial
import itertools
import math

import jax
import jax.numpy as jnp
from jax import lax
from jax.sharding import PartitionSpec as P
from jax.experimental import pallas as pl

ITERS = 2


kernel_width_factor = 0.05


def shifted(block, axis, distance):
    devices = range(lax.axis_size(axis))
    route = [((i - distance) % len(devices), i) for i in devices]
    return lax.ppermute(block, axis, route)


def ring_gap(offset, span):
    offset %= span
    return min(offset, span - offset)


def difference_plan(span, far_reach):
    candidates = sorted(range(1, span), key=lambda s: (ring_gap(s, span), s))
    for count in range(1, span):
        best = None
        for chosen in itertools.combinations(candidates, count):
            points = (0,) + chosen
            plan = {}
            for a, b in itertools.permutations(points, 2):
                gap = (b - a) % span
                if 1 <= gap <= far_reach and gap not in plan:
                    plan[gap] = (a, b)
            if len(plan) == far_reach:
                cost = sum(ring_gap(s, span) for s in chosen)
                if best is None or cost < best[0]:
                    best = (cost, chosen, plan)
        if best is not None:
            return list(best[1]), [best[2][gap] for gap in range(1, far_reach + 1)]
    raise ValueError("no plan")


def normalize_rows(values):
    values_wide = values.astype(jnp.float32)
    scaling = lax.rsqrt(jnp.mean(values_wide * values_wide, axis=-1, keepdims=True) + 1e-06)
    return (values_wide * scaling / math.sqrt(values_wide.shape[-1])).astype(jnp.bfloat16)


def scores_tile(leftside_block, right_block):
    kernel_entries = lax.dot_general(
        leftside_block, right_block, (((1,), (1,)), ((), ())), preferred_element_type=jnp.float32
    )
    return jnp.exp(kernel_entries / kernel_width_factor).astype(jnp.bfloat16)


def row_product(affinity, weights):
    return jnp.dot(affinity, weights, preferred_element_type=jnp.float32)


def col_product(affinity, weights):
    return lax.dot_general(
        affinity, weights, (((0,), (0,)), ((), ())), preferred_element_type=jnp.float32
    )


def first_pass(owned, left_unit, right_unit, left_weights, right_weights):
    block_rows = left_unit.shape[0]
    vector_count = left_weights.shape[1]

    def compute_pair():
        affinity = scores_tile(left_unit, right_unit)
        return (
            affinity,
            row_product(affinity, right_weights),
            jnp.sum(affinity, axis=1, dtype=jnp.float32),
            col_product(affinity, left_weights),
            jnp.sum(affinity, axis=0, dtype=jnp.float32),
        )

    def skip_pair():
        zero_part = jnp.zeros((block_rows, vector_count), jnp.float32)
        zero_sum = jnp.zeros((block_rows,), jnp.float32)
        return (
            jnp.zeros((block_rows, block_rows), jnp.bfloat16),
            zero_part,
            zero_sum,
            zero_part,
            zero_sum,
        )

    return lax.cond(owned, compute_pair, skip_pair)


def early_pass(owned, left_unit, right_unit, near_weights, near_is_right):
    block_rows = left_unit.shape[0]
    vector_count = near_weights.shape[1]

    def compute_pair():
        affinity = scores_tile(left_unit, right_unit)
        if near_is_right:
            part = row_product(affinity, near_weights)
        else:
            part = col_product(affinity, near_weights)
        return (
            affinity,
            part,
            jnp.sum(affinity, axis=1, dtype=jnp.float32),
            jnp.sum(affinity, axis=0, dtype=jnp.float32),
        )

    def skip_pair():
        zero_sum = jnp.zeros((block_rows,), jnp.float32)
        return (
            jnp.zeros((block_rows, block_rows), jnp.bfloat16),
            jnp.zeros((block_rows, vector_count), jnp.float32),
            zero_sum,
            zero_sum,
        )

    return lax.cond(owned, compute_pair, skip_pair)


def deferred_pass(owned, affinity, far_weights, far_is_right):
    block_rows = affinity.shape[0]
    vector_count = far_weights.shape[1]

    def compute_pair():
        if far_is_right:
            return row_product(affinity, far_weights)
        return col_product(affinity, far_weights)

    return lax.cond(
        owned, compute_pair, lambda: jnp.zeros((block_rows, vector_count), jnp.float32)
    )


def column_chunk(owned, left_unit, right_chunk, left_weights, right_weights_chunk):
    block_rows = left_unit.shape[0]
    chunk_rows = right_chunk.shape[0]
    vector_count = left_weights.shape[1]

    def compute_pair():
        affinity = scores_tile(left_unit, right_chunk)
        return (
            affinity,
            row_product(affinity, right_weights_chunk),
            jnp.sum(affinity, axis=1, dtype=jnp.float32),
            col_product(affinity, left_weights),
            jnp.sum(affinity, axis=0, dtype=jnp.float32),
        )

    def skip_pair():
        return (
            jnp.zeros((block_rows, chunk_rows), jnp.bfloat16),
            jnp.zeros((block_rows, vector_count), jnp.float32),
            jnp.zeros((block_rows,), jnp.float32),
            jnp.zeros((chunk_rows, vector_count), jnp.float32),
            jnp.zeros((chunk_rows,), jnp.float32),
        )

    return lax.cond(owned, compute_pair, skip_pair)


def later_pass(owned, affinity, left_weights, right_weights):
    block_rows = affinity.shape[0]
    vector_count = left_weights.shape[1]

    def compute_pair():
        return (row_product(affinity, right_weights), col_product(affinity, left_weights))

    def skip_pair():
        zero_part = jnp.zeros((block_rows, vector_count), jnp.float32)
        return (zero_part, zero_part)

    return lax.cond(owned, compute_pair, skip_pair)


def butterfly(axis, block):
    size = lax.axis_size(axis)
    if size & (size - 1):
        return lax.psum(block, axis)
    step = 1
    while step < size:
        route = [(i, i ^ step) for i in range(size)]
        block = block + lax.ppermute(block, axis, route)
        step *= 2
    return block


def as_rows(vector, lanes=128):
    pad = (-vector.shape[0]) % lanes
    return jnp.pad(vector, (0, pad)).reshape(-1, lanes)


def hdot(left, right):
    return jnp.dot(left, right, precision=lax.Precision.HIGHEST, preferred_element_type=jnp.float32)


def factor_kernel(gram_ref, inverse_ref):
    size = gram_ref.shape[0]
    rows = lax.broadcasted_iota(jnp.int32, (size, size), 0)
    cols = lax.broadcasted_iota(jnp.int32, (size, size), 1)
    eye = jnp.where(rows == cols, 1.0, 0.0).astype(jnp.float32)

    def step(j, carry):
        remaining, inverse = carry
        pivot_row = jnp.sum(jnp.where(rows == j, remaining, 0.0), axis=0, keepdims=True)
        pivot = jnp.sum(jnp.where(cols[:1] == j, pivot_row, 0.0), axis=1, keepdims=True)
        column = jnp.sum(jnp.where(cols == j, remaining, 0.0), axis=1, keepdims=True)
        scale = lax.rsqrt(pivot)
        factor_column = jnp.where(rows[:, :1] >= j, column * scale, 0.0)
        factor_row = jnp.where(cols[:1] >= j, pivot_row * scale, 0.0)
        remaining = remaining - factor_column * factor_row
        inverse_row = jnp.sum(jnp.where(rows == j, inverse, 0.0), axis=0, keepdims=True) * scale
        inverse = jnp.where(rows == j, inverse_row, inverse)
        below = jnp.where(rows[:, :1] > j, factor_column, 0.0)
        inverse = inverse - below * inverse_row
        return remaining, inverse

    _, inverse = lax.fori_loop(0, size, step, (gram_ref[...], eye))
    inverse_ref[...] = inverse


def factor_inverse(gram_matrix):
    return pl.pallas_call(
        factor_kernel, out_shape=jax.ShapeDtypeStruct(gram_matrix.shape, jnp.float32)
    )(gram_matrix)


def orthonormal(product, vertex_valence, total_rows, fetch_offsets=()):
    block_rows, vector_count = product.shape
    walk = product / vertex_valence[:, None]
    partner_walks = [shifted(walk, "wide", -offset) for offset in fetch_offsets]
    centre = jnp.mean(walk, axis=0)
    centred = walk - centre
    local_gram = hdot(centred.T, centred)
    local_drift = jnp.sum(centred, axis=0)
    summed = jnp.concatenate(
        [
            as_rows(local_gram.reshape(-1)),
            as_rows(jnp.concatenate([jnp.sum(product, axis=0), jnp.sum(vertex_valence)[None]])),
        ]
    )
    summed_rows = summed.shape[0]
    own_rows = as_rows(jnp.concatenate([centre, local_drift]))
    gather_width = own_rows.shape[0]
    device_count = lax.axis_size("wide") * lax.axis_size("narrow")
    device_index = lax.axis_index("wide") * lax.axis_size("narrow") + lax.axis_index("narrow")
    slots = lax.dynamic_update_slice(
        jnp.zeros((device_count * gather_width, own_rows.shape[1]), jnp.float32),
        own_rows,
        (device_index * gather_width, 0),
    )
    block = jnp.concatenate([summed, slots])
    for axis in ("narrow", "wide"):
        block = butterfly(axis, block)
    totals = block[:summed_rows].reshape(-1)
    gram_sum = totals[: vector_count * vector_count].reshape(vector_count, vector_count)
    column_sums = totals[vector_count * vector_count : vector_count * vector_count + vector_count]
    total_degree_sum = totals[vector_count * vector_count + vector_count]
    gathered = block[summed_rows:].reshape(-1, gather_width * 128)
    mean_walk = column_sums / total_degree_sum
    centres = gathered[:, :vector_count] - mean_walk
    drifts = gathered[:, vector_count:]
    cross = hdot(centres.T, drifts)
    gram_matrix = (gram_sum + cross + cross.T + block_rows * hdot(centres.T, centres)) / total_rows
    displaced_entries = jnp.concatenate([walk] + partner_walks) - mean_walk
    inverse_factor = factor_inverse(gram_matrix)
    bases = hdot(displaced_entries, inverse_factor.T)
    return [bases[i * block_rows : (i + 1) * block_rows] for i in range(1 + len(partner_walks))]


def on_device(embeddings, start, neighbours):
    wide_count = lax.axis_size("wide")
    lane_count = lax.axis_size("narrow")
    broad_index = lax.axis_index("wide")
    lane_index = lax.axis_index("narrow")
    far_reach = wide_count // 2 - 1
    fetch_offsets, pair_plan = difference_plan(wide_count, far_reach)
    unit_block = normalize_rows(embeddings)
    block_rows = unit_block.shape[0]
    total_rows = block_rows * wide_count * lane_count

    def block_at(offset):
        return (broad_index + offset) % wide_count * lane_count + lane_index

    owned_list = []
    for left, right in pair_plan:
        own_row = lax.dynamic_slice_in_dim(neighbours, block_at(left), 1, 0)[0]
        owned_list.append(jnp.any(own_row == block_at(right)))

    vector_count = start.shape[1]
    units = {0: unit_block}
    weights = {0: start}
    halves = {}
    half_rows = block_rows // 2
    for offset in fetch_offsets:
        if offset == fetch_offsets[-1]:
            units[offset] = normalize_rows(shifted(embeddings, "wide", -offset))
        else:
            halves[offset] = [
                shifted(unit_block[:half_rows], "wide", -offset),
                shifted(unit_block[half_rows:], "wide", -offset),
            ]
            units[offset] = None
        weights[offset] = shifted(start, "wide", -offset)

    self_mask = lax.broadcasted_iota(
        jnp.int32, (block_rows, block_rows), 0
    ) == lax.broadcasted_iota(jnp.int32, (block_rows, block_rows), 1)
    near_tile = jnp.where(
        self_mask, jnp.zeros((), jnp.bfloat16), scores_tile(unit_block, unit_block)
    )

    zero_part = jnp.zeros((block_rows, vector_count), jnp.float32)
    zero_sum = jnp.zeros((block_rows,), jnp.float32)
    parts = {offset: zero_part for offset in units}
    sums = {offset: zero_sum for offset in units}
    early = fetch_offsets[-1]
    early_ids = [i for i, pair in enumerate(pair_plan) if set(pair) <= {0, early}]
    tiles = [None] * len(pair_plan)
    early_results = []
    for i in early_ids:
        left, right = pair_plan[i]
        near_is_right = right == 0
        near_weights = weights[0]
        early_results.append(
            early_pass(owned_list[i], units[left], units[right], near_weights, near_is_right)
        )
    late_offsets = [offset for offset in fetch_offsets if offset != early]
    split_ids = [
        i
        for i, (left, right) in enumerate(pair_plan)
        if i not in early_ids and right in halves and left not in halves
    ]
    chunk_results = {}

    def run_chunk(i, h):
        left, right = pair_plan[i]
        rows = slice(h * half_rows, (h + 1) * half_rows)
        return column_chunk(
            owned_list[i], units[left], halves[right][h], weights[left], weights[right][rows]
        )

    for i in split_ids:
        chunk_results[(i, 0)] = run_chunk(i, 0)
    if early_ids or split_ids:
        late_halves, late_weights, early_results, first_chunks = lax.optimization_barrier(
            (
                [halves[o][1] for o in late_offsets if o in halves],
                [weights[o] for o in late_offsets],
                early_results,
                [chunk_results[(i, 0)] for i in split_ids],
            )
        )
        for position, offset in enumerate([o for o in late_offsets if o in halves]):
            halves[offset][1] = late_halves[position]
        for position, offset in enumerate(late_offsets):
            weights[offset] = late_weights[position]
        for position, i in enumerate(split_ids):
            chunk_results[(i, 0)] = first_chunks[position]
    for offset in halves:
        units[offset] = jnp.concatenate(halves[offset])
    for i in split_ids:
        chunk_results[(i, 1)] = run_chunk(i, 1)
        left, right = pair_plan[i]
        first, second = chunk_results[(i, 0)], chunk_results[(i, 1)]
        tiles[i] = jnp.concatenate([first[0], second[0]], axis=1)
        parts[left] = parts[left] + first[1] + second[1]
        sums[left] = sums[left] + first[2] + second[2]
        parts[right] = parts[right] + jnp.concatenate([first[3], second[3]])
        sums[right] = sums[right] + jnp.concatenate([first[4], second[4]])
    for i, (affinity, part, row_sum, col_sum) in zip(early_ids, early_results):
        left, right = pair_plan[i]
        near_is_right = right == 0
        tiles[i] = affinity
        far = left if near_is_right else right
        far_part = deferred_pass(owned_list[i], affinity, weights[far], not near_is_right)
        if near_is_right:
            row_part, col_part = part, far_part
        else:
            row_part, col_part = far_part, part
        parts[left] = parts[left] + row_part
        sums[left] = sums[left] + row_sum
        parts[right] = parts[right] + col_part
        sums[right] = sums[right] + col_sum
    for i, ((left, right), owned) in enumerate(zip(pair_plan, owned_list)):
        if i in early_ids or i in split_ids:
            continue
        affinity, row_part, row_sum, col_part, col_sum = first_pass(
            owned, units[left], units[right], weights[left], weights[right]
        )
        tiles[i] = affinity
        parts[left] = parts[left] + row_part
        sums[left] = sums[left] + row_sum
        parts[right] = parts[right] + col_part
        sums[right] = sums[right] + col_sum

    product = row_product(near_tile, start) + parts[0]
    vertex_valence = jnp.sum(near_tile, axis=1, dtype=jnp.float32) + sums[0]
    part_size = block_rows * vector_count
    for offset in fetch_offsets:
        sent = jnp.concatenate([as_rows(parts[offset].reshape(-1)), as_rows(sums[offset])])
        returned = shifted(sent, "wide", offset).reshape(-1)
        product = product + returned[:part_size].reshape(block_rows, vector_count)
        vertex_valence = vertex_valence + returned[part_size : part_size + block_rows]
    bases = orthonormal(product, vertex_valence, total_rows, fetch_offsets if ITERS > 1 else ())

    for iteration in range(1, ITERS):
        weights = {0: bases[0].astype(jnp.bfloat16)}
        for position, offset in enumerate(fetch_offsets):
            weights[offset] = bases[position + 1].astype(jnp.bfloat16)
        current = weights[0]
        parts = {offset: zero_part for offset in units}
        for (left, right), owned, affinity in zip(pair_plan, owned_list, tiles):
            row_part, col_part = later_pass(owned, affinity, weights[left], weights[right])
            parts[left] = parts[left] + row_part
            parts[right] = parts[right] + col_part
        product = row_product(near_tile, current) + parts[0]
        for offset in fetch_offsets:
            product = product + shifted(parts[offset], "wide", offset)
        last = iteration == ITERS - 1
        bases = orthonormal(product, vertex_valence, total_rows, () if last else fetch_offsets)
    return (bases[0], vertex_valence / block_rows)


def solution(mesh):
    in_specs = (P(("wide", "narrow"), None), P(("wide", "narrow"), None), P())
    out_specs = (P(("wide", "narrow"), None), P(("wide", "narrow")))
    return jax.shard_map(
        on_device, mesh=mesh, in_specs=in_specs, out_specs=out_specs, check_vma=False
    )
```

```python
from functools import partial
import itertools
import math

import jax
import jax.numpy as jnp
from jax import lax
from jax.sharding import PartitionSpec as P
from jax.experimental import pallas as pl

ITERS = 2


kernel_width_factor = 0.05


def shifted(block, axis, distance):
    devices = range(lax.axis_size(axis))
    route = [((i - distance) % len(devices), i) for i in devices]
    return lax.ppermute(block, axis, route)


def ring_gap(offset, span):
    offset %= span
    return min(offset, span - offset)


def difference_plan(span, far_reach):
    candidates = sorted(range(1, span), key=lambda s: (ring_gap(s, span), s))
    for count in range(1, span):
        best = None
        for chosen in itertools.combinations(candidates, count):
            points = (0,) + chosen
            plan = {}
            for a, b in itertools.permutations(points, 2):
                gap = (b - a) % span
                if 1 <= gap <= far_reach and gap not in plan:
                    plan[gap] = (a, b)
            if len(plan) == far_reach:
                cost = sum(ring_gap(s, span) for s in chosen)
                if best is None or cost < best[0]:
                    best = (cost, chosen, plan)
        if best is not None:
            return list(best[1]), [best[2][gap] for gap in range(1, far_reach + 1)]
    raise ValueError("no plan")


def normalize_rows(values):
    values_wide = values.astype(jnp.float32)
    scaling = lax.rsqrt(jnp.mean(values_wide * values_wide, axis=-1, keepdims=True) + 1e-06)
    return (values_wide * scaling / math.sqrt(values_wide.shape[-1])).astype(jnp.bfloat16)


def scores_tile(leftside_block, right_block):
    kernel_entries = lax.dot_general(
        leftside_block, right_block, (((1,), (1,)), ((), ())), preferred_element_type=jnp.float32
    )
    return jnp.exp(kernel_entries / kernel_width_factor).astype(jnp.bfloat16)


def row_product(affinity, weights):
    return jnp.dot(affinity, weights, preferred_element_type=jnp.float32)


def col_product(affinity, weights):
    return lax.dot_general(
        affinity, weights, (((0,), (0,)), ((), ())), preferred_element_type=jnp.float32
    )


def first_pass(owned, left_unit, right_unit, left_weights, right_weights):
    block_rows = left_unit.shape[0]
    vector_count = left_weights.shape[1]

    def compute_pair():
        affinity = scores_tile(left_unit, right_unit)
        return (
            affinity,
            row_product(affinity, right_weights),
            jnp.sum(affinity, axis=1, dtype=jnp.float32),
            col_product(affinity, left_weights),
            jnp.sum(affinity, axis=0, dtype=jnp.float32),
        )

    def skip_pair():
        zero_part = jnp.zeros((block_rows, vector_count), jnp.float32)
        zero_sum = jnp.zeros((block_rows,), jnp.float32)
        return (
            jnp.zeros((block_rows, block_rows), jnp.bfloat16),
            zero_part,
            zero_sum,
            zero_part,
            zero_sum,
        )

    return lax.cond(owned, compute_pair, skip_pair)


def early_pass(owned, left_unit, right_unit, near_weights, near_is_right):
    block_rows = left_unit.shape[0]
    vector_count = near_weights.shape[1]

    def compute_pair():
        affinity = scores_tile(left_unit, right_unit)
        if near_is_right:
            part = row_product(affinity, near_weights)
        else:
            part = col_product(affinity, near_weights)
        return (
            affinity,
            part,
            jnp.sum(affinity, axis=1, dtype=jnp.float32),
            jnp.sum(affinity, axis=0, dtype=jnp.float32),
        )

    def skip_pair():
        zero_sum = jnp.zeros((block_rows,), jnp.float32)
        return (
            jnp.zeros((block_rows, block_rows), jnp.bfloat16),
            jnp.zeros((block_rows, vector_count), jnp.float32),
            zero_sum,
            zero_sum,
        )

    return lax.cond(owned, compute_pair, skip_pair)


def deferred_pass(owned, affinity, far_weights, far_is_right):
    block_rows = affinity.shape[0]
    vector_count = far_weights.shape[1]

    def compute_pair():
        if far_is_right:
            return row_product(affinity, far_weights)
        return col_product(affinity, far_weights)

    return lax.cond(
        owned, compute_pair, lambda: jnp.zeros((block_rows, vector_count), jnp.float32)
    )


def column_chunk(owned, left_unit, right_chunk, left_weights, right_weights_chunk):
    block_rows = left_unit.shape[0]
    chunk_rows = right_chunk.shape[0]
    vector_count = left_weights.shape[1]

    def compute_pair():
        affinity = scores_tile(left_unit, right_chunk)
        return (
            affinity,
            row_product(affinity, right_weights_chunk),
            jnp.sum(affinity, axis=1, dtype=jnp.float32),
            col_product(affinity, left_weights),
            jnp.sum(affinity, axis=0, dtype=jnp.float32),
        )

    def skip_pair():
        return (
            jnp.zeros((block_rows, chunk_rows), jnp.bfloat16),
            jnp.zeros((block_rows, vector_count), jnp.float32),
            jnp.zeros((block_rows,), jnp.float32),
            jnp.zeros((chunk_rows, vector_count), jnp.float32),
            jnp.zeros((chunk_rows,), jnp.float32),
        )

    return lax.cond(owned, compute_pair, skip_pair)


def later_pass(owned, affinity, left_weights, right_weights):
    block_rows = left_weights.shape[0]
    vector_count = left_weights.shape[1]

    def compute_pair():
        if isinstance(affinity, list):
            width = affinity[0].shape[1]
            row_part = sum(
                row_product(piece, right_weights[h * width : (h + 1) * width])
                for h, piece in enumerate(affinity)
            )
            col_part = jnp.concatenate([col_product(piece, left_weights) for piece in affinity])
            return (row_part, col_part)
        return (row_product(affinity, right_weights), col_product(affinity, left_weights))

    def skip_pair():
        zero_part = jnp.zeros((block_rows, vector_count), jnp.float32)
        return (zero_part, zero_part)

    return lax.cond(owned, compute_pair, skip_pair)


def butterfly(axis, summed_rows, block):
    size = lax.axis_size(axis)
    if size & (size - 1):
        return jnp.concatenate(
            [
                lax.psum(block[:summed_rows], axis),
                lax.all_gather(block[summed_rows:], axis, tiled=True),
            ]
        )
    index = lax.axis_index(axis)
    step = 1
    while step < size:
        route = [(i, i ^ step) for i in range(size)]
        other = lax.ppermute(block, axis, route)
        summed = block[:summed_rows] + other[:summed_rows]
        mine = block[summed_rows:]
        theirs = other[summed_rows:]
        upper = (index // step) % 2 == 1
        gathered = jnp.where(
            upper, jnp.concatenate([theirs, mine]), jnp.concatenate([mine, theirs])
        )
        block = jnp.concatenate([summed, gathered])
        step *= 2
    return block


def as_rows(vector, lanes=128):
    pad = (-vector.shape[0]) % lanes
    return jnp.pad(vector, (0, pad)).reshape(-1, lanes)


def hdot(left, right):
    return jnp.dot(left, right, precision=lax.Precision.HIGHEST, preferred_element_type=jnp.float32)


def factor_kernel(gram_ref, inverse_ref):
    size = gram_ref.shape[0]
    rows = lax.broadcasted_iota(jnp.int32, (size, size), 0)
    cols = lax.broadcasted_iota(jnp.int32, (size, size), 1)
    eye = jnp.where(rows == cols, 1.0, 0.0).astype(jnp.float32)

    def step(j, carry):
        remaining, inverse = carry
        pivot_row = jnp.sum(jnp.where(rows == j, remaining, 0.0), axis=0, keepdims=True)
        pivot = jnp.sum(jnp.where(cols[:1] == j, pivot_row, 0.0), axis=1, keepdims=True)
        column = jnp.sum(jnp.where(cols == j, remaining, 0.0), axis=1, keepdims=True)
        scale = lax.rsqrt(pivot)
        factor_column = jnp.where(rows[:, :1] >= j, column * scale, 0.0)
        factor_row = jnp.where(cols[:1] >= j, pivot_row * scale, 0.0)
        remaining = remaining - factor_column * factor_row
        inverse_row = jnp.sum(jnp.where(rows == j, inverse, 0.0), axis=0, keepdims=True) * scale
        inverse = jnp.where(rows == j, inverse_row, inverse)
        below = jnp.where(rows[:, :1] > j, factor_column, 0.0)
        inverse = inverse - below * inverse_row
        return remaining, inverse

    _, inverse = lax.fori_loop(0, size, step, (gram_ref[...], eye))
    inverse_ref[...] = inverse


def factor_inverse(gram_matrix):
    return pl.pallas_call(
        factor_kernel, out_shape=jax.ShapeDtypeStruct(gram_matrix.shape, jnp.float32)
    )(gram_matrix)


def orthonormal(product, vertex_valence, total_rows, fetch_offsets=()):
    block_rows, vector_count = product.shape
    walk = product / vertex_valence[:, None]
    partner_walks = [shifted(walk, "wide", -offset) for offset in fetch_offsets]
    centre = jnp.mean(walk, axis=0)
    centred = walk - centre
    local_gram = hdot(centred.T, centred)
    local_drift = jnp.sum(centred, axis=0)
    summed = jnp.concatenate(
        [
            as_rows(local_gram.reshape(-1)),
            as_rows(jnp.concatenate([jnp.sum(product, axis=0), jnp.sum(vertex_valence)[None]])),
        ]
    )
    summed_rows = summed.shape[0]
    block = jnp.concatenate([summed, as_rows(jnp.concatenate([centre, local_drift]))])
    gather_width = block.shape[0] - summed_rows
    for axis in ("narrow", "wide"):
        block = butterfly(axis, summed_rows, block)
    totals = block[:summed_rows].reshape(-1)
    gram_sum = totals[: vector_count * vector_count].reshape(vector_count, vector_count)
    column_sums = totals[vector_count * vector_count : vector_count * vector_count + vector_count]
    total_degree_sum = totals[vector_count * vector_count + vector_count]
    gathered = block[summed_rows:].reshape(-1, gather_width * 128)
    mean_walk = column_sums / total_degree_sum
    centres = gathered[:, :vector_count] - mean_walk
    drifts = gathered[:, vector_count:]
    cross = hdot(centres.T, drifts)
    gram_matrix = (gram_sum + cross + cross.T + block_rows * hdot(centres.T, centres)) / total_rows
    displaced_entries = jnp.concatenate([walk] + partner_walks) - mean_walk
    inverse_factor = factor_inverse(gram_matrix)
    bases = hdot(displaced_entries, inverse_factor.T)
    return [bases[i * block_rows : (i + 1) * block_rows] for i in range(1 + len(partner_walks))]


def on_device(embeddings, start, neighbours):
    wide_count = lax.axis_size("wide")
    lane_count = lax.axis_size("narrow")
    broad_index = lax.axis_index("wide")
    lane_index = lax.axis_index("narrow")
    far_reach = wide_count // 2 - 1
    fetch_offsets, pair_plan = difference_plan(wide_count, far_reach)
    unit_block = normalize_rows(embeddings)
    block_rows = unit_block.shape[0]
    total_rows = block_rows * wide_count * lane_count

    def block_at(offset):
        return (broad_index + offset) % wide_count * lane_count + lane_index

    owned_list = []
    for left, right in pair_plan:
        own_row = lax.dynamic_slice_in_dim(neighbours, block_at(left), 1, 0)[0]
        owned_list.append(jnp.any(own_row == block_at(right)))

    vector_count = start.shape[1]
    units = {0: unit_block}
    weights = {0: start}
    halves = {}
    half_rows = block_rows // 2
    for offset in fetch_offsets:
        if offset == fetch_offsets[-1]:
            units[offset] = normalize_rows(shifted(embeddings, "wide", -offset))
        else:
            halves[offset] = [
                shifted(unit_block[:half_rows], "wide", -offset),
                shifted(unit_block[half_rows:], "wide", -offset),
            ]
            units[offset] = None
        weights[offset] = shifted(start, "wide", -offset)

    self_mask = lax.broadcasted_iota(
        jnp.int32, (block_rows, block_rows), 0
    ) == lax.broadcasted_iota(jnp.int32, (block_rows, block_rows), 1)
    near_tile = jnp.where(
        self_mask, jnp.zeros((), jnp.bfloat16), scores_tile(unit_block, unit_block)
    )

    zero_part = jnp.zeros((block_rows, vector_count), jnp.float32)
    zero_sum = jnp.zeros((block_rows,), jnp.float32)
    parts = {offset: zero_part for offset in units}
    sums = {offset: zero_sum for offset in units}
    early = fetch_offsets[-1]
    early_ids = [i for i, pair in enumerate(pair_plan) if set(pair) <= {0, early}]
    tiles = [None] * len(pair_plan)
    early_results = []
    for i in early_ids:
        left, right = pair_plan[i]
        near_is_right = right == 0
        near_weights = weights[0]
        early_results.append(
            early_pass(owned_list[i], units[left], units[right], near_weights, near_is_right)
        )
    late_offsets = [offset for offset in fetch_offsets if offset != early]
    split_ids = [
        i
        for i, (left, right) in enumerate(pair_plan)
        if i not in early_ids and right in halves and left not in halves
    ]
    chunk_results = {}

    def run_chunk(i, h):
        left, right = pair_plan[i]
        rows = slice(h * half_rows, (h + 1) * half_rows)
        return column_chunk(
            owned_list[i], units[left], halves[right][h], weights[left], weights[right][rows]
        )

    for i in split_ids:
        chunk_results[(i, 0)] = run_chunk(i, 0)
    if early_ids or split_ids:
        late_halves, late_weights, early_results, first_chunks = lax.optimization_barrier(
            (
                [halves[o][1] for o in late_offsets if o in halves],
                [weights[o] for o in late_offsets],
                early_results,
                [chunk_results[(i, 0)] for i in split_ids],
            )
        )
        for position, offset in enumerate([o for o in late_offsets if o in halves]):
            halves[offset][1] = late_halves[position]
        for position, offset in enumerate(late_offsets):
            weights[offset] = late_weights[position]
        for position, i in enumerate(split_ids):
            chunk_results[(i, 0)] = first_chunks[position]
    for offset in halves:
        units[offset] = jnp.concatenate(halves[offset])
    for i in split_ids:
        chunk_results[(i, 1)] = run_chunk(i, 1)
        left, right = pair_plan[i]
        first, second = chunk_results[(i, 0)], chunk_results[(i, 1)]
        tiles[i] = [first[0], second[0]]
        parts[left] = parts[left] + first[1] + second[1]
        sums[left] = sums[left] + first[2] + second[2]
        parts[right] = parts[right] + jnp.concatenate([first[3], second[3]])
        sums[right] = sums[right] + jnp.concatenate([first[4], second[4]])
    for i, (affinity, part, row_sum, col_sum) in zip(early_ids, early_results):
        left, right = pair_plan[i]
        near_is_right = right == 0
        tiles[i] = affinity
        far = left if near_is_right else right
        far_part = deferred_pass(owned_list[i], affinity, weights[far], not near_is_right)
        if near_is_right:
            row_part, col_part = part, far_part
        else:
            row_part, col_part = far_part, part
        parts[left] = parts[left] + row_part
        sums[left] = sums[left] + row_sum
        parts[right] = parts[right] + col_part
        sums[right] = sums[right] + col_sum
    for i, ((left, right), owned) in enumerate(zip(pair_plan, owned_list)):
        if i in early_ids or i in split_ids:
            continue
        affinity, row_part, row_sum, col_part, col_sum = first_pass(
            owned, units[left], units[right], weights[left], weights[right]
        )
        tiles[i] = affinity
        parts[left] = parts[left] + row_part
        sums[left] = sums[left] + row_sum
        parts[right] = parts[right] + col_part
        sums[right] = sums[right] + col_sum

    product = row_product(near_tile, start) + parts[0]
    vertex_valence = jnp.sum(near_tile, axis=1, dtype=jnp.float32) + sums[0]
    part_size = block_rows * vector_count
    for offset in fetch_offsets:
        sent = jnp.concatenate([as_rows(parts[offset].reshape(-1)), as_rows(sums[offset])])
        returned = shifted(sent, "wide", offset).reshape(-1)
        product = product + returned[:part_size].reshape(block_rows, vector_count)
        vertex_valence = vertex_valence + returned[part_size : part_size + block_rows]
    bases = orthonormal(product, vertex_valence, total_rows, fetch_offsets if ITERS > 1 else ())

    for iteration in range(1, ITERS):
        weights = {0: bases[0].astype(jnp.bfloat16)}
        for position, offset in enumerate(fetch_offsets):
            weights[offset] = bases[position + 1].astype(jnp.bfloat16)
        current = weights[0]
        parts = {offset: zero_part for offset in units}
        for (left, right), owned, affinity in zip(pair_plan, owned_list, tiles):
            row_part, col_part = later_pass(owned, affinity, weights[left], weights[right])
            parts[left] = parts[left] + row_part
            parts[right] = parts[right] + col_part
        product = row_product(near_tile, current) + parts[0]
        for offset in fetch_offsets:
            product = product + shifted(parts[offset], "wide", offset)
        last = iteration == ITERS - 1
        bases = orthonormal(product, vertex_valence, total_rows, () if last else fetch_offsets)
    return (bases[0], vertex_valence / block_rows)


def solution(mesh):
    in_specs = (P(("wide", "narrow"), None), P(("wide", "narrow"), None), P())
    out_specs = (P(("wide", "narrow"), None), P(("wide", "narrow")))
    return jax.shard_map(
        on_device, mesh=mesh, in_specs=in_specs, out_specs=out_specs, check_vma=False
    )
```
